32 devices in a mesh: tm: 8 (over y, x, core), src: 4 (over z).
Axes of the slice: x: 2, y: 2, z: 4, core: 2. Of those that a mesh axis runs over, the one named last changes fastest.
Arguments:
- observed_residual: float32 [12, 262144], P(None, ('tm', 'src')), may hold values from -6 to 6
- source_partials: float32 [5, 262144], P(None, ('tm', 'src')), may hold values from -6 to 6
- spread_derivative_table: float32 [12, 62], replicated, may hold values from -6 to 6
- detector_index: int32 [262144], P(('tm', 'src')), may hold values from 0 to 61
- first_knot_interval: int32 [262144], P(('tm', 'src')), may hold values from 0 to 1023
- interval_fraction: float32 [262144], P(('tm', 'src')), may hold values from 0 to 1
- live_slot_count: int32 [32, 32], P(('tm', 'src')), may hold values from 64 to 256, as said below
- slot_owned_source: int32 [32, 8192], P(('tm', 'src')), may hold values from 0 to 32767
Outputs:
- source_update: float32 [5, 1048576], P(None, ('tm', 'src'))
- attitude_update: float32 [8192], P('tm')
- residual: float32 [12, 262144], P(None, ('tm', 'src'))
The draws below stay inside these ranges and needn't reach their ends.
Inputs may be any that keep to these rules, and one draw needn't show every extreme that they name: live_slot_count[d, o] counts the live slots among the 256 that device d holds for owner o; one owner, drawn from the seed, has 256 live slots from every device.
All inputs are finite; a program needn't handle non-finite values.
Results may differ from the reference program's by a relative error of at most 0.00011.
Values sent between devices are 32-bit elements; how exact they have to be, the bound alone decides.
No kernel may reach another device: no remote copies, remote signals or barrier semaphores. Data moves between devices by JAX's collectives and lax.ppermute only.
A program may use at most 64 MiB of HBM per device.

```python
import jax
import jax.numpy as jnp

TR = 8192
SRC_DEV = 32768
KN = 1024
SCAN_SAMPLES = 12
PARAMS = 5
CCD_COUNT = 62
ITERS = 2
RANKS = 32
CAP = 256
TRANS = 262144
NSRC = 1048576
NKNOT = 8192
N_SRC = 4


def draw_live_slot_count(key, part):
    first, second = jax.random.split(jax.random.fold_in(key, 11))
    counts = jax.random.randint(first, (RANKS, RANKS), max(1, CAP // 4), CAP + 1)
    chosen = jax.random.randint(second, (), 0, RANKS)
    columns = jnp.arange(RANKS)[None, :]
    return jnp.where(columns == chosen, CAP, counts).astype(jnp.int32)


def plant(values, key, least, largest):
    shape = values.shape
    spot = [jax.random.randint(jax.random.fold_in(key, axis), (), 0, shape[axis]) for axis in range(len(shape))]
    values = values.at[tuple(spot)].set(least)
    longest = shape.index(max(shape))
    spot[longest] = (spot[longest] + 1) % shape[longest]
    return values.at[tuple(spot)].set(largest)


def block_scale(stream_key, extent, pieces, least, top_value):
    loudness, own = 1.0, jax.random.fold_in(stream_key, 6)
    for axis_at, shards_of in pieces:
        heights = jnp.exp(jax.random.uniform(jax.random.fold_in(own, axis_at), (shards_of,), jnp.float32, least / len(pieces), top_value / len(pieces)))
        loudness = loudness * jnp.repeat(heights, extent[axis_at] // shards_of).reshape([-1 if axis == axis_at else 1 for axis in range(len(extent))])
    return loudness


def normal_values(rng, shape, scale, bound, cuts=(), held_as=jnp.bfloat16):
    array = scale * jax.random.normal(rng, shape, jnp.float32)
    if cuts:
        array = array * block_scale(rng, shape, cuts, -0.22, 0.18)
    return jnp.clip(array, -bound, bound).astype(held_as)


def setup_inputs(seed: int = 0) -> dict:
    key_of = jax.random.split(jax.random.key(seed), 9)
    return {
        "observed_residual": normal_values(key_of[0], (SCAN_SAMPLES, TRANS), 1.0, 6.0, ((1, 32),), jnp.float32),
        "source_partials": normal_values(key_of[1], (PARAMS, TRANS), 1.0, 6.0, ((1, 32),), jnp.float32),
        "spread_derivative_table": normal_values(key_of[2], (SCAN_SAMPLES, CCD_COUNT), 1.0, 6.0, (), jnp.float32),
        "detector_index": plant(jax.random.randint(key_of[3], (TRANS,), 0, CCD_COUNT), jax.random.fold_in(key_of[3], 1), 0, CCD_COUNT - 1).astype(jnp.int32),
        "first_knot_interval": plant(jax.random.randint(key_of[4], (TRANS,), 0, KN), jax.random.fold_in(key_of[4], 1), 0, KN - 1).astype(jnp.int32),
        "interval_fraction": jnp.clip(1.0 * jax.random.uniform(key_of[5], (TRANS,), jnp.float32) ** block_scale(key_of[5], (TRANS,), ((0, 32),), -0.2, 0.2), 0.0, 1.0),
        "live_slot_count": draw_live_slot_count(jax.random.fold_in(key_of[8], 71), 0),
        "slot_owned_source": plant(jax.random.randint(key_of[7], (RANKS, TR), 0, SRC_DEV), jax.random.fold_in(key_of[7], 1), 0, SRC_DEV - 1).astype(jnp.int32),
    }


def spline_basis(frac):
    u2 = frac * frac
    u3 = u2 * frac
    one = 1.0 - frac
    return [one * one * one / 6.0, (3.0 * u3 - 6.0 * u2 + 4.0) / 6.0, (-3.0 * u3 + 3.0 * u2 + 3.0 * frac + 1.0) / 6.0, u3 / 6.0]


def reference(observed_residual, source_partials, spread_derivative_table, detector_index, first_knot_interval, interval_fraction, live_slot_count, slot_owned_source):
    slot = jnp.arange(TRANS, dtype=jnp.int32)
    device = slot // TR
    within = slot % TR
    owner = within // CAP
    place = within % CAP
    local_id = slot_owned_source[owner, device * CAP + place]
    src_glob = (owner * SRC_DEV + local_id).astype(jnp.int32)
    live = (place < live_slot_count[device, owner]).astype(jnp.float32)
    base = ((device // N_SRC) * KN + first_knot_interval).astype(jnp.int32)
    weight_factor = jnp.take(spread_derivative_table, detector_index, axis=1)
    basis = spline_basis(interval_fraction)

    def forward(srcs, att):
        zsrc = jnp.sum(source_partials * jnp.take(srcs, src_glob, axis=1), axis=0)
        padded = jnp.concatenate([att, jnp.zeros((3,), jnp.float32)])
        zatt = jnp.zeros((TRANS,), jnp.float32)
        for q in range(4):
            zatt = zatt + basis[q] * jnp.take(padded, base + q)
        return weight_factor * ((zsrc + zatt) * live)[None, :]

    def adjoint(resid):
        zbar = live * jnp.sum(weight_factor * resid, axis=0)
        grad_s = jnp.zeros((PARAMS, NSRC), jnp.float32).at[:, src_glob].add(source_partials * zbar[None, :])
        grad_a = jnp.zeros((NKNOT + 3,), jnp.float32)
        for q in range(4):
            grad_a = grad_a.at[base + q].add(basis[q] * zbar)
        return grad_s, grad_a[:NKNOT]

    def sqnorm(s_part, a_part):
        return jnp.sum(s_part * s_part) + jnp.sum(a_part * a_part)

    sol_s = jnp.zeros((PARAMS, NSRC), jnp.float32)
    sol_a = jnp.zeros((NKNOT,), jnp.float32)
    resid = observed_residual
    grad_s, grad_a = adjoint(resid)
    dir_s, dir_a = grad_s, grad_a
    gamma = sqnorm(grad_s, grad_a)
    for step in range(ITERS):
        image = forward(dir_s, dir_a)
        alpha = gamma / jnp.sum(image * image)
        sol_s = sol_s + alpha * dir_s
        sol_a = sol_a + alpha * dir_a
        resid = resid - alpha * image
        if step + 1 < ITERS:
            grad_s, grad_a = adjoint(resid)
            fresh = sqnorm(grad_s, grad_a)
            dir_s = grad_s + (fresh / gamma) * dir_s
            dir_a = grad_a + (fresh / gamma) * dir_a
            gamma = fresh
    return sol_s, sol_a, resid
```

```python
import jax
import jax.numpy as jnp
from jax import lax
from jax.experimental import pallas as pl
from jax.experimental.pallas import tpu as pltpu
from jax.sharding import PartitionSpec as P

SRC_DEV = 32768
KN = 1024
ITERS = 2
HI = 256
CHUNK = 512


def passed_along(block, axis, distance):
    devices = range(lax.axis_size(axis))
    route = [(i - distance, i) for i in devices if i - distance in devices]
    return lax.ppermute(block, axis, route)


def spline_basis(frac):
    u2 = frac * frac
    u3 = u2 * frac
    one = 1.0 - frac
    return [
        one * one * one / 6.0,
        (3.0 * u3 - 6.0 * u2 + 4.0) / 6.0,
        (-3.0 * u3 + 3.0 * u2 + 3.0 * frac + 1.0) / 6.0,
        u3 / 6.0,
    ]


def pieces(x):
    h = x.astype(jnp.bfloat16)
    r = x - h.astype(jnp.float32)
    m = r.astype(jnp.bfloat16)
    l = (r - m.astype(jnp.float32)).astype(jnp.bfloat16)
    return h, m, l


def hot_rows(ids, width):
    low = jnp.bitwise_and(ids, HI - 1)
    return (lax.broadcasted_iota(jnp.int32, (HI, width), 0) == low).astype(jnp.bfloat16)


def group_mask(ids, rows, width, groups):
    high = lax.shift_right_logical(ids, 8)
    iota = lax.broadcasted_iota(jnp.int32, (rows, width), 0)
    return (iota % groups) == high


def chunks(total, body):
    def step(i, carry):
        body(pl.multiple_of(i * CHUNK, CHUNK))
        return carry

    lax.fori_loop(0, total // CHUNK, step, 0)


def split_into(src_ref, big_ref):
    rows = src_ref.shape[0]
    for k, part in enumerate(pieces(src_ref[...])):
        big_ref[k * rows:(k + 1) * rows, :] = part


def source_gather(table, ids):
    n, width = table.shape
    cols = width // HI
    rows = n * cols
    total = ids.shape[1]

    def kernel(tab_ref, ids_ref, out_ref, big_ref):
        split_into(tab_ref, big_ref)

        def body(off):
            idc = ids_ref[:, pl.ds(off, CHUNK)]
            picked = jnp.dot(big_ref[...], hot_rows(idc, CHUNK), preferred_element_type=jnp.float32)
            sel = group_mask(idc, cols, CHUNK, cols)
            for p in range(n):
                acc = (
                    picked[p * cols:(p + 1) * cols]
                    + picked[rows + p * cols:rows + (p + 1) * cols]
                ) + picked[2 * rows + p * cols:2 * rows + (p + 1) * cols]
                out_ref[pl.ds(p, 1), pl.ds(off, CHUNK)] = jnp.sum(
                    jnp.where(sel, acc, 0.0), axis=0, keepdims=True
                )

        chunks(total, body)

    return pl.pallas_call(
        kernel,
        out_shape=jax.ShapeDtypeStruct((n, total), jnp.float32),
        scratch_shapes=[pltpu.VMEM((3 * rows, HI), jnp.bfloat16)],
    )(table.reshape(rows, HI), ids)


def source_scatter(values, ids, width):
    n, total = values.shape
    cols = width // HI
    rows = n * cols

    def kernel(val_ref, ids_ref, out_ref):
        out_ref[...] = jnp.zeros(out_ref.shape, jnp.float32)

        def body(off):
            idc = ids_ref[:, pl.ds(off, CHUNK)]
            v = val_ref[:, pl.ds(off, CHUNK)]
            sel = group_mask(idc, cols, CHUNK, cols)
            parts = []
            for piece in pieces(v):
                for p in range(n):
                    parts.append(jnp.where(sel, piece[p:p + 1, :], jnp.zeros((), jnp.bfloat16)))
            spread = jnp.concatenate(parts, axis=0)
            res = lax.dot_general(
                spread, hot_rows(idc, CHUNK), (((1,), (1,)), ((), ())),
                preferred_element_type=jnp.float32,
            )
            out_ref[...] += (res[:rows] + res[rows:2 * rows]) + res[2 * rows:]

        chunks(total, body)

    out = pl.pallas_call(
        kernel, out_shape=jax.ShapeDtypeStruct((rows, HI), jnp.float32)
    )(values, ids)
    return out.reshape(n, width)


def knot_gather(extended, first_ids, basis16, knots):
    total = first_ids.shape[1]
    cols = knots // HI
    shifted = jnp.stack([extended[q:q + knots] for q in range(4)], axis=0)
    rows = 4 * cols

    def kernel(tab_ref, ids_ref, basis_ref, out_ref, big_ref):
        split_into(tab_ref, big_ref)

        def body(off):
            idc = ids_ref[:, pl.ds(off, CHUNK)]
            picked = jnp.dot(big_ref[...], hot_rows(idc, CHUNK), preferred_element_type=jnp.float32)
            acc = (picked[:rows] + picked[rows:2 * rows]) + picked[2 * rows:]
            sel = group_mask(idc, rows, CHUNK, cols)
            weight = jnp.where(sel, basis_ref[:, pl.ds(off, CHUNK)], 0.0)
            out_ref[:, pl.ds(off, CHUNK)] = jnp.sum(acc * weight, axis=0, keepdims=True)

        chunks(total, body)

    return pl.pallas_call(
        kernel,
        out_shape=jax.ShapeDtypeStruct((1, total), jnp.float32),
        scratch_shapes=[pltpu.VMEM((3 * rows, HI), jnp.bfloat16)],
    )(shifted.reshape(rows, HI), first_ids, basis16)


def knot_scatter(values, first_ids, basis16, knots):
    total = first_ids.shape[1]
    cols = knots // HI
    rows = 4 * cols

    def kernel(val_ref, ids_ref, basis_ref, out_ref):
        out_ref[...] = jnp.zeros(out_ref.shape, jnp.float32)

        def body(off):
            idc = ids_ref[:, pl.ds(off, CHUNK)]
            sel = group_mask(idc, rows, CHUNK, cols)
            v = jnp.where(sel, basis_ref[:, pl.ds(off, CHUNK)] * val_ref[:, pl.ds(off, CHUNK)], 0.0)
            spread = jnp.concatenate(pieces(v), axis=0)
            res = lax.dot_general(
                spread, hot_rows(idc, CHUNK), (((1,), (1,)), ((), ())),
                preferred_element_type=jnp.float32,
            )
            out_ref[...] += (res[:rows] + res[rows:2 * rows]) + res[2 * rows:]

        chunks(total, body)

    out = pl.pallas_call(
        kernel, out_shape=jax.ShapeDtypeStruct((rows, HI), jnp.float32)
    )(values, first_ids, basis16)
    per_shift = out.reshape(4, knots)
    grad = jnp.zeros((knots + 3,), jnp.float32)
    for q in range(4):
        grad = grad.at[q:q + knots].add(per_shift[q])
    return grad


def per_device(
    observed_residual,
    source_partials,
    spread_derivative_table,
    detector_index,
    first_knot_interval,
    interval_fraction,
    live_slot_count,
    slot_owned_source,
):
    rows = observed_residual.shape[1]
    n_time = lax.axis_size("tm")
    n_share = lax.axis_size("src")
    n_ranks = n_time * n_share
    capacity = rows // n_ranks
    n_params = source_partials.shape[0]
    detector_count = spread_derivative_table.shape[1]
    knots = KN
    owned = SRC_DEV
    place = jnp.arange(capacity, dtype=jnp.int32)[None, :]
    live = (place < live_slot_count[0][:, None]).astype(jnp.float32).reshape(rows)
    indicator = (
        detector_index[None, :] == jnp.arange(detector_count, dtype=jnp.int32)[:, None]
    ).astype(jnp.float32)
    weight_factor = jnp.dot(
        spread_derivative_table,
        indicator,
        precision=lax.Precision.HIGHEST,
        preferred_element_type=jnp.float32,
    )
    basis16 = jnp.repeat(jnp.stack(spline_basis(interval_fraction), axis=0), knots // HI, axis=0)
    first_ids = first_knot_interval.reshape(1, rows)
    ids = slot_owned_source[0].reshape(1, rows)
    held = lax.all_to_all(source_partials, ("tm", "src"), split_axis=1, concat_axis=1, tiled=True)

    def adjoint(resid):
        zbar = live * jnp.sum(weight_factor * resid, axis=0)
        returned = held * lax.all_to_all(zbar, ("tm", "src"), split_axis=0, concat_axis=0, tiled=True)[None, :]
        grad_s = source_scatter(returned, ids, owned)
        grad_a = knot_scatter(zbar.reshape(1, rows), first_ids, basis16, knots)
        grad_a = lax.psum(grad_a, "src")
        carried = passed_along(grad_a[knots:], "tm", 1)
        return (grad_s, grad_a[:knots].at[:3].add(carried))

    def local_inner(s_one, a_one, s_two, a_two):
        return jnp.sum(s_one * s_two) + jnp.sum(a_one * a_two) / n_share

    def total(value):
        return lax.psum(value, ("tm", "src"))

    sol_s = jnp.zeros((n_params, owned), jnp.float32)
    sol_a = jnp.zeros((knots,), jnp.float32)
    resid = observed_residual
    grad_s, grad_a = adjoint(resid)
    dir_s, dir_a = (grad_s, grad_a)
    gamma = total(local_inner(grad_s, grad_a, grad_s, grad_a))
    for step in range(ITERS):
        pulled = source_gather(dir_s, ids)
        column = jnp.sum(held * pulled, axis=0)
        zsrc = lax.all_to_all(column, ("tm", "src"), split_axis=0, concat_axis=0, tiled=True)
        rim = passed_along(dir_a[:3], "tm", -1)
        extended = jnp.concatenate([dir_a, rim])
        zatt = knot_gather(extended, first_ids, basis16, knots).reshape(rows)
        shift_total = (zsrc + zatt) * live
        image = weight_factor * shift_total[None, :]
        alpha = gamma / total(jnp.sum(image * image))
        sol_s = sol_s + alpha * dir_s
        sol_a = sol_a + alpha * dir_a
        resid = resid - alpha * image
        if step + 1 < ITERS:
            grad_s, grad_a = adjoint(resid)
            fresh = total(local_inner(grad_s, grad_a, grad_s, grad_a))
            dir_s = grad_s + fresh / gamma * dir_s
            dir_a = grad_a + fresh / gamma * dir_a
            gamma = fresh
    return (sol_s, sol_a, resid)


def solution(mesh):
    placed = (
        P(None, ("tm", "src")),
        P(None, ("tm", "src")),
        P(),
        P(("tm", "src")),
        P(("tm", "src")),
        P(("tm", "src")),
        P(("tm", "src"), None),
        P(("tm", "src"), None),
    )
    return jax.shard_map(
        per_device,
        mesh=mesh,
        in_specs=placed,
        out_specs=(P(None, ("tm", "src")), P("tm"), P(None, ("tm", "src"))),
        check_vma=False,
    )
```

```python
import jax
import jax.numpy as jnp
from jax import lax
from jax.experimental import pallas as pl
from jax.experimental.pallas import tpu as pltpu
from jax.sharding import PartitionSpec as P

SRC_DEV = 32768
KN = 1024
ITERS = 2
HI = 256
CHUNK = 512


def passed_along(block, axis, distance):
    devices = range(lax.axis_size(axis))
    route = [(i - distance, i) for i in devices if i - distance in devices]
    return lax.ppermute(block, axis, route)


def spline_basis(frac):
    u2 = frac * frac
    u3 = u2 * frac
    one = 1.0 - frac
    return [
        one * one * one / 6.0,
        (3.0 * u3 - 6.0 * u2 + 4.0) / 6.0,
        (-3.0 * u3 + 3.0 * u2 + 3.0 * frac + 1.0) / 6.0,
        u3 / 6.0,
    ]


def pieces(x):
    h = x.astype(jnp.bfloat16)
    r = x - h.astype(jnp.float32)
    m = r.astype(jnp.bfloat16)
    l = (r - m.astype(jnp.float32)).astype(jnp.bfloat16)
    return h, m, l


def hot_rows(ids, width):
    low = jnp.bitwise_and(ids, HI - 1)
    return (lax.broadcasted_iota(jnp.int32, (HI, width), 0) == low).astype(jnp.bfloat16)


def group_mask(ids, rows, width, groups):
    high = lax.shift_right_logical(ids, 8)
    iota = lax.broadcasted_iota(jnp.int32, (rows, width), 0)
    return (iota % groups) == high


def chunks(total, body):
    def step(i, carry):
        body(pl.multiple_of(i * CHUNK, CHUNK))
        return carry

    lax.fori_loop(0, total // CHUNK, step, 0)


def split_into(src_ref, big_ref):
    rows = src_ref.shape[0]
    for k, part in enumerate(pieces(src_ref[...])):
        big_ref[k * rows:(k + 1) * rows, :] = part


def source_gather(table, ids):
    n, width = table.shape
    cols = width // HI
    rows = n * cols
    total = ids.shape[1]

    def kernel(tab_ref, ids_ref, out_ref, big_ref):
        split_into(tab_ref, big_ref)

        def body(off):
            idc = ids_ref[:, pl.ds(off, CHUNK)]
            picked = jnp.dot(big_ref[...], hot_rows(idc, CHUNK), preferred_element_type=jnp.float32)
            sel = group_mask(idc, cols, CHUNK, cols)
            for p in range(n):
                acc = (
                    picked[p * cols:(p + 1) * cols]
                    + picked[rows + p * cols:rows + (p + 1) * cols]
                ) + picked[2 * rows + p * cols:2 * rows + (p + 1) * cols]
                out_ref[pl.ds(p, 1), pl.ds(off, CHUNK)] = jnp.sum(
                    jnp.where(sel, acc, 0.0), axis=0, keepdims=True
                )

        chunks(total, body)

    return pl.pallas_call(
        kernel,
        out_shape=jax.ShapeDtypeStruct((n, total), jnp.float32),
        scratch_shapes=[pltpu.VMEM((3 * rows, HI), jnp.bfloat16)],
    )(table.reshape(rows, HI), ids)


def source_scatter(values, ids, width):
    n, total = values.shape
    cols = width // HI
    rows = n * cols

    def kernel(val_ref, ids_ref, out_ref):
        out_ref[...] = jnp.zeros(out_ref.shape, jnp.float32)

        def body(off):
            idc = ids_ref[:, pl.ds(off, CHUNK)]
            v = val_ref[:, pl.ds(off, CHUNK)]
            sel = group_mask(idc, cols, CHUNK, cols)
            parts = []
            for piece in pieces(v):
                for p in range(n):
                    parts.append(jnp.where(sel, piece[p:p + 1, :], jnp.zeros((), jnp.bfloat16)))
            spread = jnp.concatenate(parts, axis=0)
            res = lax.dot_general(
                spread, hot_rows(idc, CHUNK), (((1,), (1,)), ((), ())),
                preferred_element_type=jnp.float32,
            )
            out_ref[...] += (res[:rows] + res[rows:2 * rows]) + res[2 * rows:]

        chunks(total, body)

    out = pl.pallas_call(
        kernel, out_shape=jax.ShapeDtypeStruct((rows, HI), jnp.float32)
    )(values, ids)
    return out.reshape(n, width)


def knot_gather(extended, first_ids, basis, knots):
    total = first_ids.shape[1]
    cols = knots // HI
    shifted = jnp.stack([extended[q:q + knots] for q in range(4)], axis=0)
    rows = 4 * cols

    def kernel(tab_ref, ids_ref, basis_ref, out_ref, big_ref):
        split_into(tab_ref, big_ref)

        def body(off):
            idc = ids_ref[:, pl.ds(off, CHUNK)]
            picked = jnp.dot(big_ref[...], hot_rows(idc, CHUNK), preferred_element_type=jnp.float32)
            acc = (picked[:rows] + picked[rows:2 * rows]) + picked[2 * rows:]
            sel = group_mask(idc, cols, CHUNK, cols)
            b = basis_ref[:, pl.ds(off, CHUNK)]
            z = jnp.zeros((1, CHUNK), jnp.float32)
            for q in range(4):
                value = jnp.sum(jnp.where(sel, acc[q * cols:(q + 1) * cols], 0.0), axis=0, keepdims=True)
                z = z + b[q:q + 1] * value
            out_ref[:, pl.ds(off, CHUNK)] = z

        chunks(total, body)

    return pl.pallas_call(
        kernel,
        out_shape=jax.ShapeDtypeStruct((1, total), jnp.float32),
        scratch_shapes=[pltpu.VMEM((3 * rows, HI), jnp.bfloat16)],
    )(shifted.reshape(rows, HI), first_ids, basis)


def knot_scatter(values, first_ids, basis16, knots):
    total = first_ids.shape[1]
    cols = knots // HI
    rows = 4 * cols

    def kernel(val_ref, ids_ref, basis_ref, out_ref):
        out_ref[...] = jnp.zeros(out_ref.shape, jnp.float32)

        def body(off):
            idc = ids_ref[:, pl.ds(off, CHUNK)]
            sel = group_mask(idc, rows, CHUNK, cols)
            v = jnp.where(sel, basis_ref[:, pl.ds(off, CHUNK)] * val_ref[:, pl.ds(off, CHUNK)], 0.0)
            spread = jnp.concatenate(pieces(v), axis=0)
            res = lax.dot_general(
                spread, hot_rows(idc, CHUNK), (((1,), (1,)), ((), ())),
                preferred_element_type=jnp.float32,
            )
            out_ref[...] += (res[:rows] + res[rows:2 * rows]) + res[2 * rows:]

        chunks(total, body)

    out = pl.pallas_call(
        kernel, out_shape=jax.ShapeDtypeStruct((rows, HI), jnp.float32)
    )(values, first_ids, basis16)
    per_shift = out.reshape(4, knots)
    grad = jnp.zeros((knots + 3,), jnp.float32)
    for q in range(4):
        grad = grad.at[q:q + knots].add(per_shift[q])
    return grad


def per_device(
    observed_residual,
    source_partials,
    spread_derivative_table,
    detector_index,
    first_knot_interval,
    interval_fraction,
    live_slot_count,
    slot_owned_source,
):
    rows = observed_residual.shape[1]
    n_time = lax.axis_size("tm")
    n_share = lax.axis_size("src")
    n_ranks = n_time * n_share
    capacity = rows // n_ranks
    n_params = source_partials.shape[0]
    detector_count = spread_derivative_table.shape[1]
    knots = KN
    n_knots = n_time * knots
    owned = SRC_DEV
    everyone = ("tm", "src")
    place = jnp.arange(capacity, dtype=jnp.int32)[None, :]
    live = (place < live_slot_count[0][:, None]).astype(jnp.float32).reshape(rows)
    indicator = (
        detector_index[None, :] == jnp.arange(detector_count, dtype=jnp.int32)[:, None]
    ).astype(jnp.float32)
    weight_factor = jnp.dot(
        spread_derivative_table,
        indicator,
        precision=lax.Precision.HIGHEST,
        preferred_element_type=jnp.float32,
    )
    weight_sq = jnp.sum(weight_factor * weight_factor, axis=0)
    basis16 = jnp.repeat(jnp.stack(spline_basis(interval_fraction), axis=0), knots // HI, axis=0)
    first_ids = first_knot_interval.reshape(1, rows)
    ids = slot_owned_source[0].reshape(1, rows)
    zbar0 = live * jnp.sum(weight_factor * observed_residual, axis=0)

    packed = jnp.concatenate(
        [
            source_partials,
            zbar0[None],
            weight_sq[None],
            live[None],
            interval_fraction[None],
            first_knot_interval.astype(jnp.float32)[None],
        ],
        axis=0,
    )
    got = lax.all_to_all(packed, everyone, split_axis=1, concat_axis=1, tiled=True)
    held = got[:n_params]
    zbar0_own = got[n_params]
    weight_sq_own = got[n_params + 1]
    live_own = got[n_params + 2]
    basis_own = jnp.stack(spline_basis(got[n_params + 3]), axis=0)
    slot_device = jnp.arange(rows, dtype=jnp.int32) // capacity
    base_own = ((slot_device // n_share) * knots + got[n_params + 4].astype(jnp.int32)).reshape(1, rows)

    def adjoint(zbar_own, zbar_slot):
        grad_s = source_scatter(held * zbar_own[None, :], ids, owned)
        part_a = knot_scatter(zbar_slot.reshape(1, rows), first_ids, basis16, knots)
        mine = jnp.concatenate([part_a, jnp.sum(grad_s * grad_s)[None]])
        every = lax.all_to_all(
            jnp.broadcast_to(mine[None, :], (n_ranks, knots + 4)), everyone, 0, 0, tiled=True
        )
        block = jnp.sum(every[:, :knots + 3].reshape(n_time, n_share, knots + 3), axis=1)
        main = block[:, :knots].at[1:, :3].add(block[:-1, knots:])
        grad_a = main.reshape(n_knots)
        norm = jnp.sum(every[:, knots + 3]) + jnp.sum(grad_a * grad_a)
        return grad_s, grad_a, norm

    def forward(dir_s, dir_a):
        pulled = source_gather(dir_s, ids)
        zsrc = jnp.sum(held * pulled, axis=0)
        extended = jnp.concatenate([dir_a, jnp.zeros((3,), jnp.float32)])
        zatt = knot_gather(extended, base_own, basis_own, n_knots).reshape(rows)
        shift_own = (zsrc + zatt) * live_own
        partial = jnp.sum(weight_sq_own * shift_own * shift_own)
        payload = jnp.concatenate(
            [shift_own.reshape(n_ranks, capacity), jnp.broadcast_to(partial, (n_ranks, 1))], axis=1
        )
        back = lax.all_to_all(payload, everyone, 0, 0, tiled=True)
        return shift_own, back[:, :capacity].reshape(rows), jnp.sum(back[:, capacity])

    sol_s = jnp.zeros((n_params, owned), jnp.float32)
    sol_a = jnp.zeros((n_knots,), jnp.float32)
    resid = observed_residual
    zbar_own, zbar_slot = zbar0_own, zbar0
    grad_s, grad_a, gamma = adjoint(zbar_own, zbar_slot)
    dir_s, dir_a = (grad_s, grad_a)
    for step in range(ITERS):
        shift_own, shift_slot, image_sq = forward(dir_s, dir_a)
        alpha = gamma / image_sq
        sol_s = sol_s + alpha * dir_s
        sol_a = sol_a + alpha * dir_a
        resid = resid - alpha * (weight_factor * shift_slot[None, :])
        if step + 1 < ITERS:
            zbar_own = zbar_own - alpha * (weight_sq_own * shift_own)
            zbar_slot = zbar_slot - alpha * (weight_sq * shift_slot)
            grad_s, grad_a, fresh = adjoint(zbar_own, zbar_slot)
            dir_s = grad_s + fresh / gamma * dir_s
            dir_a = grad_a + fresh / gamma * dir_a
            gamma = fresh
    mine_a = lax.dynamic_slice(sol_a, (lax.axis_index("tm") * knots,), (knots,))
    return (sol_s, mine_a, resid)


def solution(mesh):
    placed = (
        P(None, ("tm", "src")),
        P(None, ("tm", "src")),
        P(),
        P(("tm", "src")),
        P(("tm", "src")),
        P(("tm", "src")),
        P(("tm", "src"), None),
        P(("tm", "src"), None),
    )
    return jax.shard_map(
        per_device,
        mesh=mesh,
        in_specs=placed,
        out_specs=(P(None, ("tm", "src")), P("tm"), P(None, ("tm", "src"))),
        check_vma=False,
    )
```

```python
import jax
import jax.numpy as jnp
from jax import lax
from jax.experimental import pallas as pl
from jax.experimental.pallas import tpu as pltpu
from jax.sharding import PartitionSpec as P

SRC_DEV = 32768
KN = 1024
ITERS = 2
HI = 256
CHUNK = 512


def passed_along(block, axis, distance):
    devices = range(lax.axis_size(axis))
    route = [(i - distance, i) for i in devices if i - distance in devices]
    return lax.ppermute(block, axis, route)


def spline_basis(frac):
    u2 = frac * frac
    u3 = u2 * frac
    one = 1.0 - frac
    return [
        one * one * one / 6.0,
        (3.0 * u3 - 6.0 * u2 + 4.0) / 6.0,
        (-3.0 * u3 + 3.0 * u2 + 3.0 * frac + 1.0) / 6.0,
        u3 / 6.0,
    ]


def pieces(x):
    h = x.astype(jnp.bfloat16)
    m = (x - h.astype(jnp.float32)).astype(jnp.bfloat16)
    return h, m


def hot_rows(ids, width):
    low = jnp.bitwise_and(ids, HI - 1)
    return (lax.broadcasted_iota(jnp.int32, (HI, width), 0) == low).astype(jnp.bfloat16)


def group_mask(ids, rows, width, groups):
    high = lax.shift_right_logical(ids, 8)
    iota = lax.broadcasted_iota(jnp.int32, (rows, width), 0)
    return (iota % groups) == high


def chunks(total, body):
    def step(i, carry):
        body(pl.multiple_of(i * CHUNK, CHUNK))
        return carry

    lax.fori_loop(0, total // CHUNK, step, 0)


def split_into(src_ref, big_ref):
    rows = src_ref.shape[0]
    for k, part in enumerate(pieces(src_ref[...])):
        big_ref[k * rows:(k + 1) * rows, :] = part


def source_gather(table, ids):
    n, width = table.shape
    cols = width // HI
    rows = n * cols
    total = ids.shape[1]

    def kernel(tab_ref, ids_ref, out_ref, big_ref):
        split_into(tab_ref, big_ref)

        def body(off):
            idc = ids_ref[:, pl.ds(off, CHUNK)]
            picked = jnp.dot(big_ref[...], hot_rows(idc, CHUNK), preferred_element_type=jnp.float32)
            sel = group_mask(idc, cols, CHUNK, cols)
            for p in range(n):
                acc = (
                    picked[p * cols:(p + 1) * cols]
                    + picked[rows + p * cols:rows + (p + 1) * cols]
                )
                out_ref[pl.ds(p, 1), pl.ds(off, CHUNK)] = jnp.sum(
                    jnp.where(sel, acc, 0.0), axis=0, keepdims=True
                )

        chunks(total, body)

    return pl.pallas_call(
        kernel,
        out_shape=jax.ShapeDtypeStruct((n, total), jnp.float32),
        scratch_shapes=[pltpu.VMEM((2 * rows, HI), jnp.bfloat16)],
    )(table.reshape(rows, HI), ids)


def source_scatter(values, ids, width):
    n, total = values.shape
    cols = width // HI
    rows = n * cols

    def kernel(val_ref, ids_ref, out_ref):
        out_ref[...] = jnp.zeros(out_ref.shape, jnp.float32)

        def body(off):
            idc = ids_ref[:, pl.ds(off, CHUNK)]
            v = val_ref[:, pl.ds(off, CHUNK)]
            sel = group_mask(idc, cols, CHUNK, cols)
            parts = []
            for piece in pieces(v):
                for p in range(n):
                    parts.append(jnp.where(sel, piece[p:p + 1, :], jnp.zeros((), jnp.bfloat16)))
            spread = jnp.concatenate(parts, axis=0)
            res = lax.dot_general(
                spread, hot_rows(idc, CHUNK), (((1,), (1,)), ((), ())),
                preferred_element_type=jnp.float32,
            )
            out_ref[...] += res[:rows] + res[rows:]

        chunks(total, body)

    out = pl.pallas_call(
        kernel, out_shape=jax.ShapeDtypeStruct((rows, HI), jnp.float32)
    )(values, ids)
    return out.reshape(n, width)


def knot_gather(extended, first_ids, basis, knots):
    total = first_ids.shape[1]
    cols = knots // HI
    shifted = jnp.stack([extended[q:q + knots] for q in range(4)], axis=0)
    rows = 4 * cols

    def kernel(tab_ref, ids_ref, basis_ref, out_ref, big_ref):
        split_into(tab_ref, big_ref)

        def body(off):
            idc = ids_ref[:, pl.ds(off, CHUNK)]
            picked = jnp.dot(big_ref[...], hot_rows(idc, CHUNK), preferred_element_type=jnp.float32)
            acc = picked[:rows] + picked[rows:]
            sel = group_mask(idc, cols, CHUNK, cols)
            b = basis_ref[:, pl.ds(off, CHUNK)]
            z = jnp.zeros((1, CHUNK), jnp.float32)
            for q in range(4):
                value = jnp.sum(jnp.where(sel, acc[q * cols:(q + 1) * cols], 0.0), axis=0, keepdims=True)
                z = z + b[q:q + 1] * value
            out_ref[:, pl.ds(off, CHUNK)] = z

        chunks(total, body)

    return pl.pallas_call(
        kernel,
        out_shape=jax.ShapeDtypeStruct((1, total), jnp.float32),
        scratch_shapes=[pltpu.VMEM((2 * rows, HI), jnp.bfloat16)],
    )(shifted.reshape(rows, HI), first_ids, basis)


def knot_scatter(values, first_ids, basis16, knots):
    total = first_ids.shape[1]
    cols = knots // HI
    rows = 4 * cols

    def kernel(val_ref, ids_ref, basis_ref, out_ref):
        out_ref[...] = jnp.zeros(out_ref.shape, jnp.float32)

        def body(off):
            idc = ids_ref[:, pl.ds(off, CHUNK)]
            sel = group_mask(idc, rows, CHUNK, cols)
            v = jnp.where(sel, basis_ref[:, pl.ds(off, CHUNK)] * val_ref[:, pl.ds(off, CHUNK)], 0.0)
            spread = jnp.concatenate(pieces(v), axis=0)
            res = lax.dot_general(
                spread, hot_rows(idc, CHUNK), (((1,), (1,)), ((), ())),
                preferred_element_type=jnp.float32,
            )
            out_ref[...] += res[:rows] + res[rows:]

        chunks(total, body)

    out = pl.pallas_call(
        kernel, out_shape=jax.ShapeDtypeStruct((rows, HI), jnp.float32)
    )(values, first_ids, basis16)
    per_shift = out.reshape(4, knots)
    grad = jnp.zeros((knots + 3,), jnp.float32)
    for q in range(4):
        grad = grad.at[q:q + knots].add(per_shift[q])
    return grad


def per_device(
    observed_residual,
    source_partials,
    spread_derivative_table,
    detector_index,
    first_knot_interval,
    interval_fraction,
    live_slot_count,
    slot_owned_source,
):
    rows = observed_residual.shape[1]
    n_time = lax.axis_size("tm")
    n_share = lax.axis_size("src")
    n_ranks = n_time * n_share
    capacity = rows // n_ranks
    n_params = source_partials.shape[0]
    detector_count = spread_derivative_table.shape[1]
    knots = KN
    n_knots = n_time * knots
    owned = SRC_DEV
    everyone = ("tm", "src")
    place = jnp.arange(capacity, dtype=jnp.int32)[None, :]
    live = (place < live_slot_count[0][:, None]).astype(jnp.float32).reshape(rows)
    indicator = (
        detector_index[None, :] == jnp.arange(detector_count, dtype=jnp.int32)[:, None]
    ).astype(jnp.float32)
    weight_factor = jnp.dot(
        spread_derivative_table,
        indicator,
        precision=lax.Precision.HIGHEST,
        preferred_element_type=jnp.float32,
    )
    weight_sq = jnp.sum(weight_factor * weight_factor, axis=0)
    basis16 = jnp.repeat(jnp.stack(spline_basis(interval_fraction), axis=0), knots // HI, axis=0)
    first_ids = first_knot_interval.reshape(1, rows)
    ids = slot_owned_source[0].reshape(1, rows)
    zbar0 = live * jnp.sum(weight_factor * observed_residual, axis=0)

    packed = jnp.concatenate(
        [
            source_partials,
            zbar0[None],
            weight_sq[None],
            live[None],
            interval_fraction[None],
            first_knot_interval.astype(jnp.float32)[None],
        ],
        axis=0,
    )
    got = lax.all_to_all(packed, everyone, split_axis=1, concat_axis=1, tiled=True)
    held = got[:n_params]
    zbar0_own = got[n_params]
    weight_sq_own = got[n_params + 1]
    live_own = got[n_params + 2]
    basis_own = jnp.stack(spline_basis(got[n_params + 3]), axis=0)
    slot_device = jnp.arange(rows, dtype=jnp.int32) // capacity
    base_own = ((slot_device // n_share) * knots + got[n_params + 4].astype(jnp.int32)).reshape(1, rows)

    def adjoint(zbar_own, zbar_slot):
        grad_s = source_scatter(held * zbar_own[None, :], ids, owned)
        part_a = knot_scatter(zbar_slot.reshape(1, rows), first_ids, basis16, knots)
        mine = jnp.concatenate([part_a, jnp.sum(grad_s * grad_s)[None]])
        every = lax.all_to_all(
            jnp.broadcast_to(mine[None, :], (n_ranks, knots + 4)), everyone, 0, 0, tiled=True
        )
        block = jnp.sum(every[:, :knots + 3].reshape(n_time, n_share, knots + 3), axis=1)
        main = block[:, :knots].at[1:, :3].add(block[:-1, knots:])
        grad_a = main.reshape(n_knots)
        norm = jnp.sum(every[:, knots + 3]) + jnp.sum(grad_a * grad_a)
        return grad_s, grad_a, norm

    def forward(dir_s, dir_a):
        pulled = source_gather(dir_s, ids)
        zsrc = jnp.sum(held * pulled, axis=0)
        extended = jnp.concatenate([dir_a, jnp.zeros((3,), jnp.float32)])
        zatt = knot_gather(extended, base_own, basis_own, n_knots).reshape(rows)
        shift_own = (zsrc + zatt) * live_own
        partial = jnp.sum(weight_sq_own * shift_own * shift_own)
        payload = jnp.concatenate(
            [shift_own.reshape(n_ranks, capacity), jnp.broadcast_to(partial, (n_ranks, 1))], axis=1
        )
        back = lax.all_to_all(payload, everyone, 0, 0, tiled=True)
        return shift_own, back[:, :capacity].reshape(rows), jnp.sum(back[:, capacity])

    sol_s = jnp.zeros((n_params, owned), jnp.float32)
    sol_a = jnp.zeros((n_knots,), jnp.float32)
    resid = observed_residual
    zbar_own, zbar_slot = zbar0_own, zbar0
    grad_s, grad_a, gamma = adjoint(zbar_own, zbar_slot)
    dir_s, dir_a = (grad_s, grad_a)
    for step in range(ITERS):
        shift_own, shift_slot, image_sq = forward(dir_s, dir_a)
        alpha = gamma / image_sq
        sol_s = sol_s + alpha * dir_s
        sol_a = sol_a + alpha * dir_a
        resid = resid - alpha * (weight_factor * shift_slot[None, :])
        if step + 1 < ITERS:
            zbar_own = zbar_own - alpha * (weight_sq_own * shift_own)
            zbar_slot = zbar_slot - alpha * (weight_sq * shift_slot)
            grad_s, grad_a, fresh = adjoint(zbar_own, zbar_slot)
            dir_s = grad_s + fresh / gamma * dir_s
            dir_a = grad_a + fresh / gamma * dir_a
            gamma = fresh
    mine_a = lax.dynamic_slice(sol_a, (lax.axis_index("tm") * knots,), (knots,))
    return (sol_s, mine_a, resid)


def solution(mesh):
    placed = (
        P(None, ("tm", "src")),
        P(None, ("tm", "src")),
        P(),
        P(("tm", "src")),
        P(("tm", "src")),
        P(("tm", "src")),
        P(("tm", "src"), None),
        P(("tm", "src"), None),
    )
    return jax.shard_map(
        per_device,
        mesh=mesh,
        in_specs=placed,
        out_specs=(P(None, ("tm", "src")), P("tm"), P(None, ("tm", "src"))),
        check_vma=False,
    )
```

```python
import jax
import jax.numpy as jnp
from jax import lax
from jax.experimental import pallas as pl
from jax.experimental.pallas import tpu as pltpu
from jax.sharding import PartitionSpec as P

SRC_DEV = 32768
KN = 1024
ITERS = 2
HI = 256
CHUNK = 512


def passed_along(block, axis, distance):
    devices = range(lax.axis_size(axis))
    route = [(i - distance, i) for i in devices if i - distance in devices]
    return lax.ppermute(block, axis, route)


def spline_basis(frac):
    u2 = frac * frac
    u3 = u2 * frac
    one = 1.0 - frac
    return [
        one * one * one / 6.0,
        (3.0 * u3 - 6.0 * u2 + 4.0) / 6.0,
        (-3.0 * u3 + 3.0 * u2 + 3.0 * frac + 1.0) / 6.0,
        u3 / 6.0,
    ]


def pieces(x):
    h = x.astype(jnp.bfloat16)
    m = (x - h.astype(jnp.float32)).astype(jnp.bfloat16)
    return h, m


def hot_rows(ids, width):
    low = jnp.bitwise_and(ids, HI - 1)
    return (lax.broadcasted_iota(jnp.int32, (HI, width), 0) == low).astype(jnp.bfloat16)


def group_mask(ids, rows, width, groups):
    high = lax.shift_right_logical(ids, 8)
    iota = lax.broadcasted_iota(jnp.int32, (rows, width), 0)
    return (iota % groups) == high


def chunks(total, body):
    def step(i, carry):
        body(pl.multiple_of(i * CHUNK, CHUNK))
        return carry

    lax.fori_loop(0, total // CHUNK, step, 0)


def split_into(src_ref, big_ref):
    rows = src_ref.shape[0]
    for k, part in enumerate(pieces(src_ref[...])):
        big_ref[k * rows:(k + 1) * rows, :] = part


def source_gather(table, ids):
    n, width = table.shape
    cols = width // HI
    rows = n * cols
    total = ids.shape[1]

    def kernel(tab_ref, ids_ref, out_ref, big_ref):
        split_into(tab_ref, big_ref)

        def body(off):
            idc = ids_ref[:, pl.ds(off, CHUNK)]
            picked = jnp.dot(big_ref[...], hot_rows(idc, CHUNK), preferred_element_type=jnp.float32)
            sel = group_mask(idc, cols, CHUNK, cols)
            for p in range(n):
                acc = (
                    picked[p * cols:(p + 1) * cols]
                    + picked[rows + p * cols:rows + (p + 1) * cols]
                )
                out_ref[pl.ds(p, 1), pl.ds(off, CHUNK)] = jnp.sum(
                    jnp.where(sel, acc, 0.0), axis=0, keepdims=True
                )

        chunks(total, body)

    return pl.pallas_call(
        kernel,
        out_shape=jax.ShapeDtypeStruct((n, total), jnp.float32),
        scratch_shapes=[pltpu.VMEM((2 * rows, HI), jnp.bfloat16)],
    )(table.reshape(rows, HI), ids)


def source_scatter(values, ids, width):
    n, total = values.shape
    cols = width // HI
    rows = n * cols

    def kernel(val_ref, ids_ref, out_ref):
        out_ref[...] = jnp.zeros(out_ref.shape, jnp.float32)

        def body(off):
            idc = ids_ref[:, pl.ds(off, CHUNK)]
            v = val_ref[:, pl.ds(off, CHUNK)]
            sel = group_mask(idc, cols, CHUNK, cols)
            parts = []
            for piece in pieces(v):
                for p in range(n):
                    parts.append(jnp.where(sel, piece[p:p + 1, :], jnp.zeros((), jnp.bfloat16)))
            spread = jnp.concatenate(parts, axis=0)
            res = lax.dot_general(
                spread, hot_rows(idc, CHUNK), (((1,), (1,)), ((), ())),
                preferred_element_type=jnp.float32,
            )
            out_ref[...] += res[:rows] + res[rows:]

        chunks(total, body)

    out = pl.pallas_call(
        kernel, out_shape=jax.ShapeDtypeStruct((rows, HI), jnp.float32)
    )(values, ids)
    return out.reshape(n, width)


def knot_gather(extended, first_ids, basis, knots):
    total = first_ids.shape[1]
    cols = knots // HI
    shifted = jnp.stack([extended[q:q + knots] for q in range(4)], axis=0)
    rows = 4 * cols

    def kernel(tab_ref, ids_ref, basis_ref, out_ref, big_ref):
        split_into(tab_ref, big_ref)

        def body(off):
            idc = ids_ref[:, pl.ds(off, CHUNK)]
            picked = jnp.dot(big_ref[...], hot_rows(idc, CHUNK), preferred_element_type=jnp.float32)
            acc = picked[:rows] + picked[rows:]
            sel = group_mask(idc, cols, CHUNK, cols)
            b = basis_ref[:, pl.ds(off, CHUNK)]
            z = jnp.zeros((1, CHUNK), jnp.float32)
            for q in range(4):
                value = jnp.sum(jnp.where(sel, acc[q * cols:(q + 1) * cols], 0.0), axis=0, keepdims=True)
                z = z + b[q:q + 1] * value
            out_ref[:, pl.ds(off, CHUNK)] = z

        chunks(total, body)

    return pl.pallas_call(
        kernel,
        out_shape=jax.ShapeDtypeStruct((1, total), jnp.float32),
        scratch_shapes=[pltpu.VMEM((2 * rows, HI), jnp.bfloat16)],
    )(shifted.reshape(rows, HI), first_ids, basis)


def knot_scatter(values, first_ids, basis16, knots):
    total = first_ids.shape[1]
    cols = knots // HI
    rows = 4 * cols

    def kernel(val_ref, ids_ref, basis_ref, out_ref):
        out_ref[...] = jnp.zeros(out_ref.shape, jnp.float32)

        def body(off):
            idc = ids_ref[:, pl.ds(off, CHUNK)]
            sel = group_mask(idc, rows, CHUNK, cols)
            v = jnp.where(sel, basis_ref[:, pl.ds(off, CHUNK)] * val_ref[:, pl.ds(off, CHUNK)], 0.0)
            spread = jnp.concatenate(pieces(v), axis=0)
            res = lax.dot_general(
                spread, hot_rows(idc, CHUNK), (((1,), (1,)), ((), ())),
                preferred_element_type=jnp.float32,
            )
            out_ref[...] += res[:rows] + res[rows:]

        chunks(total, body)

    out = pl.pallas_call(
        kernel, out_shape=jax.ShapeDtypeStruct((rows, HI), jnp.float32)
    )(values, first_ids, basis16)
    per_shift = out.reshape(4, knots)
    grad = jnp.zeros((knots + 3,), jnp.float32)
    for q in range(4):
        grad = grad.at[q:q + knots].add(per_shift[q])
    return grad


def per_device(
    observed_residual,
    source_partials,
    spread_derivative_table,
    detector_index,
    first_knot_interval,
    interval_fraction,
    live_slot_count,
    slot_owned_source,
):
    rows = observed_residual.shape[1]
    n_time = lax.axis_size("tm")
    n_share = lax.axis_size("src")
    n_ranks = n_time * n_share
    capacity = rows // n_ranks
    n_params = source_partials.shape[0]
    detector_count = spread_derivative_table.shape[1]
    knots = KN
    n_knots = n_time * knots
    owned = SRC_DEV
    everyone = ("tm", "src")
    place = jnp.arange(capacity, dtype=jnp.int32)[None, :]
    live = (place < live_slot_count[0][:, None]).astype(jnp.float32).reshape(rows)
    indicator = (
        detector_index[None, :] == jnp.arange(detector_count, dtype=jnp.int32)[:, None]
    ).astype(jnp.float32)
    weight_factor = jnp.dot(
        spread_derivative_table,
        indicator,
        precision=lax.Precision.HIGHEST,
        preferred_element_type=jnp.float32,
    )
    weight_sq = jnp.sum(weight_factor * weight_factor, axis=0)
    basis16 = jnp.repeat(jnp.stack(spline_basis(interval_fraction), axis=0), knots // HI, axis=0)
    first_ids = first_knot_interval.reshape(1, rows)
    ids = slot_owned_source[0].reshape(1, rows)
    zbar0 = live * jnp.sum(weight_factor * observed_residual, axis=0)

    packed = jnp.concatenate(
        [
            source_partials,
            zbar0[None],
            weight_sq[None],
            live[None],
            interval_fraction[None],
            first_knot_interval.astype(jnp.float32)[None],
        ],
        axis=0,
    )
    got = lax.all_to_all(packed, everyone, split_axis=1, concat_axis=1, tiled=True)
    held = got[:n_params]
    zbar0_own = got[n_params]
    weight_sq_own = got[n_params + 1]
    live_own = got[n_params + 2]
    basis_own = jnp.stack(spline_basis(got[n_params + 3]), axis=0)
    slot_device = jnp.arange(rows, dtype=jnp.int32) // capacity
    base_own = ((slot_device // n_share) * knots + got[n_params + 4].astype(jnp.int32)).reshape(1, rows)

    def combine(part_a, grad_s):
        mine = jnp.concatenate([part_a, jnp.sum(grad_s * grad_s)[None]])
        every = lax.all_to_all(
            jnp.broadcast_to(mine[None, :], (n_ranks, knots + 4)), everyone, 0, 0, tiled=True
        )
        block = jnp.sum(every[:, :knots + 3].reshape(n_time, n_share, knots + 3), axis=1)
        main = block[:, :knots].at[1:, :3].add(block[:-1, knots:])
        grad_a = main.reshape(n_knots)
        norm = jnp.sum(every[:, knots + 3]) + jnp.sum(grad_a * grad_a)
        return grad_a, norm

    def forward(pulled, dir_a):
        zsrc = jnp.sum(held * pulled, axis=0)
        extended = jnp.concatenate([dir_a, jnp.zeros((3,), jnp.float32)])
        zatt = knot_gather(extended, base_own, basis_own, n_knots).reshape(rows)
        shift_own = (zsrc + zatt) * live_own
        partial = jnp.sum(weight_sq_own * shift_own * shift_own)
        payload = jnp.concatenate(
            [shift_own.reshape(n_ranks, capacity), jnp.broadcast_to(partial, (n_ranks, 1))], axis=1
        )
        back = lax.all_to_all(payload, everyone, 0, 0, tiled=True)
        return shift_own, back[:, :capacity].reshape(rows), jnp.sum(back[:, capacity])

    sol_s = jnp.zeros((n_params, owned), jnp.float32)
    sol_a = jnp.zeros((n_knots,), jnp.float32)
    resid = observed_residual
    zbar_slot = zbar0
    grad_s = source_scatter(held * zbar0_own[None, :], ids, owned)
    grad_a, gamma = combine(knot_scatter(zbar_slot.reshape(1, rows), first_ids, basis16, knots), grad_s)
    dir_s, dir_a = (grad_s, grad_a)
    pulled = source_gather(dir_s, ids)
    for step in range(ITERS):
        shift_own, shift_slot, image_sq = forward(pulled, dir_a)
        alpha = gamma / image_sq
        sol_s = sol_s + alpha * dir_s
        sol_a = sol_a + alpha * dir_a
        resid = resid - alpha * (weight_factor * shift_slot[None, :])
        if step + 1 < ITERS:
            pushed = source_scatter(held * (weight_sq_own * shift_own)[None, :], ids, owned)
            zbar_slot = zbar_slot - alpha * (weight_sq * shift_slot)
            grad_s = grad_s - alpha * pushed
            grad_a, fresh = combine(
                knot_scatter(zbar_slot.reshape(1, rows), first_ids, basis16, knots), grad_s
            )
            raw = source_gather(grad_s, ids)
            beta = fresh / gamma
            dir_s = grad_s + beta * dir_s
            dir_a = grad_a + beta * dir_a
            pulled = raw + beta * pulled
            gamma = fresh
    mine_a = lax.dynamic_slice(sol_a, (lax.axis_index("tm") * knots,), (knots,))
    return (sol_s, mine_a, resid)


def solution(mesh):
    placed = (
        P(None, ("tm", "src")),
        P(None, ("tm", "src")),
        P(),
        P(("tm", "src")),
        P(("tm", "src")),
        P(("tm", "src")),
        P(("tm", "src"), None),
        P(("tm", "src"), None),
    )
    return jax.shard_map(
        per_device,
        mesh=mesh,
        in_specs=placed,
        out_specs=(P(None, ("tm", "src")), P("tm"), P(None, ("tm", "src"))),
        check_vma=False,
    )
```

```python
import jax
import jax.numpy as jnp
from jax import lax
from jax.experimental import pallas as pl
from jax.experimental.pallas import tpu as pltpu
from jax.sharding import PartitionSpec as P

SRC_DEV = 32768
KN = 1024
ITERS = 2
HI = 256
CHUNK = 2048


def passed_along(block, axis, distance):
    devices = range(lax.axis_size(axis))
    route = [(i - distance, i) for i in devices if i - distance in devices]
    return lax.ppermute(block, axis, route)


def spline_basis(frac):
    u2 = frac * frac
    u3 = u2 * frac
    one = 1.0 - frac
    return [
        one * one * one / 6.0,
        (3.0 * u3 - 6.0 * u2 + 4.0) / 6.0,
        (-3.0 * u3 + 3.0 * u2 + 3.0 * frac + 1.0) / 6.0,
        u3 / 6.0,
    ]


def pieces(x):
    h = x.astype(jnp.bfloat16)
    m = (x - h.astype(jnp.float32)).astype(jnp.bfloat16)
    return h, m


def hot_rows(ids, width):
    low = jnp.bitwise_and(ids, HI - 1)
    return (lax.broadcasted_iota(jnp.int32, (HI, width), 0) == low).astype(jnp.bfloat16)


def group_mask(ids, rows, width, groups):
    high = lax.shift_right_logical(ids, 8)
    iota = lax.broadcasted_iota(jnp.int32, (rows, width), 0)
    return (iota % groups) == high


def chunks(total, body):
    def step(i, carry):
        body(pl.multiple_of(i * CHUNK, CHUNK))
        return carry

    lax.fori_loop(0, total // CHUNK, step, 0)


def split_into(src_ref, big_ref):
    rows = src_ref.shape[0]
    for k, part in enumerate(pieces(src_ref[...])):
        big_ref[k * rows:(k + 1) * rows, :] = part


def source_gather(table, ids):
    n, width = table.shape
    cols = width // HI
    rows = n * cols
    total = ids.shape[1]

    def kernel(tab_ref, ids_ref, out_ref, big_ref):
        split_into(tab_ref, big_ref)

        def body(off):
            idc = ids_ref[:, pl.ds(off, CHUNK)]
            picked = jnp.dot(big_ref[...], hot_rows(idc, CHUNK), preferred_element_type=jnp.float32)
            sel = group_mask(idc, cols, CHUNK, cols)
            for p in range(n):
                acc = (
                    picked[p * cols:(p + 1) * cols]
                    + picked[rows + p * cols:rows + (p + 1) * cols]
                )
                out_ref[pl.ds(p, 1), pl.ds(off, CHUNK)] = jnp.sum(
                    jnp.where(sel, acc, 0.0), axis=0, keepdims=True
                )

        chunks(total, body)

    return pl.pallas_call(
        kernel,
        out_shape=jax.ShapeDtypeStruct((n, total), jnp.float32),
        scratch_shapes=[pltpu.VMEM((2 * rows, HI), jnp.bfloat16)],
    )(table.reshape(rows, HI), ids)


def source_scatter(values, ids, width):
    n, total = values.shape
    cols = width // HI
    rows = n * cols

    def kernel(val_ref, ids_ref, out_ref):
        out_ref[...] = jnp.zeros(out_ref.shape, jnp.float32)

        def body(off):
            idc = ids_ref[:, pl.ds(off, CHUNK)]
            v = val_ref[:, pl.ds(off, CHUNK)]
            sel = group_mask(idc, cols, CHUNK, cols)
            parts = []
            for piece in pieces(v):
                for p in range(n):
                    parts.append(jnp.where(sel, piece[p:p + 1, :], jnp.zeros((), jnp.bfloat16)))
            spread = jnp.concatenate(parts, axis=0)
            res = lax.dot_general(
                spread, hot_rows(idc, CHUNK), (((1,), (1,)), ((), ())),
                preferred_element_type=jnp.float32,
            )
            out_ref[...] += res[:rows] + res[rows:]

        chunks(total, body)

    out = pl.pallas_call(
        kernel, out_shape=jax.ShapeDtypeStruct((rows, HI), jnp.float32)
    )(values, ids)
    return out.reshape(n, width)


def knot_gather(extended, first_ids, basis, knots):
    total = first_ids.shape[1]
    cols = knots // HI
    shifted = jnp.stack([extended[q:q + knots] for q in range(4)], axis=0)
    rows = 4 * cols

    def kernel(tab_ref, ids_ref, basis_ref, out_ref, big_ref):
        split_into(tab_ref, big_ref)

        def body(off):
            idc = ids_ref[:, pl.ds(off, CHUNK)]
            picked = jnp.dot(big_ref[...], hot_rows(idc, CHUNK), preferred_element_type=jnp.float32)
            acc = picked[:rows] + picked[rows:]
            sel = group_mask(idc, cols, CHUNK, cols)
            b = basis_ref[:, pl.ds(off, CHUNK)]
            z = jnp.zeros((1, CHUNK), jnp.float32)
            for q in range(4):
                value = jnp.sum(jnp.where(sel, acc[q * cols:(q + 1) * cols], 0.0), axis=0, keepdims=True)
                z = z + b[q:q + 1] * value
            out_ref[:, pl.ds(off, CHUNK)] = z

        chunks(total, body)

    return pl.pallas_call(
        kernel,
        out_shape=jax.ShapeDtypeStruct((1, total), jnp.float32),
        scratch_shapes=[pltpu.VMEM((2 * rows, HI), jnp.bfloat16)],
    )(shifted.reshape(rows, HI), first_ids, basis)


def knot_scatter(values, first_ids, basis16, knots):
    total = first_ids.shape[1]
    cols = knots // HI
    rows = 4 * cols

    def kernel(val_ref, ids_ref, basis_ref, out_ref):
        out_ref[...] = jnp.zeros(out_ref.shape, jnp.float32)

        def body(off):
            idc = ids_ref[:, pl.ds(off, CHUNK)]
            sel = group_mask(idc, rows, CHUNK, cols)
            v = jnp.where(sel, basis_ref[:, pl.ds(off, CHUNK)] * val_ref[:, pl.ds(off, CHUNK)], 0.0)
            spread = jnp.concatenate(pieces(v), axis=0)
            res = lax.dot_general(
                spread, hot_rows(idc, CHUNK), (((1,), (1,)), ((), ())),
                preferred_element_type=jnp.float32,
            )
            out_ref[...] += res[:rows] + res[rows:]

        chunks(total, body)

    out = pl.pallas_call(
        kernel, out_shape=jax.ShapeDtypeStruct((rows, HI), jnp.float32)
    )(values, first_ids, basis16)
    per_shift = out.reshape(4, knots)
    grad = jnp.zeros((knots + 3,), jnp.float32)
    for q in range(4):
        grad = grad.at[q:q + knots].add(per_shift[q])
    return grad


def per_device(
    observed_residual,
    source_partials,
    spread_derivative_table,
    detector_index,
    first_knot_interval,
    interval_fraction,
    live_slot_count,
    slot_owned_source,
):
    rows = observed_residual.shape[1]
    n_time = lax.axis_size("tm")
    n_share = lax.axis_size("src")
    n_ranks = n_time * n_share
    capacity = rows // n_ranks
    n_params = source_partials.shape[0]
    detector_count = spread_derivative_table.shape[1]
    knots = KN
    n_knots = n_time * knots
    owned = SRC_DEV
    everyone = ("tm", "src")
    place = jnp.arange(capacity, dtype=jnp.int32)[None, :]
    live = (place < live_slot_count[0][:, None]).astype(jnp.float32).reshape(rows)
    indicator = (
        detector_index[None, :] == jnp.arange(detector_count, dtype=jnp.int32)[:, None]
    ).astype(jnp.float32)
    weight_factor = jnp.dot(
        spread_derivative_table,
        indicator,
        precision=lax.Precision.HIGHEST,
        preferred_element_type=jnp.float32,
    )
    weight_sq = jnp.sum(weight_factor * weight_factor, axis=0)
    basis16 = jnp.repeat(jnp.stack(spline_basis(interval_fraction), axis=0), knots // HI, axis=0)
    first_ids = first_knot_interval.reshape(1, rows)
    ids = slot_owned_source[0].reshape(1, rows)
    zbar0 = live * jnp.sum(weight_factor * observed_residual, axis=0)

    packed = jnp.concatenate(
        [
            source_partials,
            zbar0[None],
            weight_sq[None],
            live[None],
            interval_fraction[None],
            first_knot_interval.astype(jnp.float32)[None],
        ],
        axis=0,
    )
    got = lax.all_to_all(packed, everyone, split_axis=1, concat_axis=1, tiled=True)
    held = got[:n_params]
    zbar0_own = got[n_params]
    weight_sq_own = got[n_params + 1]
    live_own = got[n_params + 2]
    basis_own = jnp.stack(spline_basis(got[n_params + 3]), axis=0)
    slot_device = jnp.arange(rows, dtype=jnp.int32) // capacity
    base_own = ((slot_device // n_share) * knots + got[n_params + 4].astype(jnp.int32)).reshape(1, rows)

    def combine(part_a, grad_s):
        mine = jnp.concatenate([part_a, jnp.sum(grad_s * grad_s)[None]])
        every = lax.all_to_all(
            jnp.broadcast_to(mine[None, :], (n_ranks, knots + 4)), everyone, 0, 0, tiled=True
        )
        block = jnp.sum(every[:, :knots + 3].reshape(n_time, n_share, knots + 3), axis=1)
        main = block[:, :knots].at[1:, :3].add(block[:-1, knots:])
        grad_a = main.reshape(n_knots)
        norm = jnp.sum(every[:, knots + 3]) + jnp.sum(grad_a * grad_a)
        return grad_a, norm

    def forward(pulled, dir_a):
        zsrc = jnp.sum(held * pulled, axis=0)
        extended = jnp.concatenate([dir_a, jnp.zeros((3,), jnp.float32)])
        zatt = knot_gather(extended, base_own, basis_own, n_knots).reshape(rows)
        shift_own = (zsrc + zatt) * live_own
        partial = jnp.sum(weight_sq_own * shift_own * shift_own)
        payload = jnp.concatenate(
            [shift_own.reshape(n_ranks, capacity), jnp.broadcast_to(partial, (n_ranks, 1))], axis=1
        )
        back = lax.all_to_all(payload, everyone, 0, 0, tiled=True)
        return shift_own, back[:, :capacity].reshape(rows), jnp.sum(back[:, capacity])

    sol_s = jnp.zeros((n_params, owned), jnp.float32)
    sol_a = jnp.zeros((n_knots,), jnp.float32)
    resid = observed_residual
    zbar_slot = zbar0
    grad_s = source_scatter(held * zbar0_own[None, :], ids, owned)
    grad_a, gamma = combine(knot_scatter(zbar_slot.reshape(1, rows), first_ids, basis16, knots), grad_s)
    dir_s, dir_a = (grad_s, grad_a)
    pulled = source_gather(dir_s, ids)
    for step in range(ITERS):
        shift_own, shift_slot, image_sq = forward(pulled, dir_a)
        alpha = gamma / image_sq
        sol_s = sol_s + alpha * dir_s
        sol_a = sol_a + alpha * dir_a
        resid = resid - alpha * (weight_factor * shift_slot[None, :])
        if step + 1 < ITERS:
            pushed = source_scatter(held * (weight_sq_own * shift_own)[None, :], ids, owned)
            zbar_slot = zbar_slot - alpha * (weight_sq * shift_slot)
            grad_s = grad_s - alpha * pushed
            grad_a, fresh = combine(
                knot_scatter(zbar_slot.reshape(1, rows), first_ids, basis16, knots), grad_s
            )
            raw = source_gather(grad_s, ids)
            beta = fresh / gamma
            dir_s = grad_s + beta * dir_s
            dir_a = grad_a + beta * dir_a
            pulled = raw + beta * pulled
            gamma = fresh
    mine_a = lax.dynamic_slice(sol_a, (lax.axis_index("tm") * knots,), (knots,))
    return (sol_s, mine_a, resid)


def solution(mesh):
    placed = (
        P(None, ("tm", "src")),
        P(None, ("tm", "src")),
        P(),
        P(("tm", "src")),
        P(("tm", "src")),
        P(("tm", "src")),
        P(("tm", "src"), None),
        P(("tm", "src"), None),
    )
    return jax.shard_map(
        per_device,
        mesh=mesh,
        in_specs=placed,
        out_specs=(P(None, ("tm", "src")), P("tm"), P(None, ("tm", "src"))),
        check_vma=False,
    )
```

```python
import jax
import jax.numpy as jnp
from jax import lax
from jax.experimental import pallas as pl
from jax.experimental.pallas import tpu as pltpu
from jax.sharding import PartitionSpec as P

SRC_DEV = 32768
KN = 1024
ITERS = 2
HI = 256
CHUNK = 2048


def passed_along(block, axis, distance):
    devices = range(lax.axis_size(axis))
    route = [(i - distance, i) for i in devices if i - distance in devices]
    return lax.ppermute(block, axis, route)


def spline_basis(frac):
    u2 = frac * frac
    u3 = u2 * frac
    one = 1.0 - frac
    return [
        one * one * one / 6.0,
        (3.0 * u3 - 6.0 * u2 + 4.0) / 6.0,
        (-3.0 * u3 + 3.0 * u2 + 3.0 * frac + 1.0) / 6.0,
        u3 / 6.0,
    ]


def pieces(x):
    h = x.astype(jnp.bfloat16)
    m = (x - h.astype(jnp.float32)).astype(jnp.bfloat16)
    return h, m


def hot_rows(ids, width):
    low = jnp.bitwise_and(ids, HI - 1)
    return (lax.broadcasted_iota(jnp.int32, (HI, width), 0) == low).astype(jnp.bfloat16)


def group_mask(ids, rows, width, groups):
    high = lax.shift_right_logical(ids, 8)
    iota = lax.broadcasted_iota(jnp.int32, (rows, width), 0)
    return (iota % groups) == high


def chunks(total, body):
    def step(i, carry):
        body(pl.multiple_of(i * CHUNK, CHUNK))
        return carry

    lax.fori_loop(0, total // CHUNK, step, 0)


def split_into(src_ref, big_ref):
    rows = src_ref.shape[0]
    for k, part in enumerate(pieces(src_ref[...])):
        big_ref[k * rows:(k + 1) * rows, :] = part


def source_gather(table, ids, held):
    n, total = held.shape
    rows = table.shape[0]
    cols = rows // n

    def kernel(tab_ref, ids_ref, held_ref, out_ref, big_ref):
        split_into(tab_ref, big_ref)

        def body(off):
            idc = ids_ref[:, pl.ds(off, CHUNK)]
            picked = jnp.dot(big_ref[...], hot_rows(idc, CHUNK), preferred_element_type=jnp.float32)
            sel = group_mask(idc, cols, CHUNK, cols)
            weights = held_ref[:, pl.ds(off, CHUNK)]
            column = jnp.zeros((1, CHUNK), jnp.float32)
            for p in range(n):
                acc = (
                    picked[p * cols:(p + 1) * cols]
                    + picked[rows + p * cols:rows + (p + 1) * cols]
                )
                value = jnp.sum(jnp.where(sel, acc, 0.0), axis=0, keepdims=True)
                column = column + weights[p:p + 1] * value
            out_ref[:, pl.ds(off, CHUNK)] = column

        chunks(total, body)

    return pl.pallas_call(
        kernel,
        out_shape=jax.ShapeDtypeStruct((1, total), jnp.float32),
        scratch_shapes=[pltpu.VMEM((2 * rows, HI), jnp.bfloat16)],
    )(table, ids, held)


def source_scatter(values, ids, width):
    n, total = values.shape
    cols = width // HI
    rows = n * cols

    def kernel(val_ref, ids_ref, out_ref):
        out_ref[...] = jnp.zeros(out_ref.shape, jnp.float32)

        def body(off):
            idc = ids_ref[:, pl.ds(off, CHUNK)]
            v = val_ref[:, pl.ds(off, CHUNK)]
            sel = group_mask(idc, cols, CHUNK, cols)
            parts = []
            for piece in pieces(v):
                for p in range(n):
                    parts.append(jnp.where(sel, piece[p:p + 1, :], jnp.zeros((), jnp.bfloat16)))
            spread = jnp.concatenate(parts, axis=0)
            res = lax.dot_general(
                spread, hot_rows(idc, CHUNK), (((1,), (1,)), ((), ())),
                preferred_element_type=jnp.float32,
            )
            out_ref[...] += res[:rows] + res[rows:]

        chunks(total, body)

    return pl.pallas_call(
        kernel, out_shape=jax.ShapeDtypeStruct((rows, HI), jnp.float32)
    )(values, ids)


def knot_gather(extended, first_ids, basis, zsrc, weight, knots):
    total = first_ids.shape[1]
    cols = knots // HI
    shifted = jnp.stack([extended[q:q + knots] for q in range(4)], axis=0)
    rows = 4 * cols

    def kernel(tab_ref, ids_ref, basis_ref, zsrc_ref, weight_ref, out_ref, norm_ref, big_ref):
        split_into(tab_ref, big_ref)
        norm_ref[...] = jnp.zeros(norm_ref.shape, jnp.float32)

        def body(off):
            idc = ids_ref[:, pl.ds(off, CHUNK)]
            picked = jnp.dot(big_ref[...], hot_rows(idc, CHUNK), preferred_element_type=jnp.float32)
            acc = picked[:rows] + picked[rows:]
            sel = group_mask(idc, cols, CHUNK, cols)
            b = basis_ref[:, pl.ds(off, CHUNK)]
            z = jnp.zeros((1, CHUNK), jnp.float32)
            for q in range(4):
                value = jnp.sum(jnp.where(sel, acc[q * cols:(q + 1) * cols], 0.0), axis=0, keepdims=True)
                z = z + b[q:q + 1] * value
            shift = zsrc_ref[:, pl.ds(off, CHUNK)] + z
            out_ref[:, pl.ds(off, CHUNK)] = shift
            norm_ref[...] += jnp.sum(weight_ref[:, pl.ds(off, CHUNK)] * shift * shift, axis=1, keepdims=True)

        chunks(total, body)

    return pl.pallas_call(
        kernel,
        out_shape=(
            jax.ShapeDtypeStruct((1, total), jnp.float32),
            jax.ShapeDtypeStruct((1, 1), jnp.float32),
        ),
        scratch_shapes=[pltpu.VMEM((2 * rows, HI), jnp.bfloat16)],
    )(shifted.reshape(rows, HI), first_ids, basis, zsrc, weight)


def knot_scatter(values, first_ids, basis16, knots):
    total = first_ids.shape[1]
    cols = knots // HI
    rows = 4 * cols

    def kernel(val_ref, ids_ref, basis_ref, out_ref):
        out_ref[...] = jnp.zeros(out_ref.shape, jnp.float32)

        def body(off):
            idc = ids_ref[:, pl.ds(off, CHUNK)]
            sel = group_mask(idc, rows, CHUNK, cols)
            v = jnp.where(sel, basis_ref[:, pl.ds(off, CHUNK)] * val_ref[:, pl.ds(off, CHUNK)], 0.0)
            spread = jnp.concatenate(pieces(v), axis=0)
            res = lax.dot_general(
                spread, hot_rows(idc, CHUNK), (((1,), (1,)), ((), ())),
                preferred_element_type=jnp.float32,
            )
            out_ref[...] += res[:rows] + res[rows:]

        chunks(total, body)

    out = pl.pallas_call(
        kernel, out_shape=jax.ShapeDtypeStruct((rows, HI), jnp.float32)
    )(values, first_ids, basis16)
    per_shift = out.reshape(4, knots)
    grad = jnp.zeros((knots + 3,), jnp.float32)
    for q in range(4):
        grad = grad.at[q:q + knots].add(per_shift[q])
    return grad


def per_device(
    observed_residual,
    source_partials,
    spread_derivative_table,
    detector_index,
    first_knot_interval,
    interval_fraction,
    live_slot_count,
    slot_owned_source,
):
    rows = observed_residual.shape[1]
    n_time = lax.axis_size("tm")
    n_share = lax.axis_size("src")
    n_ranks = n_time * n_share
    capacity = rows // n_ranks
    n_params = source_partials.shape[0]
    detector_count = spread_derivative_table.shape[1]
    knots = KN
    n_knots = n_time * knots
    owned = SRC_DEV
    everyone = ("tm", "src")
    place = jnp.arange(capacity, dtype=jnp.int32)[None, :]
    live = (place < live_slot_count[0][:, None]).astype(jnp.float32).reshape(rows)
    indicator = (
        detector_index[None, :] == jnp.arange(detector_count, dtype=jnp.int32)[:, None]
    ).astype(jnp.float32)
    weight_factor = jnp.dot(
        spread_derivative_table,
        indicator,
        precision=lax.Precision.HIGHEST,
        preferred_element_type=jnp.float32,
    )
    weight_sq = live * jnp.sum(weight_factor * weight_factor, axis=0)
    basis16 = jnp.repeat(jnp.stack(spline_basis(interval_fraction), axis=0), knots // HI, axis=0)
    first_ids = first_knot_interval.reshape(1, rows)
    ids = slot_owned_source[0].reshape(1, rows)
    zbar0 = live * jnp.sum(weight_factor * observed_residual, axis=0)

    packed = jnp.concatenate(
        [
            source_partials,
            zbar0[None],
            weight_sq[None],
            interval_fraction[None],
            first_knot_interval.astype(jnp.float32)[None],
        ],
        axis=0,
    )
    got = lax.all_to_all(packed, everyone, split_axis=1, concat_axis=1, tiled=True)
    held = got[:n_params]
    zbar0_own = got[n_params]
    weight_sq_own = got[n_params + 1]
    basis_own = jnp.stack(spline_basis(got[n_params + 2]), axis=0)
    slot_device = jnp.arange(rows, dtype=jnp.int32) // capacity
    base_own = ((slot_device // n_share) * knots + got[n_params + 3].astype(jnp.int32)).reshape(1, rows)
    table_rows = n_params * (owned // HI)

    def combine(part_a, grad_s):
        mine = jnp.concatenate([part_a, jnp.sum(grad_s * grad_s)[None]])
        every = lax.all_to_all(
            jnp.broadcast_to(mine[None, :], (n_ranks, knots + 4)), everyone, 0, 0, tiled=True
        )
        block = jnp.sum(every[:, :knots + 3].reshape(n_time, n_share, knots + 3), axis=1)
        main = block[:, :knots].at[1:, :3].add(block[:-1, knots:])
        grad_a = main.reshape(n_knots)
        norm = jnp.sum(every[:, knots + 3]) + jnp.sum(grad_a * grad_a)
        return grad_a, norm

    def forward(zsrc, dir_a):
        extended = jnp.concatenate([dir_a, jnp.zeros((3,), jnp.float32)])
        shift_own, partial = knot_gather(
            extended, base_own, basis_own, zsrc, weight_sq_own.reshape(1, rows), n_knots
        )
        shift_own = shift_own.reshape(rows)
        payload = jnp.concatenate(
            [shift_own.reshape(n_ranks, capacity), jnp.broadcast_to(partial, (n_ranks, 1))], axis=1
        )
        back = lax.all_to_all(payload, everyone, 0, 0, tiled=True)
        return shift_own, back[:, :capacity].reshape(rows) * live, jnp.sum(back[:, capacity])

    sol_s = jnp.zeros((table_rows, HI), jnp.float32)
    sol_a = jnp.zeros((n_knots,), jnp.float32)
    resid = observed_residual
    zbar_slot = zbar0
    grad_s = source_scatter(held * zbar0_own[None, :], ids, owned)
    grad_a, gamma = combine(knot_scatter(zbar_slot.reshape(1, rows), first_ids, basis16, knots), grad_s)
    dir_s, dir_a = (grad_s, grad_a)
    pulled = source_gather(dir_s, ids, held)
    for step in range(ITERS):
        shift_own, shift_slot, image_sq = forward(pulled, dir_a)
        alpha = gamma / image_sq
        sol_s = sol_s + alpha * dir_s
        sol_a = sol_a + alpha * dir_a
        resid = resid - alpha * (weight_factor * shift_slot[None, :])
        if step + 1 < ITERS:
            pushed = source_scatter(held * (weight_sq_own * shift_own)[None, :], ids, owned)
            zbar_slot = zbar_slot - alpha * (weight_sq * shift_slot)
            grad_s = grad_s - alpha * pushed
            grad_a, fresh = combine(
                knot_scatter(zbar_slot.reshape(1, rows), first_ids, basis16, knots), grad_s
            )
            raw = source_gather(grad_s, ids, held)
            beta = fresh / gamma
            dir_s = grad_s + beta * dir_s
            dir_a = grad_a + beta * dir_a
            pulled = raw + beta * pulled
            gamma = fresh
    mine_a = lax.dynamic_slice(sol_a, (lax.axis_index("tm") * knots,), (knots,))
    return (sol_s.reshape(n_params, owned), mine_a, resid)


def solution(mesh):
    placed = (
        P(None, ("tm", "src")),
        P(None, ("tm", "src")),
        P(),
        P(("tm", "src")),
        P(("tm", "src")),
        P(("tm", "src")),
        P(("tm", "src"), None),
        P(("tm", "src"), None),
    )
    return jax.shard_map(
        per_device,
        mesh=mesh,
        in_specs=placed,
        out_specs=(P(None, ("tm", "src")), P("tm"), P(None, ("tm", "src"))),
        check_vma=False,
    )
```

```python
import jax
import jax.numpy as jnp
from jax import lax
from jax.experimental import pallas as pl
from jax.experimental.pallas import tpu as pltpu
from jax.sharding import PartitionSpec as P

SRC_DEV = 32768
KN = 1024
ITERS = 2
HI = 256
CHUNK = 4096


def passed_along(block, axis, distance):
    devices = range(lax.axis_size(axis))
    route = [(i - distance, i) for i in devices if i - distance in devices]
    return lax.ppermute(block, axis, route)


def spline_basis(frac):
    u2 = frac * frac
    u3 = u2 * frac
    one = 1.0 - frac
    return [
        one * one * one / 6.0,
        (3.0 * u3 - 6.0 * u2 + 4.0) / 6.0,
        (-3.0 * u3 + 3.0 * u2 + 3.0 * frac + 1.0) / 6.0,
        u3 / 6.0,
    ]


def pieces(x):
    h = x.astype(jnp.bfloat16)
    m = (x - h.astype(jnp.float32)).astype(jnp.bfloat16)
    return h, m


def hot_rows(ids, width):
    low = jnp.bitwise_and(ids, HI - 1)
    return (lax.broadcasted_iota(jnp.int32, (HI, width), 0) == low).astype(jnp.bfloat16)


def group_mask(ids, rows, width, groups):
    high = lax.shift_right_logical(ids, 8)
    iota = lax.broadcasted_iota(jnp.int32, (rows, width), 0)
    return (iota % groups) == high


def chunks(total, body):
    def step(i, carry):
        body(pl.multiple_of(i * CHUNK, CHUNK))
        return carry

    lax.fori_loop(0, total // CHUNK, step, 0)


def split_into(src_ref, big_ref):
    rows = src_ref.shape[0]
    for k, part in enumerate(pieces(src_ref[...])):
        big_ref[k * rows:(k + 1) * rows, :] = part


def source_gather(table, ids, held):
    n, total = held.shape
    rows = table.shape[0]
    cols = rows // n

    def kernel(tab_ref, ids_ref, held_ref, out_ref, big_ref):
        split_into(tab_ref, big_ref)

        def body(off):
            idc = ids_ref[:, pl.ds(off, CHUNK)]
            picked = jnp.dot(big_ref[...], hot_rows(idc, CHUNK), preferred_element_type=jnp.float32)
            sel = group_mask(idc, cols, CHUNK, cols)
            weights = held_ref[:, pl.ds(off, CHUNK)]
            column = jnp.zeros((1, CHUNK), jnp.float32)
            for p in range(n):
                acc = (
                    picked[p * cols:(p + 1) * cols]
                    + picked[rows + p * cols:rows + (p + 1) * cols]
                )
                value = jnp.sum(jnp.where(sel, acc, 0.0), axis=0, keepdims=True)
                column = column + weights[p:p + 1] * value
            out_ref[:, pl.ds(off, CHUNK)] = column

        chunks(total, body)

    return pl.pallas_call(
        kernel,
        out_shape=jax.ShapeDtypeStruct((1, total), jnp.float32),
        scratch_shapes=[pltpu.VMEM((2 * rows, HI), jnp.bfloat16)],
    )(table, ids, held)


def source_scatter(values, ids, width):
    n, total = values.shape
    cols = width // HI
    rows = n * cols

    def kernel(val_ref, ids_ref, out_ref):
        out_ref[...] = jnp.zeros(out_ref.shape, jnp.float32)

        def body(off):
            idc = ids_ref[:, pl.ds(off, CHUNK)]
            v = val_ref[:, pl.ds(off, CHUNK)]
            sel = group_mask(idc, cols, CHUNK, cols)
            parts = []
            for piece in pieces(v):
                for p in range(n):
                    parts.append(jnp.where(sel, piece[p:p + 1, :], jnp.zeros((), jnp.bfloat16)))
            spread = jnp.concatenate(parts, axis=0)
            res = lax.dot_general(
                spread, hot_rows(idc, CHUNK), (((1,), (1,)), ((), ())),
                preferred_element_type=jnp.float32,
            )
            out_ref[...] += res[:rows] + res[rows:]

        chunks(total, body)

    return pl.pallas_call(
        kernel, out_shape=jax.ShapeDtypeStruct((rows, HI), jnp.float32)
    )(values, ids)


def knot_gather(extended, first_ids, basis, zsrc, weight, knots):
    total = first_ids.shape[1]
    cols = knots // HI
    shifted = jnp.stack([extended[q:q + knots] for q in range(4)], axis=0)
    rows = 4 * cols

    def kernel(tab_ref, ids_ref, basis_ref, zsrc_ref, weight_ref, out_ref, norm_ref, big_ref):
        split_into(tab_ref, big_ref)
        norm_ref[...] = jnp.zeros(norm_ref.shape, jnp.float32)

        def body(off):
            idc = ids_ref[:, pl.ds(off, CHUNK)]
            picked = jnp.dot(big_ref[...], hot_rows(idc, CHUNK), preferred_element_type=jnp.float32)
            acc = picked[:rows] + picked[rows:]
            sel = group_mask(idc, cols, CHUNK, cols)
            b = basis_ref[:, pl.ds(off, CHUNK)]
            z = jnp.zeros((1, CHUNK), jnp.float32)
            for q in range(4):
                value = jnp.sum(jnp.where(sel, acc[q * cols:(q + 1) * cols], 0.0), axis=0, keepdims=True)
                z = z + b[q:q + 1] * value
            shift = zsrc_ref[:, pl.ds(off, CHUNK)] + z
            out_ref[:, pl.ds(off, CHUNK)] = shift
            norm_ref[...] += jnp.sum(weight_ref[:, pl.ds(off, CHUNK)] * shift * shift, axis=1, keepdims=True)

        chunks(total, body)

    return pl.pallas_call(
        kernel,
        out_shape=(
            jax.ShapeDtypeStruct((1, total), jnp.float32),
            jax.ShapeDtypeStruct((1, 1), jnp.float32),
        ),
        scratch_shapes=[pltpu.VMEM((2 * rows, HI), jnp.bfloat16)],
    )(shifted.reshape(rows, HI), first_ids, basis, zsrc, weight)


def knot_scatter(values, first_ids, basis16, knots):
    total = first_ids.shape[1]
    cols = knots // HI
    rows = 4 * cols

    def kernel(val_ref, ids_ref, basis_ref, out_ref):
        out_ref[...] = jnp.zeros(out_ref.shape, jnp.float32)

        def body(off):
            idc = ids_ref[:, pl.ds(off, CHUNK)]
            sel = group_mask(idc, rows, CHUNK, cols)
            v = jnp.where(sel, basis_ref[:, pl.ds(off, CHUNK)] * val_ref[:, pl.ds(off, CHUNK)], 0.0)
            spread = jnp.concatenate(pieces(v), axis=0)
            res = lax.dot_general(
                spread, hot_rows(idc, CHUNK), (((1,), (1,)), ((), ())),
                preferred_element_type=jnp.float32,
            )
            out_ref[...] += res[:rows] + res[rows:]

        chunks(total, body)

    out = pl.pallas_call(
        kernel, out_shape=jax.ShapeDtypeStruct((rows, HI), jnp.float32)
    )(values, first_ids, basis16)
    per_shift = out.reshape(4, knots)
    grad = jnp.zeros((knots + 3,), jnp.float32)
    for q in range(4):
        grad = grad.at[q:q + knots].add(per_shift[q])
    return grad


def per_device(
    observed_residual,
    source_partials,
    spread_derivative_table,
    detector_index,
    first_knot_interval,
    interval_fraction,
    live_slot_count,
    slot_owned_source,
):
    rows = observed_residual.shape[1]
    n_time = lax.axis_size("tm")
    n_share = lax.axis_size("src")
    n_ranks = n_time * n_share
    capacity = rows // n_ranks
    n_params = source_partials.shape[0]
    detector_count = spread_derivative_table.shape[1]
    knots = KN
    n_knots = n_time * knots
    owned = SRC_DEV
    everyone = ("tm", "src")
    place = jnp.arange(capacity, dtype=jnp.int32)[None, :]
    live = (place < live_slot_count[0][:, None]).astype(jnp.float32).reshape(rows)
    indicator = (
        detector_index[None, :] == jnp.arange(detector_count, dtype=jnp.int32)[:, None]
    ).astype(jnp.float32)
    weight_factor = jnp.dot(
        spread_derivative_table,
        indicator,
        precision=lax.Precision.HIGHEST,
        preferred_element_type=jnp.float32,
    )
    weight_sq = live * jnp.sum(weight_factor * weight_factor, axis=0)
    basis16 = jnp.repeat(jnp.stack(spline_basis(interval_fraction), axis=0), knots // HI, axis=0)
    first_ids = first_knot_interval.reshape(1, rows)
    ids = slot_owned_source[0].reshape(1, rows)
    zbar0 = live * jnp.sum(weight_factor * observed_residual, axis=0)

    packed = jnp.concatenate(
        [
            source_partials,
            zbar0[None],
            weight_sq[None],
            interval_fraction[None],
            first_knot_interval.astype(jnp.float32)[None],
        ],
        axis=0,
    )
    got = lax.all_to_all(packed, everyone, split_axis=1, concat_axis=1, tiled=True)
    held = got[:n_params]
    zbar0_own = got[n_params]
    weight_sq_own = got[n_params + 1]
    basis_own = jnp.stack(spline_basis(got[n_params + 2]), axis=0)
    slot_device = jnp.arange(rows, dtype=jnp.int32) // capacity
    base_own = ((slot_device // n_share) * knots + got[n_params + 3].astype(jnp.int32)).reshape(1, rows)
    table_rows = n_params * (owned // HI)

    def combine(part_a, s_norm):
        mine = jnp.concatenate([part_a, s_norm[None]])
        every = lax.all_to_all(
            jnp.broadcast_to(mine[None, :], (n_ranks, knots + 4)), everyone, 0, 0, tiled=True
        )
        block = jnp.sum(every[:, :knots + 3].reshape(n_time, n_share, knots + 3), axis=1)
        main = block[:, :knots].at[1:, :3].add(block[:-1, knots:])
        grad_a = main.reshape(n_knots)
        norm = jnp.sum(every[:, knots + 3]) + jnp.sum(grad_a * grad_a)
        return grad_a, norm

    def forward(zsrc, dir_a, extra):
        extended = jnp.concatenate([dir_a, jnp.zeros((3,), jnp.float32)])
        shift_own, partial = knot_gather(
            extended, base_own, basis_own, zsrc, weight_sq_own.reshape(1, rows), n_knots
        )
        shift_own = shift_own.reshape(rows)
        sums = jnp.concatenate([partial.reshape(1), extra.reshape(1)])
        payload = jnp.concatenate(
            [shift_own.reshape(n_ranks, capacity), jnp.broadcast_to(sums[None, :], (n_ranks, 2))], axis=1
        )
        back = lax.all_to_all(payload, everyone, 0, 0, tiled=True)
        totals = jnp.sum(back[:, capacity:], axis=0)
        return shift_own, back[:, :capacity].reshape(rows) * live, totals[0], totals[1]

    sol_s = jnp.zeros((table_rows, HI), jnp.float32)
    sol_a = jnp.zeros((n_knots,), jnp.float32)
    resid = observed_residual
    zbar_slot = zbar0
    part_a = knot_scatter(zbar_slot.reshape(1, rows), first_ids, basis16, knots)
    part_a, held, zbar0_own = lax.optimization_barrier((part_a, held, zbar0_own))
    grad_a, gamma_a = combine(part_a, jnp.zeros((), jnp.float32))
    grad_s = source_scatter(held * zbar0_own[None, :], ids, owned)
    extra = jnp.sum(grad_s * grad_s)
    dir_s, dir_a = (grad_s, grad_a)
    pulled = source_gather(dir_s, ids, held)
    for step in range(ITERS):
        shift_own, shift_slot, image_sq, extra_sum = forward(pulled, dir_a, extra)
        if step == 0:
            gamma = extra_sum + gamma_a
        alpha = gamma / image_sq
        sol_s = sol_s + alpha * dir_s
        sol_a = sol_a + alpha * dir_a
        resid = resid - alpha * (weight_factor * shift_slot[None, :])
        if step + 1 < ITERS:
            pushed = source_scatter(held * (weight_sq_own * shift_own)[None, :], ids, owned)
            zbar_slot = zbar_slot - alpha * (weight_sq * shift_slot)
            grad_s = grad_s - alpha * pushed
            grad_a, fresh = combine(
                knot_scatter(zbar_slot.reshape(1, rows), first_ids, basis16, knots),
                jnp.sum(grad_s * grad_s),
            )
            raw = source_gather(grad_s, ids, held)
            beta = fresh / gamma
            dir_s = grad_s + beta * dir_s
            dir_a = grad_a + beta * dir_a
            pulled = raw + beta * pulled
            gamma = fresh
            extra = jnp.zeros((), jnp.float32)
    mine_a = lax.dynamic_slice(sol_a, (lax.axis_index("tm") * knots,), (knots,))
    return (sol_s.reshape(n_params, owned), mine_a, resid)


def solution(mesh):
    placed = (
        P(None, ("tm", "src")),
        P(None, ("tm", "src")),
        P(),
        P(("tm", "src")),
        P(("tm", "src")),
        P(("tm", "src")),
        P(("tm", "src"), None),
        P(("tm", "src"), None),
    )
    return jax.shard_map(
        per_device,
        mesh=mesh,
        in_specs=placed,
        out_specs=(P(None, ("tm", "src")), P("tm"), P(None, ("tm", "src"))),
        check_vma=False,
    )
```

```python
import jax
import jax.numpy as jnp
from jax import lax
from jax.experimental import pallas as pl
from jax.experimental.pallas import tpu as pltpu
from jax.sharding import PartitionSpec as P

SRC_DEV = 32768
KN = 1024
ITERS = 2
HI = 256
CHUNK = 4096


def passed_along(block, axis, distance):
    devices = range(lax.axis_size(axis))
    route = [(i - distance, i) for i in devices if i - distance in devices]
    return lax.ppermute(block, axis, route)


def spline_basis(frac):
    u2 = frac * frac
    u3 = u2 * frac
    one = 1.0 - frac
    return [
        one * one * one / 6.0,
        (3.0 * u3 - 6.0 * u2 + 4.0) / 6.0,
        (-3.0 * u3 + 3.0 * u2 + 3.0 * frac + 1.0) / 6.0,
        u3 / 6.0,
    ]


def pieces(x):
    h = x.astype(jnp.bfloat16)
    m = (x - h.astype(jnp.float32)).astype(jnp.bfloat16)
    return h, m


def hot_rows(ids, width):
    low = jnp.bitwise_and(ids, HI - 1)
    return (lax.broadcasted_iota(jnp.int32, (HI, width), 0) == low).astype(jnp.bfloat16)


def group_mask(ids, rows, width, groups):
    high = lax.shift_right_logical(ids, 8)
    iota = lax.broadcasted_iota(jnp.int32, (rows, width), 0)
    return (iota % groups) == high


def chunks(total, body):
    def step(i, carry):
        body(pl.multiple_of(i * CHUNK, CHUNK))
        return carry

    lax.fori_loop(0, total // CHUNK, step, 0)


def split_into(src_ref, big_ref):
    rows = src_ref.shape[0]
    for k, part in enumerate(pieces(src_ref[...])):
        big_ref[k * rows:(k + 1) * rows, :] = part


def source_gather(table, ids, held):
    n, total = held.shape
    rows = table.shape[0]
    cols = rows // n

    def kernel(tab_ref, ids_ref, held_ref, out_ref, big_ref):
        split_into(tab_ref, big_ref)

        def body(off):
            idc = ids_ref[:, pl.ds(off, CHUNK)]
            picked = jnp.dot(big_ref[...], hot_rows(idc, CHUNK), preferred_element_type=jnp.float32)
            sel = group_mask(idc, cols, CHUNK, cols)
            weights = held_ref[:, pl.ds(off, CHUNK)]
            column = jnp.zeros((1, CHUNK), jnp.float32)
            for p in range(n):
                acc = (
                    picked[p * cols:(p + 1) * cols]
                    + picked[rows + p * cols:rows + (p + 1) * cols]
                )
                value = jnp.sum(jnp.where(sel, acc, 0.0), axis=0, keepdims=True)
                column = column + weights[p:p + 1] * value
            out_ref[:, pl.ds(off, CHUNK)] = column

        chunks(total, body)

    return pl.pallas_call(
        kernel,
        out_shape=jax.ShapeDtypeStruct((1, total), jnp.float32),
        scratch_shapes=[pltpu.VMEM((2 * rows, HI), jnp.bfloat16)],
    )(table, ids, held)


def source_scatter(values, ids, width):
    n, total = values.shape
    cols = width // HI
    rows = n * cols

    def kernel(val_ref, ids_ref, out_ref):
        out_ref[...] = jnp.zeros(out_ref.shape, jnp.float32)

        def body(off):
            idc = ids_ref[:, pl.ds(off, CHUNK)]
            v = val_ref[:, pl.ds(off, CHUNK)]
            sel = group_mask(idc, cols, CHUNK, cols)
            parts = []
            for piece in pieces(v):
                for p in range(n):
                    parts.append(jnp.where(sel, piece[p:p + 1, :], jnp.zeros((), jnp.bfloat16)))
            spread = jnp.concatenate(parts, axis=0)
            res = lax.dot_general(
                spread, hot_rows(idc, CHUNK), (((1,), (1,)), ((), ())),
                preferred_element_type=jnp.float32,
            )
            out_ref[...] += res[:rows] + res[rows:]

        chunks(total, body)

    return pl.pallas_call(
        kernel, out_shape=jax.ShapeDtypeStruct((rows, HI), jnp.float32)
    )(values, ids)


def knot_gather(extended, first_ids, basis, zsrc, weight, knots):
    total = first_ids.shape[1]
    cols = knots // HI
    shifted = jnp.stack([extended[q:q + knots] for q in range(4)], axis=0)
    rows = 4 * cols

    def kernel(tab_ref, ids_ref, basis_ref, zsrc_ref, weight_ref, out_ref, norm_ref, big_ref):
        split_into(tab_ref, big_ref)
        norm_ref[...] = jnp.zeros(norm_ref.shape, jnp.float32)

        def body(off):
            idc = ids_ref[:, pl.ds(off, CHUNK)]
            picked = jnp.dot(big_ref[...], hot_rows(idc, CHUNK), preferred_element_type=jnp.float32)
            acc = picked[:rows] + picked[rows:]
            sel = group_mask(idc, cols, CHUNK, cols)
            b = basis_ref[:, pl.ds(off, CHUNK)]
            z = jnp.zeros((1, CHUNK), jnp.float32)
            for q in range(4):
                value = jnp.sum(jnp.where(sel, acc[q * cols:(q + 1) * cols], 0.0), axis=0, keepdims=True)
                z = z + b[q:q + 1] * value
            shift = zsrc_ref[:, pl.ds(off, CHUNK)] + z
            out_ref[:, pl.ds(off, CHUNK)] = shift
            norm_ref[...] += jnp.sum(weight_ref[:, pl.ds(off, CHUNK)] * shift * shift, axis=1, keepdims=True)

        chunks(total, body)

    return pl.pallas_call(
        kernel,
        out_shape=(
            jax.ShapeDtypeStruct((1, total), jnp.float32),
            jax.ShapeDtypeStruct((1, 1), jnp.float32),
        ),
        scratch_shapes=[pltpu.VMEM((2 * rows, HI), jnp.bfloat16)],
    )(shifted.reshape(rows, HI), first_ids, basis, zsrc, weight)


def knot_scatter(values, first_ids, basis16, knots):
    total = first_ids.shape[1]
    cols = knots // HI
    rows = 4 * cols

    def kernel(val_ref, ids_ref, basis_ref, out_ref):
        out_ref[...] = jnp.zeros(out_ref.shape, jnp.float32)

        def body(off):
            idc = ids_ref[:, pl.ds(off, CHUNK)]
            sel = group_mask(idc, rows, CHUNK, cols)
            v = jnp.where(sel, basis_ref[:, pl.ds(off, CHUNK)] * val_ref[:, pl.ds(off, CHUNK)], 0.0)
            spread = jnp.concatenate(pieces(v), axis=0)
            res = lax.dot_general(
                spread, hot_rows(idc, CHUNK), (((1,), (1,)), ((), ())),
                preferred_element_type=jnp.float32,
            )
            out_ref[...] += res[:rows] + res[rows:]

        chunks(total, body)

    out = pl.pallas_call(
        kernel, out_shape=jax.ShapeDtypeStruct((rows, HI), jnp.float32)
    )(values, first_ids, basis16)
    per_shift = out.reshape(4, knots)
    grad = jnp.zeros((knots + 3,), jnp.float32)
    for q in range(4):
        grad = grad.at[q:q + knots].add(per_shift[q])
    return grad


def per_device(
    observed_residual,
    source_partials,
    spread_derivative_table,
    detector_index,
    first_knot_interval,
    interval_fraction,
    live_slot_count,
    slot_owned_source,
):
    rows = observed_residual.shape[1]
    n_time = lax.axis_size("tm")
    n_share = lax.axis_size("src")
    n_ranks = n_time * n_share
    capacity = rows // n_ranks
    n_params = source_partials.shape[0]
    detector_count = spread_derivative_table.shape[1]
    knots = KN
    n_knots = n_time * knots
    owned = SRC_DEV
    everyone = ("tm", "src")
    place = jnp.arange(capacity, dtype=jnp.int32)[None, :]
    live = (place < live_slot_count[0][:, None]).astype(jnp.float32).reshape(rows)
    indicator = (
        detector_index[None, :] == jnp.arange(detector_count, dtype=jnp.int32)[:, None]
    ).astype(jnp.float32)
    weight_factor = jnp.dot(
        spread_derivative_table,
        indicator,
        precision=lax.Precision.HIGHEST,
        preferred_element_type=jnp.float32,
    )
    weight_sq = live * jnp.sum(weight_factor * weight_factor, axis=0)
    basis16 = jnp.repeat(jnp.stack(spline_basis(interval_fraction), axis=0), knots // HI, axis=0)
    first_ids = first_knot_interval.reshape(1, rows)
    ids = slot_owned_source[0].reshape(1, rows)
    zbar0 = live * jnp.sum(weight_factor * observed_residual, axis=0)

    packed = jnp.concatenate(
        [
            source_partials,
            zbar0[None],
            weight_sq[None],
            interval_fraction[None],
            first_knot_interval.astype(jnp.float32)[None],
        ],
        axis=0,
    )
    n_rows = packed.shape[0]
    blocks = packed.reshape(n_rows, n_ranks, capacity).transpose(1, 0, 2).reshape(n_ranks, n_rows * capacity)
    got = lax.all_to_all(blocks, everyone, 0, 0, tiled=True)
    got = got.reshape(n_ranks, n_rows, capacity).transpose(1, 0, 2).reshape(n_rows, rows)
    held = got[:n_params]
    zbar0_own = got[n_params]
    weight_sq_own = got[n_params + 1]
    basis_own = jnp.stack(spline_basis(got[n_params + 2]), axis=0)
    slot_device = jnp.arange(rows, dtype=jnp.int32) // capacity
    base_own = ((slot_device // n_share) * knots + got[n_params + 3].astype(jnp.int32)).reshape(1, rows)
    table_rows = n_params * (owned // HI)

    def combine(part_a, s_norm):
        mine = jnp.concatenate([part_a, s_norm[None]])
        every = lax.all_to_all(
            jnp.broadcast_to(mine[None, :], (n_ranks, knots + 4)), everyone, 0, 0, tiled=True
        )
        block = jnp.sum(every[:, :knots + 3].reshape(n_time, n_share, knots + 3), axis=1)
        main = block[:, :knots].at[1:, :3].add(block[:-1, knots:])
        grad_a = main.reshape(n_knots)
        norm = jnp.sum(every[:, knots + 3]) + jnp.sum(grad_a * grad_a)
        return grad_a, norm

    def forward(zsrc, dir_a, extra):
        extended = jnp.concatenate([dir_a, jnp.zeros((3,), jnp.float32)])
        shift_own, partial = knot_gather(
            extended, base_own, basis_own, zsrc, weight_sq_own.reshape(1, rows), n_knots
        )
        shift_own = shift_own.reshape(rows)
        sums = jnp.concatenate([partial.reshape(1), extra.reshape(1)])
        payload = jnp.concatenate(
            [shift_own.reshape(n_ranks, capacity), jnp.broadcast_to(sums[None, :], (n_ranks, 2))], axis=1
        )
        back = lax.all_to_all(payload, everyone, 0, 0, tiled=True)
        totals = jnp.sum(back[:, capacity:], axis=0)
        return shift_own, back[:, :capacity].reshape(rows) * live, totals[0], totals[1]

    sol_s = jnp.zeros((table_rows, HI), jnp.float32)
    sol_a = jnp.zeros((n_knots,), jnp.float32)
    resid = observed_residual
    zbar_slot = zbar0
    part_a = knot_scatter(zbar_slot.reshape(1, rows), first_ids, basis16, knots)
    part_a, held, zbar0_own = lax.optimization_barrier((part_a, held, zbar0_own))
    grad_a, gamma_a = combine(part_a, jnp.zeros((), jnp.float32))
    grad_s = source_scatter(held * zbar0_own[None, :], ids, owned)
    extra = jnp.sum(grad_s * grad_s)
    dir_s, dir_a = (grad_s, grad_a)
    pulled = source_gather(dir_s, ids, held)
    for step in range(ITERS):
        shift_own, shift_slot, image_sq, extra_sum = forward(pulled, dir_a, extra)
        if step == 0:
            gamma = extra_sum + gamma_a
        alpha = gamma / image_sq
        sol_s = sol_s + alpha * dir_s
        sol_a = sol_a + alpha * dir_a
        resid = resid - alpha * (weight_factor * shift_slot[None, :])
        if step + 1 < ITERS:
            pushed = source_scatter(held * (weight_sq_own * shift_own)[None, :], ids, owned)
            zbar_slot = zbar_slot - alpha * (weight_sq * shift_slot)
            grad_s = grad_s - alpha * pushed
            grad_a, fresh = combine(
                knot_scatter(zbar_slot.reshape(1, rows), first_ids, basis16, knots),
                jnp.sum(grad_s * grad_s),
            )
            raw = source_gather(grad_s, ids, held)
            beta = fresh / gamma
            dir_s = grad_s + beta * dir_s
            dir_a = grad_a + beta * dir_a
            pulled = raw + beta * pulled
            gamma = fresh
            extra = jnp.zeros((), jnp.float32)
    mine_a = lax.dynamic_slice(sol_a, (lax.axis_index("tm") * knots,), (knots,))
    return (sol_s.reshape(n_params, owned), mine_a, resid)


def solution(mesh):
    placed = (
        P(None, ("tm", "src")),
        P(None, ("tm", "src")),
        P(),
        P(("tm", "src")),
        P(("tm", "src")),
        P(("tm", "src")),
        P(("tm", "src"), None),
        P(("tm", "src"), None),
    )
    return jax.shard_map(
        per_device,
        mesh=mesh,
        in_specs=placed,
        out_specs=(P(None, ("tm", "src")), P("tm"), P(None, ("tm", "src"))),
        check_vma=False,
    )
```

```python
import jax
import jax.numpy as jnp
from jax import lax
from jax.experimental import pallas as pl
from jax.experimental.pallas import tpu as pltpu
from jax.sharding import PartitionSpec as P

SRC_DEV = 32768
KN = 1024
ITERS = 2
HI = 256
CHUNK = 4096


def passed_along(block, axis, distance):
    devices = range(lax.axis_size(axis))
    route = [(i - distance, i) for i in devices if i - distance in devices]
    return lax.ppermute(block, axis, route)


def spline_basis(frac):
    u2 = frac * frac
    u3 = u2 * frac
    one = 1.0 - frac
    return [
        one * one * one / 6.0,
        (3.0 * u3 - 6.0 * u2 + 4.0) / 6.0,
        (-3.0 * u3 + 3.0 * u2 + 3.0 * frac + 1.0) / 6.0,
        u3 / 6.0,
    ]


def pieces(x):
    h = x.astype(jnp.bfloat16)
    m = (x - h.astype(jnp.float32)).astype(jnp.bfloat16)
    return h, m


def hot_rows(ids, width):
    low = jnp.bitwise_and(ids, HI - 1)
    return (lax.broadcasted_iota(jnp.int32, (HI, width), 0) == low).astype(jnp.bfloat16)


def group_mask(ids, rows, width, groups):
    high = lax.shift_right_logical(ids, 8)
    iota = lax.broadcasted_iota(jnp.int32, (rows, width), 0)
    return (iota % groups) == high


def chunks(total, body):
    def step(i, carry):
        body(pl.multiple_of(i * CHUNK, CHUNK))
        return carry

    lax.fori_loop(0, total // CHUNK, step, 0)


def split_into(src_ref, big_ref):
    rows = src_ref.shape[0]
    for k, part in enumerate(pieces(src_ref[...])):
        big_ref[k * rows:(k + 1) * rows, :] = part


def source_gather(table, ids, held):
    n, total = held.shape
    rows = table.shape[0]
    cols = rows // n

    def kernel(tab_ref, ids_ref, held_ref, out_ref, big_ref):
        split_into(tab_ref, big_ref)

        def body(off):
            idc = ids_ref[:, pl.ds(off, CHUNK)]
            picked = jnp.dot(big_ref[...], hot_rows(idc, CHUNK), preferred_element_type=jnp.float32)
            sel = group_mask(idc, cols, CHUNK, cols)
            weights = held_ref[:, pl.ds(off, CHUNK)]
            column = jnp.zeros((1, CHUNK), jnp.float32)
            for p in range(n):
                acc = (
                    picked[p * cols:(p + 1) * cols]
                    + picked[rows + p * cols:rows + (p + 1) * cols]
                )
                value = jnp.sum(jnp.where(sel, acc, 0.0), axis=0, keepdims=True)
                column = column + weights[p:p + 1] * value
            out_ref[:, pl.ds(off, CHUNK)] = column

        chunks(total, body)

    return pl.pallas_call(
        kernel,
        out_shape=jax.ShapeDtypeStruct((1, total), jnp.float32),
        scratch_shapes=[pltpu.VMEM((2 * rows, HI), jnp.bfloat16)],
    )(table, ids, held)


def source_scatter(values, ids, width):
    n, total = values.shape
    cols = width // HI
    rows = n * cols

    def kernel(val_ref, ids_ref, out_ref):
        out_ref[...] = jnp.zeros(out_ref.shape, jnp.float32)

        def body(off):
            idc = ids_ref[:, pl.ds(off, CHUNK)]
            v = val_ref[:, pl.ds(off, CHUNK)]
            sel = group_mask(idc, cols, CHUNK, cols)
            parts = []
            for piece in pieces(v):
                for p in range(n):
                    parts.append(jnp.where(sel, piece[p:p + 1, :], jnp.zeros((), jnp.bfloat16)))
            spread = jnp.concatenate(parts, axis=0)
            res = lax.dot_general(
                spread, hot_rows(idc, CHUNK), (((1,), (1,)), ((), ())),
                preferred_element_type=jnp.float32,
            )
            out_ref[...] += res[:rows] + res[rows:]

        chunks(total, body)

    return pl.pallas_call(
        kernel, out_shape=jax.ShapeDtypeStruct((rows, HI), jnp.float32)
    )(values, ids)


def knot_gather(extended, first_ids, basis, zsrc, weight, knots):
    total = first_ids.shape[1]
    cols = knots // HI
    shifted = jnp.stack([extended[q:q + knots] for q in range(4)], axis=0)
    rows = 4 * cols

    def kernel(tab_ref, ids_ref, basis_ref, zsrc_ref, weight_ref, out_ref, norm_ref, big_ref):
        split_into(tab_ref, big_ref)
        norm_ref[...] = jnp.zeros(norm_ref.shape, jnp.float32)

        def body(off):
            idc = ids_ref[:, pl.ds(off, CHUNK)]
            picked = jnp.dot(big_ref[...], hot_rows(idc, CHUNK), preferred_element_type=jnp.float32)
            acc = picked[:rows] + picked[rows:]
            sel = group_mask(idc, cols, CHUNK, cols)
            b = basis_ref[:, pl.ds(off, CHUNK)]
            z = jnp.zeros((1, CHUNK), jnp.float32)
            for q in range(4):
                value = jnp.sum(jnp.where(sel, acc[q * cols:(q + 1) * cols], 0.0), axis=0, keepdims=True)
                z = z + b[q:q + 1] * value
            shift = zsrc_ref[:, pl.ds(off, CHUNK)] + z
            out_ref[:, pl.ds(off, CHUNK)] = shift
            norm_ref[...] += jnp.sum(weight_ref[:, pl.ds(off, CHUNK)] * shift * shift, axis=1, keepdims=True)

        chunks(total, body)

    return pl.pallas_call(
        kernel,
        out_shape=(
            jax.ShapeDtypeStruct((1, total), jnp.float32),
            jax.ShapeDtypeStruct((1, 1), jnp.float32),
        ),
        scratch_shapes=[pltpu.VMEM((2 * rows, HI), jnp.bfloat16)],
    )(shifted.reshape(rows, HI), first_ids, basis, zsrc, weight)


def knot_scatter(values, first_ids, basis16, knots):
    total = first_ids.shape[1]
    cols = knots // HI
    rows = 4 * cols

    def kernel(val_ref, ids_ref, basis_ref, out_ref):
        out_ref[...] = jnp.zeros(out_ref.shape, jnp.float32)

        def body(off):
            idc = ids_ref[:, pl.ds(off, CHUNK)]
            sel = group_mask(idc, rows, CHUNK, cols)
            v = jnp.where(sel, basis_ref[:, pl.ds(off, CHUNK)] * val_ref[:, pl.ds(off, CHUNK)], 0.0)
            spread = jnp.concatenate(pieces(v), axis=0)
            res = lax.dot_general(
                spread, hot_rows(idc, CHUNK), (((1,), (1,)), ((), ())),
                preferred_element_type=jnp.float32,
            )
            out_ref[...] += res[:rows] + res[rows:]

        chunks(total, body)

    out = pl.pallas_call(
        kernel, out_shape=jax.ShapeDtypeStruct((rows, HI), jnp.float32)
    )(values, first_ids, basis16)
    per_shift = out.reshape(4, knots)
    grad = jnp.zeros((knots + 3,), jnp.float32)
    for q in range(4):
        grad = grad.at[q:q + knots].add(per_shift[q])
    return grad


def per_device(
    observed_residual,
    source_partials,
    spread_derivative_table,
    detector_index,
    first_knot_interval,
    interval_fraction,
    live_slot_count,
    slot_owned_source,
):
    rows = observed_residual.shape[1]
    n_time = lax.axis_size("tm")
    n_share = lax.axis_size("src")
    n_ranks = n_time * n_share
    capacity = rows // n_ranks
    n_params = source_partials.shape[0]
    detector_count = spread_derivative_table.shape[1]
    knots = KN
    n_knots = n_time * knots
    owned = SRC_DEV
    everyone = ("tm", "src")
    place = jnp.arange(capacity, dtype=jnp.int32)[None, :]
    live = (place < live_slot_count[0][:, None]).astype(jnp.float32).reshape(1, rows)
    indicator = (
        detector_index[None, :] == jnp.arange(detector_count, dtype=jnp.int32)[:, None]
    ).astype(jnp.float32)
    weight_factor = jnp.dot(
        spread_derivative_table,
        indicator,
        precision=lax.Precision.HIGHEST,
        preferred_element_type=jnp.float32,
    )
    weight_sq = live * jnp.sum(weight_factor * weight_factor, axis=0, keepdims=True)
    basis16 = jnp.repeat(jnp.stack(spline_basis(interval_fraction), axis=0), knots // HI, axis=0)
    first_ids = first_knot_interval.reshape(1, rows)
    ids = slot_owned_source[0].reshape(1, rows)
    zbar0 = live * jnp.sum(weight_factor * observed_residual, axis=0, keepdims=True)

    packed = jnp.concatenate(
        [
            source_partials,
            zbar0,
            weight_sq,
            interval_fraction[None],
            first_knot_interval.astype(jnp.float32)[None],
        ],
        axis=0,
    )
    n_rows = packed.shape[0]
    blocks = packed.reshape(n_rows, n_ranks, capacity).transpose(1, 0, 2).reshape(n_ranks, n_rows * capacity)
    got = lax.all_to_all(blocks, everyone, 0, 0, tiled=True)
    got = got.reshape(n_ranks, n_rows, capacity).transpose(1, 0, 2).reshape(n_rows, rows)
    held = got[:n_params]
    zbar0_own = got[n_params:n_params + 1]
    weight_sq_own = got[n_params + 1:n_params + 2]
    basis_own = jnp.concatenate(spline_basis(got[n_params + 2:n_params + 3]), axis=0)
    slot_device = jnp.arange(rows, dtype=jnp.int32)[None, :] // capacity
    base_own = (slot_device // n_share) * knots + got[n_params + 3:n_params + 4].astype(jnp.int32)
    table_rows = n_params * (owned // HI)

    def combine(part_a, s_norm):
        mine = jnp.concatenate([part_a, s_norm[None]])
        every = lax.all_to_all(
            jnp.broadcast_to(mine[None, :], (n_ranks, knots + 4)), everyone, 0, 0, tiled=True
        )
        block = jnp.sum(every[:, :knots + 3].reshape(n_time, n_share, knots + 3), axis=1)
        main = block[:, :knots].at[1:, :3].add(block[:-1, knots:])
        grad_a = main.reshape(n_knots)
        norm = jnp.sum(every[:, knots + 3]) + jnp.sum(grad_a * grad_a)
        return grad_a, norm

    def forward(zsrc, dir_a, extra):
        extended = jnp.concatenate([dir_a, jnp.zeros((3,), jnp.float32)])
        shift_own, partial = knot_gather(extended, base_own, basis_own, zsrc, weight_sq_own, n_knots)
        sums = jnp.concatenate([partial.reshape(1), extra.reshape(1)])
        payload = jnp.concatenate(
            [shift_own.reshape(n_ranks, capacity), jnp.broadcast_to(sums[None, :], (n_ranks, 2))], axis=1
        )
        back = lax.all_to_all(payload, everyone, 0, 0, tiled=True)
        totals = jnp.sum(back[:, capacity:], axis=0)
        return shift_own, back[:, :capacity].reshape(1, rows) * live, totals[0], totals[1]

    sol_s = jnp.zeros((table_rows, HI), jnp.float32)
    sol_a = jnp.zeros((n_knots,), jnp.float32)
    resid = observed_residual
    zbar_slot = zbar0
    part_a = knot_scatter(zbar_slot, first_ids, basis16, knots)
    part_a, held, zbar0_own = lax.optimization_barrier((part_a, held, zbar0_own))
    grad_a, gamma_a = combine(part_a, jnp.zeros((), jnp.float32))
    grad_s = source_scatter(held * zbar0_own, ids, owned)
    extra = jnp.sum(grad_s * grad_s)
    dir_s, dir_a = (grad_s, grad_a)
    pulled = source_gather(dir_s, ids, held)
    for step in range(ITERS):
        shift_own, shift_slot, image_sq, extra_sum = forward(pulled, dir_a, extra)
        if step == 0:
            gamma = extra_sum + gamma_a
        alpha = gamma / image_sq
        sol_s = sol_s + alpha * dir_s
        sol_a = sol_a + alpha * dir_a
        resid = resid - alpha * (weight_factor * shift_slot)
        if step + 1 < ITERS:
            pushed = source_scatter(held * (weight_sq_own * shift_own), ids, owned)
            zbar_slot = zbar_slot - alpha * (weight_sq * shift_slot)
            grad_s = grad_s - alpha * pushed
            grad_a, fresh = combine(
                knot_scatter(zbar_slot, first_ids, basis16, knots),
                jnp.sum(grad_s * grad_s),
            )
            raw = source_gather(grad_s, ids, held)
            beta = fresh / gamma
            dir_s = grad_s + beta * dir_s
            dir_a = grad_a + beta * dir_a
            pulled = raw + beta * pulled
            gamma = fresh
            extra = jnp.zeros((), jnp.float32)
    mine_a = lax.dynamic_slice(sol_a, (lax.axis_index("tm") * knots,), (knots,))
    return (sol_s.reshape(n_params, owned), mine_a, resid)


def solution(mesh):
    placed = (
        P(None, ("tm", "src")),
        P(None, ("tm", "src")),
        P(),
        P(("tm", "src")),
        P(("tm", "src")),
        P(("tm", "src")),
        P(("tm", "src"), None),
        P(("tm", "src"), None),
    )
    return jax.shard_map(
        per_device,
        mesh=mesh,
        in_specs=placed,
        out_specs=(P(None, ("tm", "src")), P("tm"), P(None, ("tm", "src"))),
        check_vma=False,
    )
```

```python
import jax
import jax.numpy as jnp
from jax import lax
from jax.experimental import pallas as pl
from jax.experimental.pallas import tpu as pltpu
from jax.sharding import PartitionSpec as P

SRC_DEV = 32768
KN = 1024
ITERS = 2
HI = 256
CHUNK = 4096


def passed_along(block, axis, distance):
    devices = range(lax.axis_size(axis))
    route = [(i - distance, i) for i in devices if i - distance in devices]
    return lax.ppermute(block, axis, route)


def spline_basis(frac):
    u2 = frac * frac
    u3 = u2 * frac
    one = 1.0 - frac
    return [
        one * one * one / 6.0,
        (3.0 * u3 - 6.0 * u2 + 4.0) / 6.0,
        (-3.0 * u3 + 3.0 * u2 + 3.0 * frac + 1.0) / 6.0,
        u3 / 6.0,
    ]


def pieces(x):
    h = x.astype(jnp.bfloat16)
    m = (x - h.astype(jnp.float32)).astype(jnp.bfloat16)
    return h, m


def hot_rows(ids, width):
    low = jnp.bitwise_and(ids, HI - 1)
    return (lax.broadcasted_iota(jnp.int32, (HI, width), 0) == low).astype(jnp.bfloat16)


def group_mask(ids, rows, width, groups):
    high = lax.shift_right_logical(ids, 8)
    iota = lax.broadcasted_iota(jnp.int32, (rows, width), 0)
    return (iota % groups) == high


def chunks(total, body):
    def step(i, carry):
        body(pl.multiple_of(i * CHUNK, CHUNK))
        return carry

    lax.fori_loop(0, total // CHUNK, step, 0)


def split_into(src_ref, big_ref):
    rows = src_ref.shape[0]
    for k, part in enumerate(pieces(src_ref[...])):
        big_ref[k * rows:(k + 1) * rows, :] = part


def source_gather(table, ids, held):
    n, total = held.shape
    rows = table.shape[0]
    cols = rows // n

    def kernel(tab_ref, ids_ref, held_ref, out_ref, big_ref):
        split_into(tab_ref, big_ref)

        def body(off):
            idc = ids_ref[:, pl.ds(off, CHUNK)]
            picked = jnp.dot(big_ref[...], hot_rows(idc, CHUNK), preferred_element_type=jnp.float32)
            sel = group_mask(idc, cols, CHUNK, cols)
            weights = held_ref[:, pl.ds(off, CHUNK)]
            column = jnp.zeros((1, CHUNK), jnp.float32)
            for p in range(n):
                acc = (
                    picked[p * cols:(p + 1) * cols]
                    + picked[rows + p * cols:rows + (p + 1) * cols]
                )
                value = jnp.sum(jnp.where(sel, acc, 0.0), axis=0, keepdims=True)
                column = column + weights[p:p + 1] * value
            out_ref[:, pl.ds(off, CHUNK)] = column

        chunks(total, body)

    return pl.pallas_call(
        kernel,
        out_shape=jax.ShapeDtypeStruct((1, total), jnp.float32),
        scratch_shapes=[pltpu.VMEM((2 * rows, HI), jnp.bfloat16)],
    )(table, ids, held)


def source_scatter(values, ids, width):
    n, total = values.shape
    cols = width // HI
    rows = n * cols

    def kernel(val_ref, ids_ref, out_ref):
        out_ref[...] = jnp.zeros(out_ref.shape, jnp.float32)

        def body(off):
            idc = ids_ref[:, pl.ds(off, CHUNK)]
            v = val_ref[:, pl.ds(off, CHUNK)]
            sel = group_mask(idc, cols, CHUNK, cols)
            parts = []
            for piece in pieces(v):
                for p in range(n):
                    parts.append(jnp.where(sel, piece[p:p + 1, :], jnp.zeros((), jnp.bfloat16)))
            spread = jnp.concatenate(parts, axis=0)
            res = lax.dot_general(
                spread, hot_rows(idc, CHUNK), (((1,), (1,)), ((), ())),
                preferred_element_type=jnp.float32,
            )
            out_ref[...] += res[:rows] + res[rows:]

        chunks(total, body)

    return pl.pallas_call(
        kernel, out_shape=jax.ShapeDtypeStruct((rows, HI), jnp.float32)
    )(values, ids)


def knot_gather(extended, first_ids, basis, zsrc, weight, extra, knots, parts, width):
    total = first_ids.shape[1]
    cols = knots // HI
    shifted = jnp.stack([extended[q:q + knots] for q in range(4)], axis=0)
    rows = 4 * cols
    per_chunk = CHUNK // width

    def kernel(tab_ref, ids_ref, basis_ref, zsrc_ref, weight_ref, extra_ref, out_ref, pay_ref, big_ref, norm_ref):
        split_into(tab_ref, big_ref)
        norm_ref[...] = jnp.zeros(norm_ref.shape, jnp.float32)

        for i in range(total // CHUNK):
            off = i * CHUNK
            idc = ids_ref[:, pl.ds(off, CHUNK)]
            picked = jnp.dot(big_ref[...], hot_rows(idc, CHUNK), preferred_element_type=jnp.float32)
            acc = picked[:rows] + picked[rows:]
            sel = group_mask(idc, cols, CHUNK, cols)
            b = basis_ref[:, pl.ds(off, CHUNK)]
            z = jnp.zeros((1, CHUNK), jnp.float32)
            for q in range(4):
                value = jnp.sum(jnp.where(sel, acc[q * cols:(q + 1) * cols], 0.0), axis=0, keepdims=True)
                z = z + b[q:q + 1] * value
            shift = zsrc_ref[:, pl.ds(off, CHUNK)] + z
            out_ref[:, pl.ds(off, CHUNK)] = shift
            for r in range(per_chunk):
                row = i * per_chunk + r
                pay_ref[row:row + 1, 128:128 + width] = shift[:, r * width:(r + 1) * width]
            norm_ref[...] += jnp.sum(weight_ref[:, pl.ds(off, CHUNK)] * shift * shift, axis=1, keepdims=True)

        lane = lax.broadcasted_iota(jnp.int32, (parts, 128), 1)
        pay_ref[:, 0:128] = jnp.where(
            lane == 0, norm_ref[...], jnp.where(lane == 1, extra_ref[...], 0.0)
        )

    return pl.pallas_call(
        kernel,
        out_shape=(
            jax.ShapeDtypeStruct((1, total), jnp.float32),
            jax.ShapeDtypeStruct((parts, 128 + width), jnp.float32),
        ),
        scratch_shapes=[pltpu.VMEM((2 * rows, HI), jnp.bfloat16), pltpu.VMEM((1, 1), jnp.float32)],
    )(shifted.reshape(rows, HI), first_ids, basis, zsrc, weight, extra.reshape(1, 1))


def knot_scatter(values, first_ids, basis16, knots):
    total = first_ids.shape[1]
    cols = knots // HI
    rows = 4 * cols

    def kernel(val_ref, ids_ref, basis_ref, out_ref):
        out_ref[...] = jnp.zeros(out_ref.shape, jnp.float32)

        def body(off):
            idc = ids_ref[:, pl.ds(off, CHUNK)]
            sel = group_mask(idc, rows, CHUNK, cols)
            v = jnp.where(sel, basis_ref[:, pl.ds(off, CHUNK)] * val_ref[:, pl.ds(off, CHUNK)], 0.0)
            spread = jnp.concatenate(pieces(v), axis=0)
            res = lax.dot_general(
                spread, hot_rows(idc, CHUNK), (((1,), (1,)), ((), ())),
                preferred_element_type=jnp.float32,
            )
            out_ref[...] += res[:rows] + res[rows:]

        chunks(total, body)

    out = pl.pallas_call(
        kernel, out_shape=jax.ShapeDtypeStruct((rows, HI), jnp.float32)
    )(values, first_ids, basis16)
    per_shift = out.reshape(4, knots)
    grad = jnp.zeros((knots + 3,), jnp.float32)
    for q in range(4):
        grad = grad.at[q:q + knots].add(per_shift[q])
    return grad


def per_device(
    observed_residual,
    source_partials,
    spread_derivative_table,
    detector_index,
    first_knot_interval,
    interval_fraction,
    live_slot_count,
    slot_owned_source,
):
    rows = observed_residual.shape[1]
    n_time = lax.axis_size("tm")
    n_share = lax.axis_size("src")
    n_ranks = n_time * n_share
    capacity = rows // n_ranks
    n_params = source_partials.shape[0]
    detector_count = spread_derivative_table.shape[1]
    knots = KN
    n_knots = n_time * knots
    owned = SRC_DEV
    everyone = ("tm", "src")
    place = jnp.arange(capacity, dtype=jnp.int32)[None, :]
    live = (place < live_slot_count[0][:, None]).astype(jnp.float32).reshape(1, rows)
    indicator = (
        detector_index[None, :] == jnp.arange(detector_count, dtype=jnp.int32)[:, None]
    ).astype(jnp.float32)
    weight_factor = jnp.dot(
        spread_derivative_table,
        indicator,
        precision=lax.Precision.HIGHEST,
        preferred_element_type=jnp.float32,
    )
    weight_sq = live * jnp.sum(weight_factor * weight_factor, axis=0, keepdims=True)
    basis16 = jnp.repeat(jnp.stack(spline_basis(interval_fraction), axis=0), knots // HI, axis=0)
    first_ids = first_knot_interval.reshape(1, rows)
    ids = slot_owned_source[0].reshape(1, rows)
    zbar0 = live * jnp.sum(weight_factor * observed_residual, axis=0, keepdims=True)

    packed = jnp.concatenate(
        [
            source_partials,
            zbar0,
            weight_sq,
            interval_fraction[None],
            first_knot_interval.astype(jnp.float32)[None],
        ],
        axis=0,
    )
    n_rows = packed.shape[0]
    blocks = packed.reshape(n_rows, n_ranks, capacity).transpose(1, 0, 2).reshape(n_ranks, n_rows * capacity)
    got = lax.all_to_all(blocks, everyone, 0, 0, tiled=True)
    got = got.reshape(n_ranks, n_rows, capacity).transpose(1, 0, 2).reshape(n_rows, rows)
    held = got[:n_params]
    zbar0_own = got[n_params:n_params + 1]
    weight_sq_own = got[n_params + 1:n_params + 2]
    basis_own = jnp.concatenate(spline_basis(got[n_params + 2:n_params + 3]), axis=0)
    slot_device = jnp.arange(rows, dtype=jnp.int32)[None, :] // capacity
    base_own = (slot_device // n_share) * knots + got[n_params + 3:n_params + 4].astype(jnp.int32)
    table_rows = n_params * (owned // HI)

    def combine(part_a, s_norm):
        mine = jnp.concatenate([part_a, s_norm[None]])
        every = lax.all_to_all(
            jnp.broadcast_to(mine[None, :], (n_ranks, knots + 4)), everyone, 0, 0, tiled=True
        )
        block = jnp.sum(every[:, :knots + 3].reshape(n_time, n_share, knots + 3), axis=1)
        main = block[:, :knots].at[1:, :3].add(block[:-1, knots:])
        grad_a = main.reshape(n_knots)
        norm = jnp.sum(every[:, knots + 3]) + jnp.sum(grad_a * grad_a)
        return grad_a, norm

    def forward(zsrc, dir_a, extra):
        extended = jnp.concatenate([dir_a, jnp.zeros((3,), jnp.float32)])
        shift_own, payload = knot_gather(
            extended, base_own, basis_own, zsrc, weight_sq_own, extra, n_knots, n_ranks, capacity
        )
        back = lax.all_to_all(payload, everyone, 0, 0, tiled=True)
        totals = jnp.sum(back[:, :2], axis=0)
        return shift_own, back[:, 128:].reshape(1, rows) * live, totals[0], totals[1]

    sol_s = jnp.zeros((table_rows, HI), jnp.float32)
    sol_a = jnp.zeros((n_knots,), jnp.float32)
    resid = observed_residual
    zbar_slot = zbar0
    part_a = knot_scatter(zbar_slot, first_ids, basis16, knots)
    part_a, held, zbar0_own = lax.optimization_barrier((part_a, held, zbar0_own))
    grad_a, gamma_a = combine(part_a, jnp.zeros((), jnp.float32))
    grad_s = source_scatter(held * zbar0_own, ids, owned)
    extra = jnp.sum(grad_s * grad_s)
    dir_s, dir_a = (grad_s, grad_a)
    pulled = source_gather(dir_s, ids, held)
    for step in range(ITERS):
        shift_own, shift_slot, image_sq, extra_sum = forward(pulled, dir_a, extra)
        if step == 0:
            gamma = extra_sum + gamma_a
        alpha = gamma / image_sq
        sol_s = sol_s + alpha * dir_s
        sol_a = sol_a + alpha * dir_a
        resid = resid - alpha * (weight_factor * shift_slot)
        if step + 1 < ITERS:
            pushed = source_scatter(held * (weight_sq_own * shift_own), ids, owned)
            zbar_slot = zbar_slot - alpha * (weight_sq * shift_slot)
            grad_s = grad_s - alpha * pushed
            grad_a, fresh = combine(
                knot_scatter(zbar_slot, first_ids, basis16, knots),
                jnp.sum(grad_s * grad_s),
            )
            raw = source_gather(grad_s, ids, held)
            beta = fresh / gamma
            dir_s = grad_s + beta * dir_s
            dir_a = grad_a + beta * dir_a
            pulled = raw + beta * pulled
            gamma = fresh
            extra = jnp.zeros((), jnp.float32)
    mine_a = lax.dynamic_slice(sol_a, (lax.axis_index("tm") * knots,), (knots,))
    return (sol_s.reshape(n_params, owned), mine_a, resid)


def solution(mesh):
    placed = (
        P(None, ("tm", "src")),
        P(None, ("tm", "src")),
        P(),
        P(("tm", "src")),
        P(("tm", "src")),
        P(("tm", "src")),
        P(("tm", "src"), None),
        P(("tm", "src"), None),
    )
    return jax.shard_map(
        per_device,
        mesh=mesh,
        in_specs=placed,
        out_specs=(P(None, ("tm", "src")), P("tm"), P(None, ("tm", "src"))),
        check_vma=False,
    )
```

```python
import jax
import jax.numpy as jnp
from jax import lax
from jax.experimental import pallas as pl
from jax.experimental.pallas import tpu as pltpu
from jax.sharding import PartitionSpec as P

SRC_DEV = 32768
KN = 1024
ITERS = 2
HI = 256
CHUNK = 4096


def passed_along(block, axis, distance):
    devices = range(lax.axis_size(axis))
    route = [(i - distance, i) for i in devices if i - distance in devices]
    return lax.ppermute(block, axis, route)


def spline_basis(frac):
    u2 = frac * frac
    u3 = u2 * frac
    one = 1.0 - frac
    return [
        one * one * one / 6.0,
        (3.0 * u3 - 6.0 * u2 + 4.0) / 6.0,
        (-3.0 * u3 + 3.0 * u2 + 3.0 * frac + 1.0) / 6.0,
        u3 / 6.0,
    ]


def pieces(x):
    h = x.astype(jnp.bfloat16)
    m = (x - h.astype(jnp.float32)).astype(jnp.bfloat16)
    return h, m


def hot_rows(ids, width):
    low = jnp.bitwise_and(ids, HI - 1)
    return (lax.broadcasted_iota(jnp.int32, (HI, width), 0) == low).astype(jnp.bfloat16)


def group_mask(ids, rows, width, groups):
    high = lax.shift_right_logical(ids, 8)
    iota = lax.broadcasted_iota(jnp.int32, (rows, width), 0)
    return (iota % groups) == high


def chunks(total, body):
    def step(i, carry):
        body(pl.multiple_of(i * CHUNK, CHUNK))
        return carry

    lax.fori_loop(0, total // CHUNK, step, 0)


def split_into(src_ref, big_ref):
    rows = src_ref.shape[0]
    for k, part in enumerate(pieces(src_ref[...])):
        big_ref[k * rows:(k + 1) * rows, :] = part


def source_gather(table, ids, held):
    n, total = held.shape
    rows = table.shape[0]
    cols = rows // n

    def kernel(tab_ref, ids_ref, held_ref, out_ref, big_ref):
        split_into(tab_ref, big_ref)

        def body(off):
            idc = ids_ref[:, pl.ds(off, CHUNK)]
            picked = jnp.dot(big_ref[...], hot_rows(idc, CHUNK), preferred_element_type=jnp.float32)
            sel = group_mask(idc, cols, CHUNK, cols)
            weights = held_ref[:, pl.ds(off, CHUNK)]
            column = jnp.zeros((1, CHUNK), jnp.float32)
            for p in range(n):
                acc = (
                    picked[p * cols:(p + 1) * cols]
                    + picked[rows + p * cols:rows + (p + 1) * cols]
                )
                value = jnp.sum(jnp.where(sel, acc, 0.0), axis=0, keepdims=True)
                column = column + weights[p:p + 1] * value
            out_ref[:, pl.ds(off, CHUNK)] = column

        chunks(total, body)

    return pl.pallas_call(
        kernel,
        out_shape=jax.ShapeDtypeStruct((1, total), jnp.float32),
        scratch_shapes=[pltpu.VMEM((2 * rows, HI), jnp.bfloat16)],
    )(table, ids, held)


def source_scatter(values, ids, width):
    n, total = values.shape
    cols = width // HI
    rows = n * cols

    def kernel(val_ref, ids_ref, out_ref):
        out_ref[...] = jnp.zeros(out_ref.shape, jnp.float32)

        def body(off):
            idc = ids_ref[:, pl.ds(off, CHUNK)]
            v = val_ref[:, pl.ds(off, CHUNK)]
            sel = group_mask(idc, cols, CHUNK, cols)
            parts = []
            for piece in pieces(v):
                for p in range(n):
                    parts.append(jnp.where(sel, piece[p:p + 1, :], jnp.zeros((), jnp.bfloat16)))
            spread = jnp.concatenate(parts, axis=0)
            res = lax.dot_general(
                spread, hot_rows(idc, CHUNK), (((1,), (1,)), ((), ())),
                preferred_element_type=jnp.float32,
            )
            out_ref[...] += res[:rows] + res[rows:]

        chunks(total, body)

    return pl.pallas_call(
        kernel, out_shape=jax.ShapeDtypeStruct((rows, HI), jnp.float32)
    )(values, ids)


def knot_gather(extended, first_ids, basis, zsrc, weight, extra, knots, parts, width):
    total = first_ids.shape[1]
    cols = knots // HI
    shifted = jnp.stack([extended[q:q + knots] for q in range(4)], axis=0)
    rows = 4 * cols
    per_chunk = CHUNK // width
    line = 128 + -(-width // 128) * 128

    def kernel(tab_ref, ids_ref, basis_ref, zsrc_ref, weight_ref, extra_ref, out_ref, pay_ref, big_ref, norm_ref):
        split_into(tab_ref, big_ref)
        norm_ref[...] = jnp.zeros(norm_ref.shape, jnp.float32)

        for i in range(total // CHUNK):
            off = i * CHUNK
            idc = ids_ref[:, pl.ds(off, CHUNK)]
            picked = jnp.dot(big_ref[...], hot_rows(idc, CHUNK), preferred_element_type=jnp.float32)
            acc = picked[:rows] + picked[rows:]
            sel = group_mask(idc, cols, CHUNK, cols)
            b = basis_ref[:, pl.ds(off, CHUNK)]
            z = jnp.zeros((1, CHUNK), jnp.float32)
            for q in range(4):
                value = jnp.sum(jnp.where(sel, acc[q * cols:(q + 1) * cols], 0.0), axis=0, keepdims=True)
                z = z + b[q:q + 1] * value
            shift = zsrc_ref[:, pl.ds(off, CHUNK)] + z
            out_ref[:, pl.ds(off, CHUNK)] = shift
            for r in range(per_chunk):
                start = (i * per_chunk + r) * line + 128
                pay_ref[:, start:start + width] = shift[:, r * width:(r + 1) * width]
            norm_ref[...] += jnp.sum(weight_ref[:, pl.ds(off, CHUNK)] * shift * shift, axis=1, keepdims=True)

        lane = lax.broadcasted_iota(jnp.int32, (1, 128), 1)
        sums = jnp.where(lane == 0, norm_ref[...], jnp.where(lane == 1, extra_ref[...], 0.0))
        for r in range(parts):
            pay_ref[:, r * line:r * line + 128] = sums
            if line > 128 + width:
                pay_ref[:, r * line + 128 + width:(r + 1) * line] = jnp.zeros((1, line - 128 - width), jnp.float32)

    return pl.pallas_call(
        kernel,
        out_shape=(
            jax.ShapeDtypeStruct((1, total), jnp.float32),
            jax.ShapeDtypeStruct((1, parts * line), jnp.float32),
        ),
        scratch_shapes=[pltpu.VMEM((2 * rows, HI), jnp.bfloat16), pltpu.VMEM((1, 1), jnp.float32)],
    )(shifted.reshape(rows, HI), first_ids, basis, zsrc, weight, extra.reshape(1, 1))


def knot_scatter(values, first_ids, basis16, knots):
    total = first_ids.shape[1]
    cols = knots // HI
    rows = 4 * cols

    def kernel(val_ref, ids_ref, basis_ref, out_ref):
        out_ref[...] = jnp.zeros(out_ref.shape, jnp.float32)

        def body(off):
            idc = ids_ref[:, pl.ds(off, CHUNK)]
            sel = group_mask(idc, rows, CHUNK, cols)
            v = jnp.where(sel, basis_ref[:, pl.ds(off, CHUNK)] * val_ref[:, pl.ds(off, CHUNK)], 0.0)
            spread = jnp.concatenate(pieces(v), axis=0)
            res = lax.dot_general(
                spread, hot_rows(idc, CHUNK), (((1,), (1,)), ((), ())),
                preferred_element_type=jnp.float32,
            )
            out_ref[...] += res[:rows] + res[rows:]

        chunks(total, body)

    out = pl.pallas_call(
        kernel, out_shape=jax.ShapeDtypeStruct((rows, HI), jnp.float32)
    )(values, first_ids, basis16)
    per_shift = out.reshape(4, knots)
    grad = jnp.zeros((knots + 3,), jnp.float32)
    for q in range(4):
        grad = grad.at[q:q + knots].add(per_shift[q])
    return grad


def per_device(
    observed_residual,
    source_partials,
    spread_derivative_table,
    detector_index,
    first_knot_interval,
    interval_fraction,
    live_slot_count,
    slot_owned_source,
):
    rows = observed_residual.shape[1]
    n_time = lax.axis_size("tm")
    n_share = lax.axis_size("src")
    n_ranks = n_time * n_share
    capacity = rows // n_ranks
    n_params = source_partials.shape[0]
    detector_count = spread_derivative_table.shape[1]
    knots = KN
    n_knots = n_time * knots
    owned = SRC_DEV
    everyone = ("tm", "src")
    place = jnp.arange(capacity, dtype=jnp.int32)[None, :]
    live = (place < live_slot_count[0][:, None]).astype(jnp.float32).reshape(1, rows)
    indicator = (
        detector_index[None, :] == jnp.arange(detector_count, dtype=jnp.int32)[:, None]
    ).astype(jnp.float32)
    weight_factor = jnp.dot(
        spread_derivative_table,
        indicator,
        precision=lax.Precision.HIGHEST,
        preferred_element_type=jnp.float32,
    )
    weight_sq = live * jnp.sum(weight_factor * weight_factor, axis=0, keepdims=True)
    basis16 = jnp.repeat(jnp.stack(spline_basis(interval_fraction), axis=0), knots // HI, axis=0)
    first_ids = first_knot_interval.reshape(1, rows)
    ids = slot_owned_source[0].reshape(1, rows)
    zbar0 = live * jnp.sum(weight_factor * observed_residual, axis=0, keepdims=True)

    packed = jnp.concatenate(
        [
            source_partials,
            zbar0,
            weight_sq,
            interval_fraction[None],
            first_knot_interval.astype(jnp.float32)[None],
        ],
        axis=0,
    )
    n_rows = packed.shape[0]
    blocks = packed.reshape(n_rows, n_ranks, capacity).transpose(1, 0, 2).reshape(n_ranks, n_rows * capacity)
    got = lax.all_to_all(blocks, everyone, 0, 0, tiled=True)
    got = got.reshape(n_ranks, n_rows, capacity).transpose(1, 0, 2).reshape(n_rows, rows)
    held = got[:n_params]
    zbar0_own = got[n_params:n_params + 1]
    weight_sq_own = got[n_params + 1:n_params + 2]
    basis_own = jnp.concatenate(spline_basis(got[n_params + 2:n_params + 3]), axis=0)
    slot_device = jnp.arange(rows, dtype=jnp.int32)[None, :] // capacity
    base_own = (slot_device // n_share) * knots + got[n_params + 3:n_params + 4].astype(jnp.int32)
    table_rows = n_params * (owned // HI)

    def combine(part_a, s_norm):
        mine = jnp.concatenate([part_a, s_norm[None]])
        every = lax.all_to_all(
            jnp.broadcast_to(mine[None, :], (n_ranks, knots + 4)), everyone, 0, 0, tiled=True
        )
        block = jnp.sum(every[:, :knots + 3].reshape(n_time, n_share, knots + 3), axis=1)
        main = block[:, :knots].at[1:, :3].add(block[:-1, knots:])
        grad_a = main.reshape(n_knots)
        norm = jnp.sum(every[:, knots + 3]) + jnp.sum(grad_a * grad_a)
        return grad_a, norm

    def forward(zsrc, dir_a, extra):
        extended = jnp.concatenate([dir_a, jnp.zeros((3,), jnp.float32)])
        shift_own, payload = knot_gather(
            extended, base_own, basis_own, zsrc, weight_sq_own, extra, n_knots, n_ranks, capacity
        )
        back = lax.all_to_all(payload.reshape(n_ranks, -1), everyone, 0, 0, tiled=True)
        totals = jnp.sum(back[:, :2], axis=0)
        return shift_own, back[:, 128:128 + capacity].reshape(1, rows) * live, totals[0], totals[1]

    sol_s = jnp.zeros((table_rows, HI), jnp.float32)
    sol_a = jnp.zeros((n_knots,), jnp.float32)
    resid = observed_residual
    zbar_slot = zbar0
    part_a = knot_scatter(zbar_slot, first_ids, basis16, knots)
    part_a, held, zbar0_own = lax.optimization_barrier((part_a, held, zbar0_own))
    grad_a, gamma_a = combine(part_a, jnp.zeros((), jnp.float32))
    grad_s = source_scatter(held * zbar0_own, ids, owned)
    extra = jnp.sum(grad_s * grad_s)
    dir_s, dir_a = (grad_s, grad_a)
    pulled = source_gather(dir_s, ids, held)
    for step in range(ITERS):
        shift_own, shift_slot, image_sq, extra_sum = forward(pulled, dir_a, extra)
        if step == 0:
            gamma = extra_sum + gamma_a
        alpha = gamma / image_sq
        sol_s = sol_s + alpha * dir_s
        sol_a = sol_a + alpha * dir_a
        resid = resid - alpha * (weight_factor * shift_slot)
        if step + 1 < ITERS:
            pushed = source_scatter(held * (weight_sq_own * shift_own), ids, owned)
            zbar_slot = zbar_slot - alpha * (weight_sq * shift_slot)
            grad_s = grad_s - alpha * pushed
            grad_a, fresh = combine(
                knot_scatter(zbar_slot, first_ids, basis16, knots),
                jnp.sum(grad_s * grad_s),
            )
            raw = source_gather(grad_s, ids, held)
            beta = fresh / gamma
            dir_s = grad_s + beta * dir_s
            dir_a = grad_a + beta * dir_a
            pulled = raw + beta * pulled
            gamma = fresh
            extra = jnp.zeros((), jnp.float32)
    mine_a = lax.dynamic_slice(sol_a, (lax.axis_index("tm") * knots,), (knots,))
    return (sol_s.reshape(n_params, owned), mine_a, resid)


def solution(mesh):
    placed = (
        P(None, ("tm", "src")),
        P(None, ("tm", "src")),
        P(),
        P(("tm", "src")),
        P(("tm", "src")),
        P(("tm", "src")),
        P(("tm", "src"), None),
        P(("tm", "src"), None),
    )
    return jax.shard_map(
        per_device,
        mesh=mesh,
        in_specs=placed,
        out_specs=(P(None, ("tm", "src")), P("tm"), P(None, ("tm", "src"))),
        check_vma=False,
    )
```

```python
import jax
import jax.numpy as jnp
from jax import lax
from jax.experimental import pallas as pl
from jax.experimental.pallas import tpu as pltpu
from jax.sharding import PartitionSpec as P

SRC_DEV = 32768
KN = 1024
ITERS = 2
HI = 256
CHUNK = 4096


def passed_along(block, axis, distance):
    devices = range(lax.axis_size(axis))
    route = [(i - distance, i) for i in devices if i - distance in devices]
    return lax.ppermute(block, axis, route)


def spline_basis(frac):
    u2 = frac * frac
    u3 = u2 * frac
    one = 1.0 - frac
    return [
        one * one * one / 6.0,
        (3.0 * u3 - 6.0 * u2 + 4.0) / 6.0,
        (-3.0 * u3 + 3.0 * u2 + 3.0 * frac + 1.0) / 6.0,
        u3 / 6.0,
    ]


def pieces(x):
    h = x.astype(jnp.bfloat16)
    m = (x - h.astype(jnp.float32)).astype(jnp.bfloat16)
    return h, m


def hot_rows(ids, width):
    low = jnp.bitwise_and(ids, HI - 1)
    return (lax.broadcasted_iota(jnp.int32, (HI, width), 0) == low).astype(jnp.bfloat16)


def group_mask(ids, rows, width, groups):
    high = lax.shift_right_logical(ids, 8)
    iota = lax.broadcasted_iota(jnp.int32, (rows, width), 0)
    return (iota % groups) == high


def chunks(total, body):
    def step(i, carry):
        body(pl.multiple_of(i * CHUNK, CHUNK))
        return carry

    lax.fori_loop(0, total // CHUNK, step, 0)


def split_into(src_ref, big_ref):
    rows = src_ref.shape[0]
    for k, part in enumerate(pieces(src_ref[...])):
        big_ref[k * rows:(k + 1) * rows, :] = part


def source_gather(table, ids, held):
    n, total = held.shape
    rows = table.shape[0]
    cols = rows // n

    def kernel(tab_ref, ids_ref, held_ref, out_ref, big_ref):
        split_into(tab_ref, big_ref)

        def body(off):
            idc = ids_ref[:, pl.ds(off, CHUNK)]
            picked = jnp.dot(big_ref[...], hot_rows(idc, CHUNK), preferred_element_type=jnp.float32)
            sel = group_mask(idc, cols, CHUNK, cols)
            weights = held_ref[:, pl.ds(off, CHUNK)]
            column = jnp.zeros((1, CHUNK), jnp.float32)
            for p in range(n):
                acc = (
                    picked[p * cols:(p + 1) * cols]
                    + picked[rows + p * cols:rows + (p + 1) * cols]
                )
                value = jnp.sum(jnp.where(sel, acc, 0.0), axis=0, keepdims=True)
                column = column + weights[p:p + 1] * value
            out_ref[:, pl.ds(off, CHUNK)] = column

        chunks(total, body)

    return pl.pallas_call(
        kernel,
        out_shape=jax.ShapeDtypeStruct((1, total), jnp.float32),
        scratch_shapes=[pltpu.VMEM((2 * rows, HI), jnp.bfloat16)],
    )(table, ids, held)


def source_scatter(values, ids, width, with_norm=False):
    n, total = values.shape
    cols = width // HI
    rows = n * cols

    def kernel(val_ref, ids_ref, out_ref, *norm_ref):
        out_ref[...] = jnp.zeros(out_ref.shape, jnp.float32)

        def body(off):
            idc = ids_ref[:, pl.ds(off, CHUNK)]
            v = val_ref[:, pl.ds(off, CHUNK)]
            sel = group_mask(idc, cols, CHUNK, cols)
            parts = []
            for piece in pieces(v):
                for p in range(n):
                    parts.append(jnp.where(sel, piece[p:p + 1, :], jnp.zeros((), jnp.bfloat16)))
            spread = jnp.concatenate(parts, axis=0)
            res = lax.dot_general(
                spread, hot_rows(idc, CHUNK), (((1,), (1,)), ((), ())),
                preferred_element_type=jnp.float32,
            )
            out_ref[...] += res[:rows] + res[rows:]

        chunks(total, body)
        if with_norm:
            grad = out_ref[...]
            norm_ref[0][...] = jnp.sum(jnp.sum(grad * grad, axis=0, keepdims=True), axis=1, keepdims=True)

    shape = jax.ShapeDtypeStruct((rows, HI), jnp.float32)
    if not with_norm:
        return pl.pallas_call(kernel, out_shape=shape)(values, ids)
    grad, norm = pl.pallas_call(
        kernel, out_shape=(shape, jax.ShapeDtypeStruct((1, 1), jnp.float32))
    )(values, ids)
    return grad, norm.reshape(())


def knot_gather(extended, first_ids, basis, zsrc, weight, extra, knots, parts, width):
    total = first_ids.shape[1]
    cols = knots // HI
    shifted = jnp.stack([extended[q:q + knots] for q in range(4)], axis=0)
    rows = 4 * cols
    per_chunk = CHUNK // width
    line = 128 + -(-width // 128) * 128

    def kernel(tab_ref, ids_ref, basis_ref, zsrc_ref, weight_ref, extra_ref, out_ref, pay_ref, big_ref, norm_ref):
        split_into(tab_ref, big_ref)
        norm_ref[...] = jnp.zeros(norm_ref.shape, jnp.float32)

        for i in range(total // CHUNK):
            off = i * CHUNK
            idc = ids_ref[:, pl.ds(off, CHUNK)]
            picked = jnp.dot(big_ref[...], hot_rows(idc, CHUNK), preferred_element_type=jnp.float32)
            acc = picked[:rows] + picked[rows:]
            sel = group_mask(idc, cols, CHUNK, cols)
            b = basis_ref[:, pl.ds(off, CHUNK)]
            z = jnp.zeros((1, CHUNK), jnp.float32)
            for q in range(4):
                value = jnp.sum(jnp.where(sel, acc[q * cols:(q + 1) * cols], 0.0), axis=0, keepdims=True)
                z = z + b[q:q + 1] * value
            shift = zsrc_ref[:, pl.ds(off, CHUNK)] + z
            out_ref[:, pl.ds(off, CHUNK)] = shift
            for r in range(per_chunk):
                start = (i * per_chunk + r) * line + 128
                pay_ref[:, start:start + width] = shift[:, r * width:(r + 1) * width]
            norm_ref[...] += jnp.sum(weight_ref[:, pl.ds(off, CHUNK)] * shift * shift, axis=1, keepdims=True)

        lane = lax.broadcasted_iota(jnp.int32, (1, 128), 1)
        sums = jnp.where(lane == 0, norm_ref[...], jnp.where(lane == 1, extra_ref[...], 0.0))
        for r in range(parts):
            pay_ref[:, r * line:r * line + 128] = sums
            if line > 128 + width:
                pay_ref[:, r * line + 128 + width:(r + 1) * line] = jnp.zeros((1, line - 128 - width), jnp.float32)

    return pl.pallas_call(
        kernel,
        out_shape=(
            jax.ShapeDtypeStruct((1, total), jnp.float32),
            jax.ShapeDtypeStruct((1, parts * line), jnp.float32),
        ),
        scratch_shapes=[pltpu.VMEM((2 * rows, HI), jnp.bfloat16), pltpu.VMEM((1, 1), jnp.float32)],
    )(shifted.reshape(rows, HI), first_ids, basis, zsrc, weight, extra.reshape(1, 1))


def knot_scatter(values, first_ids, basis16, knots):
    total = first_ids.shape[1]
    cols = knots // HI
    rows = 4 * cols

    def kernel(val_ref, ids_ref, basis_ref, out_ref):
        out_ref[...] = jnp.zeros(out_ref.shape, jnp.float32)

        def body(off):
            idc = ids_ref[:, pl.ds(off, CHUNK)]
            sel = group_mask(idc, rows, CHUNK, cols)
            v = jnp.where(sel, basis_ref[:, pl.ds(off, CHUNK)] * val_ref[:, pl.ds(off, CHUNK)], 0.0)
            spread = jnp.concatenate(pieces(v), axis=0)
            res = lax.dot_general(
                spread, hot_rows(idc, CHUNK), (((1,), (1,)), ((), ())),
                preferred_element_type=jnp.float32,
            )
            out_ref[...] += res[:rows] + res[rows:]

        chunks(total, body)

    out = pl.pallas_call(
        kernel, out_shape=jax.ShapeDtypeStruct((rows, HI), jnp.float32)
    )(values, first_ids, basis16)
    per_shift = out.reshape(4, knots)
    grad = jnp.zeros((knots + 3,), jnp.float32)
    for q in range(4):
        grad = grad.at[q:q + knots].add(per_shift[q])
    return grad


def per_device(
    observed_residual,
    source_partials,
    spread_derivative_table,
    detector_index,
    first_knot_interval,
    interval_fraction,
    live_slot_count,
    slot_owned_source,
):
    rows = observed_residual.shape[1]
    n_time = lax.axis_size("tm")
    n_share = lax.axis_size("src")
    n_ranks = n_time * n_share
    capacity = rows // n_ranks
    n_params = source_partials.shape[0]
    detector_count = spread_derivative_table.shape[1]
    knots = KN
    n_knots = n_time * knots
    owned = SRC_DEV
    everyone = ("tm", "src")
    place = jnp.arange(capacity, dtype=jnp.int32)[None, :]
    live = (place < live_slot_count[0][:, None]).astype(jnp.float32).reshape(1, rows)
    indicator = (
        detector_index[None, :] == jnp.arange(detector_count, dtype=jnp.int32)[:, None]
    ).astype(jnp.float32)
    weight_factor = jnp.dot(
        spread_derivative_table,
        indicator,
        precision=lax.Precision.HIGHEST,
        preferred_element_type=jnp.float32,
    )
    weight_sq = live * jnp.sum(weight_factor * weight_factor, axis=0, keepdims=True)
    basis16 = jnp.repeat(jnp.stack(spline_basis(interval_fraction), axis=0), knots // HI, axis=0)
    first_ids = first_knot_interval.reshape(1, rows)
    ids = slot_owned_source[0].reshape(1, rows)
    zbar0 = live * jnp.sum(weight_factor * observed_residual, axis=0, keepdims=True)

    packed = jnp.concatenate(
        [
            source_partials,
            zbar0,
            weight_sq,
            interval_fraction[None],
            first_knot_interval.astype(jnp.float32)[None],
        ],
        axis=0,
    )
    n_rows = packed.shape[0]
    blocks = packed.reshape(n_rows, n_ranks, capacity).transpose(1, 0, 2).reshape(n_ranks, n_rows * capacity)
    got = lax.all_to_all(blocks, everyone, 0, 0, tiled=True)
    got = got.reshape(n_ranks, n_rows, capacity).transpose(1, 0, 2).reshape(n_rows, rows)
    held = got[:n_params]
    zbar0_own = got[n_params:n_params + 1]
    weight_sq_own = got[n_params + 1:n_params + 2]
    basis_own = jnp.concatenate(spline_basis(got[n_params + 2:n_params + 3]), axis=0)
    slot_device = jnp.arange(rows, dtype=jnp.int32)[None, :] // capacity
    base_own = (slot_device // n_share) * knots + got[n_params + 3:n_params + 4].astype(jnp.int32)
    table_rows = n_params * (owned // HI)

    def outgoing(part_a, s_norm):
        mine = jnp.concatenate([part_a, s_norm[None]])
        return jnp.broadcast_to(mine[None, :], (n_ranks, knots + 4))

    def combine(sent):
        every = lax.all_to_all(sent, everyone, 0, 0, tiled=True)
        block = jnp.sum(every[:, :knots + 3].reshape(n_time, n_share, knots + 3), axis=1)
        main = block[:, :knots].at[1:, :3].add(block[:-1, knots:])
        grad_a = main.reshape(n_knots)
        norm = jnp.sum(every[:, knots + 3]) + jnp.sum(grad_a * grad_a)
        return grad_a, norm

    def forward(zsrc, dir_a, extra):
        extended = jnp.concatenate([dir_a, jnp.zeros((3,), jnp.float32)])
        shift_own, payload = knot_gather(
            extended, base_own, basis_own, zsrc, weight_sq_own, extra, n_knots, n_ranks, capacity
        )
        back = lax.all_to_all(payload.reshape(n_ranks, -1), everyone, 0, 0, tiled=True)
        totals = jnp.sum(back[:, :2], axis=0)
        return shift_own, back[:, 128:128 + capacity].reshape(1, rows) * live, totals[0], totals[1]

    sol_s = jnp.zeros((n_params, owned), jnp.float32)
    sol_a = jnp.zeros((n_knots,), jnp.float32)
    resid = observed_residual
    zbar_slot = zbar0
    sent = outgoing(knot_scatter(zbar_slot, first_ids, basis16, knots), jnp.zeros((), jnp.float32))
    sent, held, zbar0_own = lax.optimization_barrier((sent, held, zbar0_own))
    grad_a, gamma_a = combine(sent)
    grad_s, extra = source_scatter(held * zbar0_own, ids, owned, with_norm=True)
    dir_s, dir_a = (grad_s, grad_a)
    pulled = source_gather(dir_s, ids, held)
    for step in range(ITERS):
        shift_own, shift_slot, image_sq, extra_sum = forward(pulled, dir_a, extra)
        if step == 0:
            gamma = extra_sum + gamma_a
        alpha = gamma / image_sq
        sol_s = sol_s + alpha * dir_s.reshape(n_params, owned)
        sol_a = sol_a + alpha * dir_a
        resid = resid - alpha * (weight_factor * shift_slot)
        if step + 1 < ITERS:
            pushed = source_scatter(held * (weight_sq_own * shift_own), ids, owned)
            zbar_slot = zbar_slot - alpha * (weight_sq * shift_slot)
            grad_s = grad_s - alpha * pushed
            grad_a, fresh = combine(
                outgoing(knot_scatter(zbar_slot, first_ids, basis16, knots), jnp.sum(grad_s * grad_s))
            )
            raw = source_gather(grad_s, ids, held)
            beta = fresh / gamma
            dir_s = grad_s + beta * dir_s
            dir_a = grad_a + beta * dir_a
            pulled = raw + beta * pulled
            gamma = fresh
            extra = jnp.zeros((), jnp.float32)
    mine_a = lax.dynamic_slice(sol_a, (lax.axis_index("tm") * knots,), (knots,))
    return (sol_s, mine_a, resid)


def solution(mesh):
    placed = (
        P(None, ("tm", "src")),
        P(None, ("tm", "src")),
        P(),
        P(("tm", "src")),
        P(("tm", "src")),
        P(("tm", "src")),
        P(("tm", "src"), None),
        P(("tm", "src"), None),
    )
    return jax.shard_map(
        per_device,
        mesh=mesh,
        in_specs=placed,
        out_specs=(P(None, ("tm", "src")), P("tm"), P(None, ("tm", "src"))),
        check_vma=False,
    )
```

```python
import jax
import jax.numpy as jnp
from jax import lax
from jax.experimental import pallas as pl
from jax.experimental.pallas import tpu as pltpu
from jax.sharding import PartitionSpec as P

SRC_DEV = 32768
KN = 1024
ITERS = 2
HI = 256
CHUNK = 4096


def passed_along(block, axis, distance):
    devices = range(lax.axis_size(axis))
    route = [(i - distance, i) for i in devices if i - distance in devices]
    return lax.ppermute(block, axis, route)


def spline_basis(frac):
    u2 = frac * frac
    u3 = u2 * frac
    one = 1.0 - frac
    return [
        one * one * one / 6.0,
        (3.0 * u3 - 6.0 * u2 + 4.0) / 6.0,
        (-3.0 * u3 + 3.0 * u2 + 3.0 * frac + 1.0) / 6.0,
        u3 / 6.0,
    ]


def pieces(x):
    h = x.astype(jnp.bfloat16)
    m = (x - h.astype(jnp.float32)).astype(jnp.bfloat16)
    return h, m


def hot_rows(ids, width):
    low = jnp.bitwise_and(ids, HI - 1)
    return (lax.broadcasted_iota(jnp.int32, (HI, width), 0) == low).astype(jnp.bfloat16)


def group_mask(ids, rows, width, groups):
    high = lax.shift_right_logical(ids, 8)
    iota = lax.broadcasted_iota(jnp.int32, (rows, width), 0)
    return (iota % groups) == high


def chunks(total, body):
    def step(i, carry):
        body(pl.multiple_of(i * CHUNK, CHUNK))
        return carry

    lax.fori_loop(0, total // CHUNK, step, 0)


def split_into(src_ref, big_ref):
    rows = src_ref.shape[0]
    for k, part in enumerate(pieces(src_ref[...])):
        big_ref[k * rows:(k + 1) * rows, :] = part


def source_gather(table, ids, held):
    n, total = held.shape
    rows = table.shape[0]
    cols = rows // n

    def kernel(tab_ref, ids_ref, held_ref, out_ref, big_ref):
        split_into(tab_ref, big_ref)

        def body(off):
            idc = ids_ref[:, pl.ds(off, CHUNK)]
            picked = jnp.dot(big_ref[...], hot_rows(idc, CHUNK), preferred_element_type=jnp.float32)
            sel = group_mask(idc, cols, CHUNK, cols)
            weights = held_ref[:, pl.ds(off, CHUNK)]
            column = jnp.zeros((1, CHUNK), jnp.float32)
            for p in range(n):
                acc = (
                    picked[p * cols:(p + 1) * cols]
                    + picked[rows + p * cols:rows + (p + 1) * cols]
                )
                value = jnp.sum(jnp.where(sel, acc, 0.0), axis=0, keepdims=True)
                column = column + weights[p:p + 1] * value
            out_ref[:, pl.ds(off, CHUNK)] = column

        chunks(total, body)

    return pl.pallas_call(
        kernel,
        out_shape=jax.ShapeDtypeStruct((1, total), jnp.float32),
        scratch_shapes=[pltpu.VMEM((2 * rows, HI), jnp.bfloat16)],
    )(table, ids, held)


def source_scatter(values, ids, width, with_norm=False):
    n, total = values.shape
    cols = width // HI
    rows = n * cols

    def kernel(val_ref, ids_ref, out_ref, *norm_ref):
        out_ref[...] = jnp.zeros(out_ref.shape, jnp.float32)

        def body(off):
            idc = ids_ref[:, pl.ds(off, CHUNK)]
            v = val_ref[:, pl.ds(off, CHUNK)]
            sel = group_mask(idc, cols, CHUNK, cols)
            parts = []
            for piece in pieces(v):
                for p in range(n):
                    parts.append(jnp.where(sel, piece[p:p + 1, :], jnp.zeros((), jnp.bfloat16)))
            spread = jnp.concatenate(parts, axis=0)
            res = lax.dot_general(
                spread, hot_rows(idc, CHUNK), (((1,), (1,)), ((), ())),
                preferred_element_type=jnp.float32,
            )
            out_ref[...] += res[:rows] + res[rows:]

        chunks(total, body)
        if with_norm:
            grad = out_ref[...]
            norm_ref[0][...] = jnp.sum(jnp.sum(grad * grad, axis=0, keepdims=True), axis=1, keepdims=True)

    shape = jax.ShapeDtypeStruct((rows, HI), jnp.float32)
    if not with_norm:
        return pl.pallas_call(kernel, out_shape=shape)(values, ids)
    grad, norm = pl.pallas_call(
        kernel, out_shape=(shape, jax.ShapeDtypeStruct((1, 1), jnp.float32))
    )(values, ids)
    return grad, norm.reshape(())


def knot_gather(extended, first_ids, basis, zsrc, weight, extra, knots, parts, width):
    total = first_ids.shape[1]
    cols = knots // HI
    shifted = jnp.stack([extended[q:q + knots] for q in range(4)], axis=0)
    rows = 4 * cols
    per_chunk = CHUNK // width
    line = 128 + -(-width // 128) * 128

    def kernel(tab_ref, ids_ref, basis_ref, zsrc_ref, weight_ref, extra_ref, out_ref, pay_ref, big_ref, norm_ref):
        split_into(tab_ref, big_ref)
        norm_ref[...] = jnp.zeros(norm_ref.shape, jnp.float32)

        for i in range(total // CHUNK):
            off = i * CHUNK
            idc = ids_ref[:, pl.ds(off, CHUNK)]
            picked = jnp.dot(big_ref[...], hot_rows(idc, CHUNK), preferred_element_type=jnp.float32)
            acc = picked[:rows] + picked[rows:]
            sel = group_mask(idc, cols, CHUNK, cols)
            b = basis_ref[:, pl.ds(off, CHUNK)]
            z = jnp.zeros((1, CHUNK), jnp.float32)
            for q in range(4):
                value = jnp.sum(jnp.where(sel, acc[q * cols:(q + 1) * cols], 0.0), axis=0, keepdims=True)
                z = z + b[q:q + 1] * value
            shift = zsrc_ref[:, pl.ds(off, CHUNK)] + z
            out_ref[:, pl.ds(off, CHUNK)] = shift
            for r in range(per_chunk):
                start = (i * per_chunk + r) * line + 128
                pay_ref[:, start:start + width] = shift[:, r * width:(r + 1) * width]
            norm_ref[...] += jnp.sum(weight_ref[:, pl.ds(off, CHUNK)] * shift * shift, axis=1, keepdims=True)

        lane = lax.broadcasted_iota(jnp.int32, (1, 128), 1)
        sums = jnp.where(lane == 0, norm_ref[...], jnp.where(lane == 1, extra_ref[...], 0.0))
        for r in range(parts):
            pay_ref[:, r * line:r * line + 128] = sums
            if line > 128 + width:
                pay_ref[:, r * line + 128 + width:(r + 1) * line] = jnp.zeros((1, line - 128 - width), jnp.float32)

    return pl.pallas_call(
        kernel,
        out_shape=(
            jax.ShapeDtypeStruct((1, total), jnp.float32),
            jax.ShapeDtypeStruct((1, parts * line), jnp.float32),
        ),
        scratch_shapes=[pltpu.VMEM((2 * rows, HI), jnp.bfloat16), pltpu.VMEM((1, 1), jnp.float32)],
    )(shifted.reshape(rows, HI), first_ids, basis, zsrc, weight, extra.reshape(1, 1))


def knot_scatter(values, first_ids, basis16, s_norm, knots, parts):
    total = first_ids.shape[1]
    cols = knots // HI
    rows = 4 * cols
    line = 128 + (cols + 1) * HI

    def kernel(val_ref, ids_ref, basis_ref, norm_ref, pay_ref, acc_ref):
        acc_ref[...] = jnp.zeros(acc_ref.shape, jnp.float32)

        def body(off):
            idc = ids_ref[:, pl.ds(off, CHUNK)]
            sel = group_mask(idc, rows, CHUNK, cols)
            v = jnp.where(sel, basis_ref[:, pl.ds(off, CHUNK)] * val_ref[:, pl.ds(off, CHUNK)], 0.0)
            spread = jnp.concatenate(pieces(v), axis=0)
            res = lax.dot_general(
                spread, hot_rows(idc, CHUNK), (((1,), (1,)), ((), ())),
                preferred_element_type=jnp.float32,
            )
            acc_ref[...] += res[:rows] + res[rows:]

        chunks(total, body)
        lane = lax.broadcasted_iota(jnp.int32, (cols, HI), 1)
        same = acc_ref[0:cols, :]
        carried = jnp.zeros((cols, HI), jnp.float32)
        for q in range(1, 4):
            moved = pltpu.roll(acc_ref[q * cols:(q + 1) * cols, :], q, 1)
            same = same + jnp.where(lane >= q, moved, 0.0)
            carried = carried + jnp.where(lane < q, moved, 0.0)
        blank = jnp.zeros((1, HI), jnp.float32)
        grid = jnp.concatenate([same, blank], axis=0) + jnp.concatenate([blank, carried], axis=0)
        head = jnp.where(lax.broadcasted_iota(jnp.int32, (1, 128), 1) == 0, norm_ref[...], 0.0)
        row = jnp.concatenate([head] + [grid[c:c + 1, :] for c in range(cols + 1)], axis=1)
        for r in range(parts):
            pay_ref[:, r * line:(r + 1) * line] = row

    return pl.pallas_call(
        kernel,
        out_shape=jax.ShapeDtypeStruct((1, parts * line), jnp.float32),
        scratch_shapes=[pltpu.VMEM((rows, HI), jnp.float32)],
    )(values, first_ids, basis16, s_norm.reshape(1, 1)).reshape(parts, line)


def per_device(
    observed_residual,
    source_partials,
    spread_derivative_table,
    detector_index,
    first_knot_interval,
    interval_fraction,
    live_slot_count,
    slot_owned_source,
):
    rows = observed_residual.shape[1]
    n_time = lax.axis_size("tm")
    n_share = lax.axis_size("src")
    n_ranks = n_time * n_share
    capacity = rows // n_ranks
    n_params = source_partials.shape[0]
    detector_count = spread_derivative_table.shape[1]
    knots = KN
    n_knots = n_time * knots
    owned = SRC_DEV
    everyone = ("tm", "src")
    place = jnp.arange(capacity, dtype=jnp.int32)[None, :]
    live = (place < live_slot_count[0][:, None]).astype(jnp.float32).reshape(1, rows)
    indicator = (
        detector_index[None, :] == jnp.arange(detector_count, dtype=jnp.int32)[:, None]
    ).astype(jnp.float32)
    weight_factor = jnp.dot(
        spread_derivative_table,
        indicator,
        precision=lax.Precision.HIGHEST,
        preferred_element_type=jnp.float32,
    )
    weight_sq = live * jnp.sum(weight_factor * weight_factor, axis=0, keepdims=True)
    basis16 = jnp.repeat(jnp.stack(spline_basis(interval_fraction), axis=0), knots // HI, axis=0)
    first_ids = first_knot_interval.reshape(1, rows)
    ids = slot_owned_source[0].reshape(1, rows)
    zbar0 = live * jnp.sum(weight_factor * observed_residual, axis=0, keepdims=True)

    packed = jnp.concatenate(
        [
            source_partials,
            zbar0,
            weight_sq,
            interval_fraction[None],
            first_knot_interval.astype(jnp.float32)[None],
        ],
        axis=0,
    )
    n_rows = packed.shape[0]
    blocks = packed.reshape(n_rows, n_ranks, capacity).transpose(1, 0, 2).reshape(n_ranks, n_rows * capacity)
    got = lax.all_to_all(blocks, everyone, 0, 0, tiled=True)
    got = got.reshape(n_ranks, n_rows, capacity).transpose(1, 0, 2).reshape(n_rows, rows)
    held = got[:n_params]
    zbar0_own = got[n_params:n_params + 1]
    weight_sq_own = got[n_params + 1:n_params + 2]
    basis_own = jnp.concatenate(spline_basis(got[n_params + 2:n_params + 3]), axis=0)
    slot_device = jnp.arange(rows, dtype=jnp.int32)[None, :] // capacity
    base_own = (slot_device // n_share) * knots + got[n_params + 3:n_params + 4].astype(jnp.int32)
    table_rows = n_params * (owned // HI)

    def combine(sent):
        every = lax.all_to_all(sent, everyone, 0, 0, tiled=True)
        block = jnp.sum(every[:, 128:128 + knots + 3].reshape(n_time, n_share, knots + 3), axis=1)
        main = block[:, :knots].at[1:, :3].add(block[:-1, knots:])
        grad_a = main.reshape(n_knots)
        norm = jnp.sum(every[:, 0]) + jnp.sum(grad_a * grad_a)
        return grad_a, norm

    def forward(zsrc, dir_a, extra):
        extended = jnp.concatenate([dir_a, jnp.zeros((3,), jnp.float32)])
        shift_own, payload = knot_gather(
            extended, base_own, basis_own, zsrc, weight_sq_own, extra, n_knots, n_ranks, capacity
        )
        back = lax.all_to_all(payload.reshape(n_ranks, -1), everyone, 0, 0, tiled=True)
        totals = jnp.sum(back[:, :2], axis=0)
        return shift_own, back[:, 128:128 + capacity].reshape(1, rows) * live, totals[0], totals[1]

    sol_s = jnp.zeros((n_params, owned), jnp.float32)
    sol_a = jnp.zeros((n_knots,), jnp.float32)
    resid = observed_residual
    zbar_slot = zbar0
    sent = knot_scatter(zbar_slot, first_ids, basis16, jnp.zeros((), jnp.float32), knots, n_ranks)
    sent, held, zbar0_own = lax.optimization_barrier((sent, held, zbar0_own))
    grad_a, gamma_a = combine(sent)
    grad_s, extra = source_scatter(held * zbar0_own, ids, owned, with_norm=True)
    dir_s, dir_a = (grad_s, grad_a)
    pulled = source_gather(dir_s, ids, held)
    for step in range(ITERS):
        shift_own, shift_slot, image_sq, extra_sum = forward(pulled, dir_a, extra)
        if step == 0:
            gamma = extra_sum + gamma_a
        alpha = gamma / image_sq
        sol_s = sol_s + alpha * lax.optimization_barrier(dir_s.reshape(n_params, owned))
        sol_a = sol_a + alpha * dir_a
        resid = resid - alpha * (weight_factor * shift_slot)
        if step + 1 < ITERS:
            pushed = source_scatter(held * (weight_sq_own * shift_own), ids, owned)
            zbar_slot = zbar_slot - alpha * (weight_sq * shift_slot)
            grad_s = grad_s - alpha * pushed
            grad_a, fresh = combine(
                knot_scatter(zbar_slot, first_ids, basis16, jnp.sum(grad_s * grad_s), knots, n_ranks)
            )
            raw = source_gather(grad_s, ids, held)
            beta = fresh / gamma
            dir_s = grad_s + beta * dir_s
            dir_a = grad_a + beta * dir_a
            pulled = raw + beta * pulled
            gamma = fresh
            extra = jnp.zeros((), jnp.float32)
    mine_a = lax.dynamic_slice(sol_a, (lax.axis_index("tm") * knots,), (knots,))
    return (sol_s, mine_a, resid)


def solution(mesh):
    placed = (
        P(None, ("tm", "src")),
        P(None, ("tm", "src")),
        P(),
        P(("tm", "src")),
        P(("tm", "src")),
        P(("tm", "src")),
        P(("tm", "src"), None),
        P(("tm", "src"), None),
    )
    return jax.shard_map(
        per_device,
        mesh=mesh,
        in_specs=placed,
        out_specs=(P(None, ("tm", "src")), P("tm"), P(None, ("tm", "src"))),
        check_vma=False,
    )
```

```python
import jax
import jax.numpy as jnp
from jax import lax
from jax.experimental import pallas as pl
from jax.experimental.pallas import tpu as pltpu
from jax.sharding import PartitionSpec as P

SRC_DEV = 32768
KN = 1024
ITERS = 2
HI = 256
CHUNK = 4096


def passed_along(block, axis, distance):
    devices = range(lax.axis_size(axis))
    route = [(i - distance, i) for i in devices if i - distance in devices]
    return lax.ppermute(block, axis, route)


def spline_basis(frac):
    u2 = frac * frac
    u3 = u2 * frac
    one = 1.0 - frac
    return [
        one * one * one / 6.0,
        (3.0 * u3 - 6.0 * u2 + 4.0) / 6.0,
        (-3.0 * u3 + 3.0 * u2 + 3.0 * frac + 1.0) / 6.0,
        u3 / 6.0,
    ]


def pieces(x):
    h = x.astype(jnp.bfloat16)
    m = (x - h.astype(jnp.float32)).astype(jnp.bfloat16)
    return h, m


def hot_rows(ids, width):
    low = jnp.bitwise_and(ids, HI - 1)
    return (lax.broadcasted_iota(jnp.int32, (HI, width), 0) == low).astype(jnp.bfloat16)


def group_mask(ids, rows, width, groups):
    high = lax.shift_right_logical(ids, 8)
    iota = lax.broadcasted_iota(jnp.int32, (rows, width), 0)
    return (iota % groups) == high


def chunks(total, body):
    def step(i, carry):
        body(pl.multiple_of(i * CHUNK, CHUNK))
        return carry

    lax.fori_loop(0, total // CHUNK, step, 0)


def split_into(src_ref, big_ref):
    rows = src_ref.shape[0]
    for k, part in enumerate(pieces(src_ref[...])):
        big_ref[k * rows:(k + 1) * rows, :] = part


def source_gather(table, ids, held):
    n, total = held.shape
    rows = table.shape[0]
    cols = rows // n

    def kernel(tab_ref, ids_ref, held_ref, out_ref, big_ref):
        split_into(tab_ref, big_ref)

        def body(off):
            idc = ids_ref[:, pl.ds(off, CHUNK)]
            picked = jnp.dot(big_ref[...], hot_rows(idc, CHUNK), preferred_element_type=jnp.float32)
            sel = group_mask(idc, cols, CHUNK, cols)
            weights = held_ref[:, pl.ds(off, CHUNK)]
            column = jnp.zeros((1, CHUNK), jnp.float32)
            for p in range(n):
                acc = (
                    picked[p * cols:(p + 1) * cols]
                    + picked[rows + p * cols:rows + (p + 1) * cols]
                )
                value = jnp.sum(jnp.where(sel, acc, 0.0), axis=0, keepdims=True)
                column = column + weights[p:p + 1] * value
            out_ref[:, pl.ds(off, CHUNK)] = column

        chunks(total, body)

    return pl.pallas_call(
        kernel,
        out_shape=jax.ShapeDtypeStruct((1, total), jnp.float32),
        scratch_shapes=[pltpu.VMEM((2 * rows, HI), jnp.bfloat16)],
    )(table, ids, held)


def source_scatter(values, scales, ids, width, with_norm=False):
    n, total = values.shape
    cols = width // HI
    rows = n * cols
    count = len(scales)

    def kernel(val_ref, *refs):
        scale_refs = refs[:count]
        ids_ref, out_ref = refs[count:count + 2]
        norm_ref = refs[count + 2:]
        out_ref[...] = jnp.zeros(out_ref.shape, jnp.float32)

        def body(off):
            idc = ids_ref[:, pl.ds(off, CHUNK)]
            scale = scale_refs[0][:, pl.ds(off, CHUNK)]
            for other in scale_refs[1:]:
                scale = scale * other[:, pl.ds(off, CHUNK)]
            v = val_ref[:, pl.ds(off, CHUNK)] * scale
            sel = group_mask(idc, cols, CHUNK, cols)
            parts = []
            for piece in pieces(v):
                for p in range(n):
                    parts.append(jnp.where(sel, piece[p:p + 1, :], jnp.zeros((), jnp.bfloat16)))
            spread = jnp.concatenate(parts, axis=0)
            res = lax.dot_general(
                spread, hot_rows(idc, CHUNK), (((1,), (1,)), ((), ())),
                preferred_element_type=jnp.float32,
            )
            out_ref[...] += res[:rows] + res[rows:]

        chunks(total, body)
        if with_norm:
            grad = out_ref[...]
            norm_ref[0][...] = jnp.sum(jnp.sum(grad * grad, axis=0, keepdims=True), axis=1, keepdims=True)

    shape = jax.ShapeDtypeStruct((rows, HI), jnp.float32)
    if not with_norm:
        return pl.pallas_call(kernel, out_shape=shape)(values, *scales, ids)
    grad, norm = pl.pallas_call(
        kernel, out_shape=(shape, jax.ShapeDtypeStruct((1, 1), jnp.float32))
    )(values, *scales, ids)
    return grad, norm.reshape(())


def knot_gather(extended, first_ids, basis, zsrc, weight, extra, knots, parts, width):
    total = first_ids.shape[1]
    cols = knots // HI
    shifted = jnp.stack([extended[q:q + knots] for q in range(4)], axis=0)
    rows = 4 * cols
    per_chunk = CHUNK // width
    line = 128 + -(-width // 128) * 128

    def kernel(tab_ref, ids_ref, basis_ref, zsrc_ref, weight_ref, extra_ref, out_ref, pay_ref, big_ref, norm_ref):
        split_into(tab_ref, big_ref)
        norm_ref[...] = jnp.zeros(norm_ref.shape, jnp.float32)

        for i in range(total // CHUNK):
            off = i * CHUNK
            idc = ids_ref[:, pl.ds(off, CHUNK)]
            picked = jnp.dot(big_ref[...], hot_rows(idc, CHUNK), preferred_element_type=jnp.float32)
            acc = picked[:rows] + picked[rows:]
            sel = group_mask(idc, cols, CHUNK, cols)
            b = basis_ref[:, pl.ds(off, CHUNK)]
            z = jnp.zeros((1, CHUNK), jnp.float32)
            for q in range(4):
                value = jnp.sum(jnp.where(sel, acc[q * cols:(q + 1) * cols], 0.0), axis=0, keepdims=True)
                z = z + b[q:q + 1] * value
            shift = zsrc_ref[:, pl.ds(off, CHUNK)] + z
            out_ref[:, pl.ds(off, CHUNK)] = shift
            for r in range(per_chunk):
                start = (i * per_chunk + r) * line + 128
                pay_ref[:, start:start + width] = shift[:, r * width:(r + 1) * width]
            norm_ref[...] += jnp.sum(weight_ref[:, pl.ds(off, CHUNK)] * shift * shift, axis=1, keepdims=True)

        lane = lax.broadcasted_iota(jnp.int32, (1, 128), 1)
        sums = jnp.where(lane == 0, norm_ref[...], jnp.where(lane == 1, extra_ref[...], 0.0))
        for r in range(parts):
            pay_ref[:, r * line:r * line + 128] = sums
            if line > 128 + width:
                pay_ref[:, r * line + 128 + width:(r + 1) * line] = jnp.zeros((1, line - 128 - width), jnp.float32)

    return pl.pallas_call(
        kernel,
        out_shape=(
            jax.ShapeDtypeStruct((1, total), jnp.float32),
            jax.ShapeDtypeStruct((1, parts * line), jnp.float32),
        ),
        scratch_shapes=[pltpu.VMEM((2 * rows, HI), jnp.bfloat16), pltpu.VMEM((1, 1), jnp.float32)],
    )(shifted.reshape(rows, HI), first_ids, basis, zsrc, weight, extra.reshape(1, 1))


def knot_scatter(values, first_ids, basis16, knots):
    total = first_ids.shape[1]
    cols = knots // HI
    rows = 4 * cols

    def kernel(val_ref, ids_ref, basis_ref, out_ref):
        out_ref[...] = jnp.zeros(out_ref.shape, jnp.float32)

        def body(off):
            idc = ids_ref[:, pl.ds(off, CHUNK)]
            sel = group_mask(idc, rows, CHUNK, cols)
            v = jnp.where(sel, basis_ref[:, pl.ds(off, CHUNK)] * val_ref[:, pl.ds(off, CHUNK)], 0.0)
            spread = jnp.concatenate(pieces(v), axis=0)
            res = lax.dot_general(
                spread, hot_rows(idc, CHUNK), (((1,), (1,)), ((), ())),
                preferred_element_type=jnp.float32,
            )
            out_ref[...] += res[:rows] + res[rows:]

        chunks(total, body)

    out = pl.pallas_call(
        kernel, out_shape=jax.ShapeDtypeStruct((rows, HI), jnp.float32)
    )(values, first_ids, basis16)
    per_shift = out.reshape(4, knots)
    grad = jnp.zeros((knots + 3,), jnp.float32)
    for q in range(4):
        grad = grad.at[q:q + knots].add(per_shift[q])
    return grad


def per_device(
    observed_residual,
    source_partials,
    spread_derivative_table,
    detector_index,
    first_knot_interval,
    interval_fraction,
    live_slot_count,
    slot_owned_source,
):
    rows = observed_residual.shape[1]
    n_time = lax.axis_size("tm")
    n_share = lax.axis_size("src")
    n_ranks = n_time * n_share
    capacity = rows // n_ranks
    n_params = source_partials.shape[0]
    detector_count = spread_derivative_table.shape[1]
    knots = KN
    n_knots = n_time * knots
    owned = SRC_DEV
    everyone = ("tm", "src")
    place = jnp.arange(capacity, dtype=jnp.int32)[None, :]
    live = (place < live_slot_count[0][:, None]).astype(jnp.float32).reshape(1, rows)
    indicator = (
        detector_index[None, :] == jnp.arange(detector_count, dtype=jnp.int32)[:, None]
    ).astype(jnp.float32)
    weight_factor = jnp.dot(
        spread_derivative_table,
        indicator,
        precision=lax.Precision.HIGHEST,
        preferred_element_type=jnp.float32,
    )
    weight_sq = live * jnp.sum(weight_factor * weight_factor, axis=0, keepdims=True)
    basis16 = jnp.repeat(jnp.stack(spline_basis(interval_fraction), axis=0), knots // HI, axis=0)
    first_ids = first_knot_interval.reshape(1, rows)
    ids = slot_owned_source[0].reshape(1, rows)
    zbar0 = live * jnp.sum(weight_factor * observed_residual, axis=0, keepdims=True)

    packed = jnp.concatenate(
        [
            source_partials,
            zbar0,
            weight_sq,
            interval_fraction[None],
            first_knot_interval.astype(jnp.float32)[None],
        ],
        axis=0,
    )
    n_rows = packed.shape[0]
    blocks = packed.reshape(n_rows, n_ranks, capacity).transpose(1, 0, 2).reshape(n_ranks, n_rows * capacity)
    got = lax.all_to_all(blocks, everyone, 0, 0, tiled=True)
    got = got.reshape(n_ranks, n_rows, capacity).transpose(1, 0, 2).reshape(n_rows, rows)
    held = got[:n_params]
    zbar0_own = got[n_params:n_params + 1]
    weight_sq_own = got[n_params + 1:n_params + 2]
    basis_own = jnp.concatenate(spline_basis(got[n_params + 2:n_params + 3]), axis=0)
    slot_device = jnp.arange(rows, dtype=jnp.int32)[None, :] // capacity
    base_own = (slot_device // n_share) * knots + got[n_params + 3:n_params + 4].astype(jnp.int32)
    table_rows = n_params * (owned // HI)

    def outgoing(part_a, s_norm):
        mine = jnp.concatenate([part_a, s_norm[None]])
        return jnp.broadcast_to(mine[None, :], (n_ranks, knots + 4))

    def combine(sent):
        every = lax.all_to_all(sent, everyone, 0, 0, tiled=True)
        block = jnp.sum(every[:, :knots + 3].reshape(n_time, n_share, knots + 3), axis=1)
        main = block[:, :knots].at[1:, :3].add(block[:-1, knots:])
        grad_a = main.reshape(n_knots)
        norm = jnp.sum(every[:, knots + 3]) + jnp.sum(grad_a * grad_a)
        return grad_a, norm

    def forward(zsrc, dir_a, extra):
        extended = jnp.concatenate([dir_a, jnp.zeros((3,), jnp.float32)])
        shift_own, payload = knot_gather(
            extended, base_own, basis_own, zsrc, weight_sq_own, extra, n_knots, n_ranks, capacity
        )
        back = lax.all_to_all(payload.reshape(n_ranks, -1), everyone, 0, 0, tiled=True)
        totals = jnp.sum(back[:, :2], axis=0)
        return shift_own, back[:, 128:128 + capacity].reshape(1, rows) * live, totals[0], totals[1]

    sol_s = jnp.zeros((n_params, owned), jnp.float32)
    sol_a = jnp.zeros((n_knots,), jnp.float32)
    resid = observed_residual
    zbar_slot = zbar0
    sent = outgoing(knot_scatter(zbar_slot, first_ids, basis16, knots), jnp.zeros((), jnp.float32))
    sent, held, zbar0_own = lax.optimization_barrier((sent, held, zbar0_own))
    grad_a, gamma_a = combine(sent)
    grad_s, extra = source_scatter(held, [zbar0_own], ids, owned, with_norm=True)
    dir_s, dir_a = (grad_s, grad_a)
    pulled = source_gather(dir_s, ids, held)
    for step in range(ITERS):
        shift_own, shift_slot, image_sq, extra_sum = forward(pulled, dir_a, extra)
        if step == 0:
            gamma = extra_sum + gamma_a
        alpha = gamma / image_sq
        sol_s = sol_s + alpha * dir_s.reshape(n_params, owned)
        sol_a = sol_a + alpha * dir_a
        resid = resid - alpha * (weight_factor * shift_slot)
        if step + 1 < ITERS:
            pushed = source_scatter(held, [weight_sq_own, shift_own], ids, owned)
            zbar_slot = zbar_slot - alpha * (weight_sq * shift_slot)
            grad_s = grad_s - alpha * pushed
            grad_a, fresh = combine(
                outgoing(knot_scatter(zbar_slot, first_ids, basis16, knots), jnp.sum(grad_s * grad_s))
            )
            raw = source_gather(grad_s, ids, held)
            beta = fresh / gamma
            dir_s = grad_s + beta * dir_s
            dir_a = grad_a + beta * dir_a
            pulled = raw + beta * pulled
            gamma = fresh
            extra = jnp.zeros((), jnp.float32)
    mine_a = lax.dynamic_slice(sol_a, (lax.axis_index("tm") * knots,), (knots,))
    return (sol_s, mine_a, resid)


def solution(mesh):
    placed = (
        P(None, ("tm", "src")),
        P(None, ("tm", "src")),
        P(),
        P(("tm", "src")),
        P(("tm", "src")),
        P(("tm", "src")),
        P(("tm", "src"), None),
        P(("tm", "src"), None),
    )
    return jax.shard_map(
        per_device,
        mesh=mesh,
        in_specs=placed,
        out_specs=(P(None, ("tm", "src")), P("tm"), P(None, ("tm", "src"))),
        check_vma=False,
    )
```

```python
import jax
import jax.numpy as jnp
from jax import lax
from jax.experimental import pallas as pl
from jax.experimental.pallas import tpu as pltpu
from jax.sharding import PartitionSpec as P

SRC_DEV = 32768
KN = 1024
ITERS = 2
HI = 256
CHUNK = 4096


def passed_along(block, axis, distance):
    devices = range(lax.axis_size(axis))
    route = [(i - distance, i) for i in devices if i - distance in devices]
    return lax.ppermute(block, axis, route)


def spline_basis(frac):
    u2 = frac * frac
    u3 = u2 * frac
    one = 1.0 - frac
    return [
        one * one * one / 6.0,
        (3.0 * u3 - 6.0 * u2 + 4.0) / 6.0,
        (-3.0 * u3 + 3.0 * u2 + 3.0 * frac + 1.0) / 6.0,
        u3 / 6.0,
    ]


def pieces(x):
    h = x.astype(jnp.bfloat16)
    m = (x - h.astype(jnp.float32)).astype(jnp.bfloat16)
    return h, m


def hot_rows(ids, width):
    low = jnp.bitwise_and(ids, HI - 1)
    return (lax.broadcasted_iota(jnp.int32, (HI, width), 0) == low).astype(jnp.bfloat16)


def group_mask(ids, rows, width, groups):
    high = lax.shift_right_logical(ids, 8)
    iota = lax.broadcasted_iota(jnp.int32, (rows, width), 0)
    return (iota % groups) == high


def chunks(total, body):
    def step(i, carry):
        body(pl.multiple_of(i * CHUNK, CHUNK))
        return carry

    lax.fori_loop(0, total // CHUNK, step, 0)


def split_into(src_ref, big_ref):
    rows = src_ref.shape[0]
    for k, part in enumerate(pieces(src_ref[...])):
        big_ref[k * rows:(k + 1) * rows, :] = part


def source_gather(table, ids, held):
    n, total = held.shape
    rows = table.shape[0]
    cols = rows // n

    def kernel(tab_ref, ids_ref, held_ref, out_ref, big_ref):
        split_into(tab_ref, big_ref)

        def body(off):
            idc = ids_ref[:, pl.ds(off, CHUNK)]
            picked = jnp.dot(big_ref[...], hot_rows(idc, CHUNK), preferred_element_type=jnp.float32)
            sel = group_mask(idc, cols, CHUNK, cols)
            weights = held_ref[:, pl.ds(off, CHUNK)]
            column = jnp.zeros((1, CHUNK), jnp.float32)
            for p in range(n):
                acc = (
                    picked[p * cols:(p + 1) * cols]
                    + picked[rows + p * cols:rows + (p + 1) * cols]
                )
                value = jnp.sum(jnp.where(sel, acc, 0.0), axis=0, keepdims=True)
                column = column + weights[p:p + 1] * value
            out_ref[:, pl.ds(off, CHUNK)] = column

        chunks(total, body)

    return pl.pallas_call(
        kernel,
        out_shape=jax.ShapeDtypeStruct((1, total), jnp.float32),
        scratch_shapes=[pltpu.VMEM((2 * rows, HI), jnp.bfloat16)],
    )(table, ids, held)


def source_scatter(values, scales, ids, width, with_norm=False):
    n, total = values.shape
    cols = width // HI
    rows = n * cols
    count = len(scales)

    def kernel(val_ref, *refs):
        scale_refs = refs[:count]
        ids_ref, out_ref = refs[count:count + 2]
        norm_ref = refs[count + 2:]
        out_ref[...] = jnp.zeros(out_ref.shape, jnp.float32)

        def body(off):
            idc = ids_ref[:, pl.ds(off, CHUNK)]
            scale = scale_refs[0][:, pl.ds(off, CHUNK)]
            for other in scale_refs[1:]:
                scale = scale * other[:, pl.ds(off, CHUNK)]
            v = val_ref[:, pl.ds(off, CHUNK)] * scale
            sel = group_mask(idc, cols, CHUNK, cols)
            parts = []
            for piece in pieces(v):
                for p in range(n):
                    parts.append(jnp.where(sel, piece[p:p + 1, :], jnp.zeros((), jnp.bfloat16)))
            spread = jnp.concatenate(parts, axis=0)
            res = lax.dot_general(
                spread, hot_rows(idc, CHUNK), (((1,), (1,)), ((), ())),
                preferred_element_type=jnp.float32,
            )
            out_ref[...] += res[:rows] + res[rows:]

        chunks(total, body)
        if with_norm:
            grad = out_ref[...]
            norm_ref[0][...] = jnp.sum(jnp.sum(grad * grad, axis=0, keepdims=True), axis=1, keepdims=True)

    shape = jax.ShapeDtypeStruct((rows, HI), jnp.float32)
    if not with_norm:
        return pl.pallas_call(kernel, out_shape=shape)(values, *scales, ids)
    grad, norm = pl.pallas_call(
        kernel, out_shape=(shape, jax.ShapeDtypeStruct((1, 1), jnp.float32))
    )(values, *scales, ids)
    return grad, norm.reshape(())


def knot_gather(extended, first_ids, basis, zsrc, weight, extra, knots, parts, width):
    total = first_ids.shape[1]
    cols = knots // HI
    shifted = jnp.stack([extended[q:q + knots] for q in range(4)], axis=0)
    rows = 4 * cols
    per_chunk = CHUNK // width
    line = 128 + -(-width // 128) * 128

    def kernel(tab_ref, ids_ref, basis_ref, zsrc_ref, weight_ref, extra_ref, out_ref, pay_ref, big_ref, norm_ref):
        split_into(tab_ref, big_ref)
        norm_ref[...] = jnp.zeros(norm_ref.shape, jnp.float32)

        for i in range(total // CHUNK):
            off = i * CHUNK
            idc = ids_ref[:, pl.ds(off, CHUNK)]
            picked = jnp.dot(big_ref[...], hot_rows(idc, CHUNK), preferred_element_type=jnp.float32)
            acc = picked[:rows] + picked[rows:]
            sel = group_mask(idc, cols, CHUNK, cols)
            b = basis_ref[:, pl.ds(off, CHUNK)]
            z = jnp.zeros((1, CHUNK), jnp.float32)
            for q in range(4):
                value = jnp.sum(jnp.where(sel, acc[q * cols:(q + 1) * cols], 0.0), axis=0, keepdims=True)
                z = z + b[q:q + 1] * value
            shift = zsrc_ref[:, pl.ds(off, CHUNK)] + z
            out_ref[:, pl.ds(off, CHUNK)] = shift
            for r in range(per_chunk):
                start = (i * per_chunk + r) * line + 128
                pay_ref[:, start:start + width] = shift[:, r * width:(r + 1) * width]
            norm_ref[...] += jnp.sum(weight_ref[:, pl.ds(off, CHUNK)] * shift * shift, axis=1, keepdims=True)

        lane = lax.broadcasted_iota(jnp.int32, (1, 128), 1)
        sums = jnp.where(lane == 0, norm_ref[...], jnp.where(lane == 1, extra_ref[...], 0.0))
        for r in range(parts):
            pay_ref[:, r * line:r * line + 128] = sums
            if line > 128 + width:
                pay_ref[:, r * line + 128 + width:(r + 1) * line] = jnp.zeros((1, line - 128 - width), jnp.float32)

    return pl.pallas_call(
        kernel,
        out_shape=(
            jax.ShapeDtypeStruct((1, total), jnp.float32),
            jax.ShapeDtypeStruct((1, parts * line), jnp.float32),
        ),
        scratch_shapes=[pltpu.VMEM((2 * rows, HI), jnp.bfloat16), pltpu.VMEM((1, 1), jnp.float32)],
    )(shifted.reshape(rows, HI), first_ids, basis, zsrc, weight, extra.reshape(1, 1))


def knot_scatter(values, first_ids, basis16, knots, step=None):
    total = first_ids.shape[1]
    cols = knots // HI
    rows = 4 * cols
    extras = [] if step is None else [step[0].reshape(1, 1), step[1], step[2]]

    def kernel(val_ref, ids_ref, basis_ref, *refs):
        out_ref = refs[-1]
        out_ref[...] = jnp.zeros(out_ref.shape, jnp.float32)

        def body(off):
            idc = ids_ref[:, pl.ds(off, CHUNK)]
            sel = group_mask(idc, rows, CHUNK, cols)
            z = val_ref[:, pl.ds(off, CHUNK)]
            if step is not None:
                alpha_ref, weight_ref, shift_ref = refs[:3]
                z = z - alpha_ref[...] * (weight_ref[:, pl.ds(off, CHUNK)] * shift_ref[:, pl.ds(off, CHUNK)])
            v = jnp.where(sel, basis_ref[:, pl.ds(off, CHUNK)] * z, 0.0)
            spread = jnp.concatenate(pieces(v), axis=0)
            res = lax.dot_general(
                spread, hot_rows(idc, CHUNK), (((1,), (1,)), ((), ())),
                preferred_element_type=jnp.float32,
            )
            out_ref[...] += res[:rows] + res[rows:]

        chunks(total, body)

    out = pl.pallas_call(
        kernel, out_shape=jax.ShapeDtypeStruct((rows, HI), jnp.float32)
    )(values, first_ids, basis16, *extras)
    per_shift = out.reshape(4, knots)
    grad = jnp.zeros((knots + 3,), jnp.float32)
    for q in range(4):
        grad = grad.at[q:q + knots].add(per_shift[q])
    return grad


def per_device(
    observed_residual,
    source_partials,
    spread_derivative_table,
    detector_index,
    first_knot_interval,
    interval_fraction,
    live_slot_count,
    slot_owned_source,
):
    rows = observed_residual.shape[1]
    n_time = lax.axis_size("tm")
    n_share = lax.axis_size("src")
    n_ranks = n_time * n_share
    capacity = rows // n_ranks
    n_params = source_partials.shape[0]
    detector_count = spread_derivative_table.shape[1]
    knots = KN
    n_knots = n_time * knots
    owned = SRC_DEV
    everyone = ("tm", "src")
    place = jnp.arange(capacity, dtype=jnp.int32)[None, :]
    live = (place < live_slot_count[0][:, None]).astype(jnp.float32).reshape(1, rows)
    indicator = (
        detector_index[None, :] == jnp.arange(detector_count, dtype=jnp.int32)[:, None]
    ).astype(jnp.float32)
    weight_factor = jnp.dot(
        spread_derivative_table,
        indicator,
        precision=lax.Precision.HIGHEST,
        preferred_element_type=jnp.float32,
    )
    weight_sq = live * jnp.sum(weight_factor * weight_factor, axis=0, keepdims=True)
    basis16 = jnp.repeat(jnp.stack(spline_basis(interval_fraction), axis=0), knots // HI, axis=0)
    first_ids = first_knot_interval.reshape(1, rows)
    ids = slot_owned_source[0].reshape(1, rows)
    zbar0 = live * jnp.sum(weight_factor * observed_residual, axis=0, keepdims=True)

    packed = jnp.concatenate(
        [
            source_partials,
            zbar0,
            weight_sq,
            interval_fraction[None],
            first_knot_interval.astype(jnp.float32)[None],
        ],
        axis=0,
    )
    n_rows = packed.shape[0]
    blocks = packed.reshape(n_rows, n_ranks, capacity).transpose(1, 0, 2).reshape(n_ranks, n_rows * capacity)
    got = lax.all_to_all(blocks, everyone, 0, 0, tiled=True)
    got = got.reshape(n_ranks, n_rows, capacity).transpose(1, 0, 2).reshape(n_rows, rows)
    held = got[:n_params]
    zbar0_own = got[n_params:n_params + 1]
    weight_sq_own = got[n_params + 1:n_params + 2]
    basis_own = jnp.concatenate(spline_basis(got[n_params + 2:n_params + 3]), axis=0)
    slot_device = jnp.arange(rows, dtype=jnp.int32)[None, :] // capacity
    base_own = (slot_device // n_share) * knots + got[n_params + 3:n_params + 4].astype(jnp.int32)
    table_rows = n_params * (owned // HI)

    def outgoing(part_a, s_norm):
        mine = jnp.concatenate([part_a, s_norm[None]])
        return jnp.broadcast_to(mine[None, :], (n_ranks, knots + 4))

    def combine(sent):
        every = lax.all_to_all(sent, everyone, 0, 0, tiled=True)
        block = jnp.sum(every[:, :knots + 3].reshape(n_time, n_share, knots + 3), axis=1)
        main = block[:, :knots].at[1:, :3].add(block[:-1, knots:])
        grad_a = main.reshape(n_knots)
        norm = jnp.sum(every[:, knots + 3]) + jnp.sum(grad_a * grad_a)
        return grad_a, norm

    def forward(zsrc, dir_a, extra):
        extended = jnp.concatenate([dir_a, jnp.zeros((3,), jnp.float32)])
        shift_own, payload = knot_gather(
            extended, base_own, basis_own, zsrc, weight_sq_own, extra, n_knots, n_ranks, capacity
        )
        back = lax.all_to_all(payload.reshape(n_ranks, -1), everyone, 0, 0, tiled=True)
        totals = jnp.sum(back[:, :2], axis=0)
        return shift_own, back[:, 128:128 + capacity].reshape(1, rows) * live, totals[0], totals[1]

    sol_s = jnp.zeros((n_params, owned), jnp.float32)
    sol_a = jnp.zeros((n_knots,), jnp.float32)
    resid = observed_residual
    zbar_slot = zbar0
    sent = outgoing(knot_scatter(zbar_slot, first_ids, basis16, knots), jnp.zeros((), jnp.float32))
    sent, held, zbar0_own = lax.optimization_barrier((sent, held, zbar0_own))
    grad_a, gamma_a = combine(sent)
    grad_s, extra = source_scatter(held, [zbar0_own], ids, owned, with_norm=True)
    dir_s, dir_a = (grad_s, grad_a)
    pulled = source_gather(dir_s, ids, held)
    for step in range(ITERS):
        shift_own, shift_slot, image_sq, extra_sum = forward(pulled, dir_a, extra)
        if step == 0:
            gamma = extra_sum + gamma_a
        alpha = gamma / image_sq
        sol_s = sol_s + alpha * dir_s.reshape(n_params, owned)
        sol_a = sol_a + alpha * dir_a
        resid = resid - alpha * (weight_factor * shift_slot)
        if step + 1 < ITERS:
            pushed = source_scatter(held, [weight_sq_own, shift_own], ids, owned)
            step_slot = (alpha, weight_sq, shift_slot)
            zbar_next = zbar_slot - alpha * (weight_sq * shift_slot)
            grad_s = grad_s - alpha * pushed
            grad_a, fresh = combine(
                outgoing(
                    knot_scatter(zbar_slot, first_ids, basis16, knots, step_slot), jnp.sum(grad_s * grad_s)
                )
            )
            raw = source_gather(grad_s, ids, held)
            beta = fresh / gamma
            dir_s = grad_s + beta * dir_s
            dir_a = grad_a + beta * dir_a
            pulled = raw + beta * pulled
            gamma = fresh
            zbar_slot = zbar_next
            extra = jnp.zeros((), jnp.float32)
    mine_a = lax.dynamic_slice(sol_a, (lax.axis_index("tm") * knots,), (knots,))
    return (sol_s, mine_a, resid)


def solution(mesh):
    placed = (
        P(None, ("tm", "src")),
        P(None, ("tm", "src")),
        P(),
        P(("tm", "src")),
        P(("tm", "src")),
        P(("tm", "src")),
        P(("tm", "src"), None),
        P(("tm", "src"), None),
    )
    return jax.shard_map(
        per_device,
        mesh=mesh,
        in_specs=placed,
        out_specs=(P(None, ("tm", "src")), P("tm"), P(None, ("tm", "src"))),
        check_vma=False,
    )
```

```python
import jax
import jax.numpy as jnp
from jax import lax
from jax.experimental import pallas as pl
from jax.experimental.pallas import tpu as pltpu
from jax.sharding import PartitionSpec as P

SRC_DEV = 32768
KN = 1024
ITERS = 2
HI = 256
CHUNK = 4096


def passed_along(block, axis, distance):
    devices = range(lax.axis_size(axis))
    route = [(i - distance, i) for i in devices if i - distance in devices]
    return lax.ppermute(block, axis, route)


def spline_basis(frac):
    u2 = frac * frac
    u3 = u2 * frac
    one = 1.0 - frac
    return [
        one * one * one / 6.0,
        (3.0 * u3 - 6.0 * u2 + 4.0) / 6.0,
        (-3.0 * u3 + 3.0 * u2 + 3.0 * frac + 1.0) / 6.0,
        u3 / 6.0,
    ]


def pieces(x):
    h = x.astype(jnp.bfloat16)
    m = (x - h.astype(jnp.float32)).astype(jnp.bfloat16)
    return h, m


def hot_rows(ids, width):
    low = jnp.bitwise_and(ids, HI - 1)
    return (lax.broadcasted_iota(jnp.int32, (HI, width), 0) == low).astype(jnp.bfloat16)


def group_mask(ids, rows, width, groups):
    high = lax.shift_right_logical(ids, 8)
    iota = lax.broadcasted_iota(jnp.int32, (rows, width), 0)
    return (iota % groups) == high


def chunks(total, body):
    def step(i, carry):
        body(pl.multiple_of(i * CHUNK, CHUNK))
        return carry

    lax.fori_loop(0, total // CHUNK, step, 0)


def split_into(src_ref, big_ref):
    rows = src_ref.shape[0]
    for k, part in enumerate(pieces(src_ref[...])):
        big_ref[k * rows:(k + 1) * rows, :] = part


def source_gather(table, ids, held):
    n, total = held.shape
    rows = table.shape[0]
    cols = rows // n

    def kernel(tab_ref, ids_ref, held_ref, out_ref, big_ref):
        split_into(tab_ref, big_ref)

        def body(off):
            idc = ids_ref[:, pl.ds(off, CHUNK)]
            picked = jnp.dot(big_ref[...], hot_rows(idc, CHUNK), preferred_element_type=jnp.float32)
            sel = group_mask(idc, cols, CHUNK, cols)
            weights = held_ref[:, pl.ds(off, CHUNK)]
            column = jnp.zeros((1, CHUNK), jnp.float32)
            for p in range(n):
                acc = (
                    picked[p * cols:(p + 1) * cols]
                    + picked[rows + p * cols:rows + (p + 1) * cols]
                )
                value = jnp.sum(jnp.where(sel, acc, 0.0), axis=0, keepdims=True)
                column = column + weights[p:p + 1] * value
            out_ref[:, pl.ds(off, CHUNK)] = column

        chunks(total, body)

    return pl.pallas_call(
        kernel,
        out_shape=jax.ShapeDtypeStruct((1, total), jnp.float32),
        scratch_shapes=[pltpu.VMEM((2 * rows, HI), jnp.bfloat16)],
    )(table, ids, held)


def source_scatter(values, scales, ids, width, with_norm=False):
    n, total = values.shape
    cols = width // HI
    rows = n * cols
    count = len(scales)

    def kernel(val_ref, *refs):
        scale_refs = refs[:count]
        ids_ref, out_ref = refs[count:count + 2]
        norm_ref = refs[count + 2:]
        out_ref[...] = jnp.zeros(out_ref.shape, jnp.float32)

        def body(off):
            idc = ids_ref[:, pl.ds(off, CHUNK)]
            scale = scale_refs[0][:, pl.ds(off, CHUNK)]
            for other in scale_refs[1:]:
                scale = scale * other[:, pl.ds(off, CHUNK)]
            v = val_ref[:, pl.ds(off, CHUNK)] * scale
            sel = group_mask(idc, cols, CHUNK, cols)
            parts = []
            for piece in pieces(v):
                for p in range(n):
                    parts.append(jnp.where(sel, piece[p:p + 1, :], jnp.zeros((), jnp.bfloat16)))
            spread = jnp.concatenate(parts, axis=0)
            res = lax.dot_general(
                spread, hot_rows(idc, CHUNK), (((1,), (1,)), ((), ())),
                preferred_element_type=jnp.float32,
            )
            out_ref[...] += res[:rows] + res[rows:]

        chunks(total, body)
        if with_norm:
            grad = out_ref[...]
            norm_ref[0][...] = jnp.sum(jnp.sum(grad * grad, axis=0, keepdims=True), axis=1, keepdims=True)

    shape = jax.ShapeDtypeStruct((rows, HI), jnp.float32)
    if not with_norm:
        return pl.pallas_call(kernel, out_shape=shape)(values, *scales, ids)
    grad, norm = pl.pallas_call(
        kernel, out_shape=(shape, jax.ShapeDtypeStruct((1, 1), jnp.float32))
    )(values, *scales, ids)
    return grad, norm.reshape(())


def knot_gather(extended, first_ids, basis, zsrc, weight, extra, knots, parts, width, carry=None):
    total = first_ids.shape[1]
    cols = knots // HI
    shifted = jnp.stack([extended[q:q + knots] for q in range(4)], axis=0)
    rows = 4 * cols
    per_chunk = CHUNK // width
    line = 128 + -(-width // 128) * 128

    extras = [] if carry is None else [carry[0].reshape(1, 1), carry[1]]

    def kernel(tab_ref, ids_ref, basis_ref, zsrc_ref, weight_ref, extra_ref, *refs):
        out_ref, pay_ref, big_ref, norm_ref = refs[-4:]
        split_into(tab_ref, big_ref)
        norm_ref[...] = jnp.zeros(norm_ref.shape, jnp.float32)

        for i in range(total // CHUNK):
            off = i * CHUNK
            idc = ids_ref[:, pl.ds(off, CHUNK)]
            picked = jnp.dot(big_ref[...], hot_rows(idc, CHUNK), preferred_element_type=jnp.float32)
            acc = picked[:rows] + picked[rows:]
            sel = group_mask(idc, cols, CHUNK, cols)
            b = basis_ref[:, pl.ds(off, CHUNK)]
            z = jnp.zeros((1, CHUNK), jnp.float32)
            for q in range(4):
                value = jnp.sum(jnp.where(sel, acc[q * cols:(q + 1) * cols], 0.0), axis=0, keepdims=True)
                z = z + b[q:q + 1] * value
            shift = zsrc_ref[:, pl.ds(off, CHUNK)] + z
            if carry is not None:
                shift = shift + refs[0][...] * refs[1][:, pl.ds(off, CHUNK)]
            out_ref[:, pl.ds(off, CHUNK)] = shift
            for r in range(per_chunk):
                start = (i * per_chunk + r) * line + 128
                pay_ref[:, start:start + width] = shift[:, r * width:(r + 1) * width]
            norm_ref[...] += jnp.sum(weight_ref[:, pl.ds(off, CHUNK)] * shift * shift, axis=1, keepdims=True)

        lane = lax.broadcasted_iota(jnp.int32, (1, 128), 1)
        sums = jnp.where(lane == 0, norm_ref[...], jnp.where(lane == 1, extra_ref[...], 0.0))
        for r in range(parts):
            pay_ref[:, r * line:r * line + 128] = sums
            if line > 128 + width:
                pay_ref[:, r * line + 128 + width:(r + 1) * line] = jnp.zeros((1, line - 128 - width), jnp.float32)

    return pl.pallas_call(
        kernel,
        out_shape=(
            jax.ShapeDtypeStruct((1, total), jnp.float32),
            jax.ShapeDtypeStruct((1, parts * line), jnp.float32),
        ),
        scratch_shapes=[pltpu.VMEM((2 * rows, HI), jnp.bfloat16), pltpu.VMEM((1, 1), jnp.float32)],
    )(shifted.reshape(rows, HI), first_ids, basis, zsrc, weight, extra.reshape(1, 1), *extras)


def knot_scatter(values, first_ids, basis16, knots):
    total = first_ids.shape[1]
    cols = knots // HI
    rows = 4 * cols

    def kernel(val_ref, ids_ref, basis_ref, out_ref):
        out_ref[...] = jnp.zeros(out_ref.shape, jnp.float32)

        def body(off):
            idc = ids_ref[:, pl.ds(off, CHUNK)]
            sel = group_mask(idc, rows, CHUNK, cols)
            v = jnp.where(sel, basis_ref[:, pl.ds(off, CHUNK)] * val_ref[:, pl.ds(off, CHUNK)], 0.0)
            spread = jnp.concatenate(pieces(v), axis=0)
            res = lax.dot_general(
                spread, hot_rows(idc, CHUNK), (((1,), (1,)), ((), ())),
                preferred_element_type=jnp.float32,
            )
            out_ref[...] += res[:rows] + res[rows:]

        chunks(total, body)

    out = pl.pallas_call(
        kernel, out_shape=jax.ShapeDtypeStruct((rows, HI), jnp.float32)
    )(values, first_ids, basis16)
    per_shift = out.reshape(4, knots)
    grad = jnp.zeros((knots + 3,), jnp.float32)
    for q in range(4):
        grad = grad.at[q:q + knots].add(per_shift[q])
    return grad


def per_device(
    observed_residual,
    source_partials,
    spread_derivative_table,
    detector_index,
    first_knot_interval,
    interval_fraction,
    live_slot_count,
    slot_owned_source,
):
    rows = observed_residual.shape[1]
    n_time = lax.axis_size("tm")
    n_share = lax.axis_size("src")
    n_ranks = n_time * n_share
    capacity = rows // n_ranks
    n_params = source_partials.shape[0]
    detector_count = spread_derivative_table.shape[1]
    knots = KN
    n_knots = n_time * knots
    owned = SRC_DEV
    everyone = ("tm", "src")
    place = jnp.arange(capacity, dtype=jnp.int32)[None, :]
    live = (place < live_slot_count[0][:, None]).astype(jnp.float32).reshape(1, rows)
    indicator = (
        detector_index[None, :] == jnp.arange(detector_count, dtype=jnp.int32)[:, None]
    ).astype(jnp.float32)
    weight_factor = jnp.dot(
        spread_derivative_table,
        indicator,
        precision=lax.Precision.HIGHEST,
        preferred_element_type=jnp.float32,
    )
    weight_sq = live * jnp.sum(weight_factor * weight_factor, axis=0, keepdims=True)
    basis16 = jnp.repeat(jnp.stack(spline_basis(interval_fraction), axis=0), knots // HI, axis=0)
    first_ids = first_knot_interval.reshape(1, rows)
    ids = slot_owned_source[0].reshape(1, rows)
    zbar0 = live * jnp.sum(weight_factor * observed_residual, axis=0, keepdims=True)

    packed = jnp.concatenate(
        [
            source_partials,
            zbar0,
            weight_sq,
            interval_fraction[None],
            first_knot_interval.astype(jnp.float32)[None],
        ],
        axis=0,
    )
    n_rows = packed.shape[0]
    blocks = packed.reshape(n_rows, n_ranks, capacity).transpose(1, 0, 2).reshape(n_ranks, n_rows * capacity)
    got = lax.all_to_all(blocks, everyone, 0, 0, tiled=True)
    got = got.reshape(n_ranks, n_rows, capacity).transpose(1, 0, 2).reshape(n_rows, rows)
    held = got[:n_params]
    zbar0_own = got[n_params:n_params + 1]
    weight_sq_own = got[n_params + 1:n_params + 2]
    basis_own = jnp.concatenate(spline_basis(got[n_params + 2:n_params + 3]), axis=0)
    slot_device = jnp.arange(rows, dtype=jnp.int32)[None, :] // capacity
    base_own = (slot_device // n_share) * knots + got[n_params + 3:n_params + 4].astype(jnp.int32)
    table_rows = n_params * (owned // HI)

    def outgoing(part_a, s_norm):
        mine = jnp.concatenate([part_a, s_norm[None]])
        return jnp.broadcast_to(mine[None, :], (n_ranks, knots + 4))

    def combine(sent):
        every = lax.all_to_all(sent, everyone, 0, 0, tiled=True)
        block = jnp.sum(every[:, :knots + 3].reshape(n_time, n_share, knots + 3), axis=1)
        main = block[:, :knots].at[1:, :3].add(block[:-1, knots:])
        grad_a = main.reshape(n_knots)
        norm = jnp.sum(every[:, knots + 3]) + jnp.sum(grad_a * grad_a)
        return grad_a, norm

    def forward(zsrc, dir_a, extra, carry=None):
        extended = jnp.concatenate([dir_a, jnp.zeros((3,), jnp.float32)])
        shift_own, payload = knot_gather(
            extended, base_own, basis_own, zsrc, weight_sq_own, extra, n_knots, n_ranks, capacity, carry
        )
        back = lax.all_to_all(payload.reshape(n_ranks, -1), everyone, 0, 0, tiled=True)
        totals = jnp.sum(back[:, :2], axis=0)
        return shift_own, back[:, 128:128 + capacity].reshape(1, rows) * live, totals[0], totals[1]

    sol_s = jnp.zeros((n_params, owned), jnp.float32)
    sol_a = jnp.zeros((n_knots,), jnp.float32)
    resid = observed_residual
    zbar_slot = zbar0
    sent = outgoing(knot_scatter(zbar_slot, first_ids, basis16, knots), jnp.zeros((), jnp.float32))
    sent, held, zbar0_own = lax.optimization_barrier((sent, held, zbar0_own))
    grad_a, gamma_a = combine(sent)
    grad_s, extra = source_scatter(held, [zbar0_own], ids, owned, with_norm=True)
    dir_s, dir_a = (grad_s, grad_a)
    zsrc, att, carry = source_gather(dir_s, ids, held), dir_a, None
    for step in range(ITERS):
        shift_own, shift_slot, image_sq, extra_sum = forward(zsrc, att, extra, carry)
        if step == 0:
            gamma = extra_sum + gamma_a
        alpha = gamma / image_sq
        sol_s = sol_s + alpha * dir_s.reshape(n_params, owned)
        sol_a = sol_a + alpha * dir_a
        resid = resid - alpha * (weight_factor * shift_slot)
        if step + 1 < ITERS:
            pushed = source_scatter(held, [weight_sq_own, shift_own], ids, owned)
            zbar_slot = zbar_slot - alpha * (weight_sq * shift_slot)
            grad_s = grad_s - alpha * pushed
            grad_a, fresh = combine(
                outgoing(knot_scatter(zbar_slot, first_ids, basis16, knots), jnp.sum(grad_s * grad_s))
            )
            zsrc, att = source_gather(grad_s, ids, held), grad_a
            beta = fresh / gamma
            carry = (beta, shift_own)
            dir_s = grad_s + beta * dir_s
            dir_a = grad_a + beta * dir_a
            gamma = fresh
            extra = jnp.zeros((), jnp.float32)
    mine_a = lax.dynamic_slice(sol_a, (lax.axis_index("tm") * knots,), (knots,))
    return (sol_s, mine_a, resid)


def solution(mesh):
    placed = (
        P(None, ("tm", "src")),
        P(None, ("tm", "src")),
        P(),
        P(("tm", "src")),
        P(("tm", "src")),
        P(("tm", "src")),
        P(("tm", "src"), None),
        P(("tm", "src"), None),
    )
    return jax.shard_map(
        per_device,
        mesh=mesh,
        in_specs=placed,
        out_specs=(P(None, ("tm", "src")), P("tm"), P(None, ("tm", "src"))),
        check_vma=False,
    )
```

```python
import jax
import jax.numpy as jnp
from jax import lax
from jax.experimental import pallas as pl
from jax.experimental.pallas import tpu as pltpu
from jax.sharding import PartitionSpec as P

SRC_DEV = 32768
KN = 1024
ITERS = 2
HI = 256
CHUNK = 4096


def passed_along(block, axis, distance):
    devices = range(lax.axis_size(axis))
    route = [(i - distance, i) for i in devices if i - distance in devices]
    return lax.ppermute(block, axis, route)


def spline_basis(frac):
    u2 = frac * frac
    u3 = u2 * frac
    one = 1.0 - frac
    return [
        one * one * one / 6.0,
        (3.0 * u3 - 6.0 * u2 + 4.0) / 6.0,
        (-3.0 * u3 + 3.0 * u2 + 3.0 * frac + 1.0) / 6.0,
        u3 / 6.0,
    ]


def pieces(x):
    h = x.astype(jnp.bfloat16)
    m = (x - h.astype(jnp.float32)).astype(jnp.bfloat16)
    return h, m


def hot_rows(ids, width):
    low = jnp.bitwise_and(ids, HI - 1)
    return (lax.broadcasted_iota(jnp.int32, (HI, width), 0) == low).astype(jnp.bfloat16)


def group_mask(ids, rows, width, groups):
    high = lax.shift_right_logical(ids, 8)
    iota = lax.broadcasted_iota(jnp.int32, (rows, width), 0)
    return (iota % groups) == high


def chunks(total, body):
    def step(i, carry):
        body(pl.multiple_of(i * CHUNK, CHUNK))
        return carry

    lax.fori_loop(0, total // CHUNK, step, 0)


def split_into(src_ref, big_ref):
    rows = src_ref.shape[0]
    for k, part in enumerate(pieces(src_ref[...])):
        big_ref[k * rows:(k + 1) * rows, :] = part


def source_gather(table, ids, held):
    n, total = held.shape
    rows = table.shape[0]
    cols = rows // n

    def kernel(tab_ref, ids_ref, held_ref, out_ref, big_ref):
        split_into(tab_ref, big_ref)

        def body(off):
            idc = ids_ref[:, pl.ds(off, CHUNK)]
            picked = jnp.dot(big_ref[...], hot_rows(idc, CHUNK), preferred_element_type=jnp.float32)
            sel = group_mask(idc, cols, CHUNK, cols)
            weights = held_ref[:, pl.ds(off, CHUNK)]
            column = jnp.zeros((1, CHUNK), jnp.float32)
            for p in range(n):
                acc = (
                    picked[p * cols:(p + 1) * cols]
                    + picked[rows + p * cols:rows + (p + 1) * cols]
                )
                value = jnp.sum(jnp.where(sel, acc, 0.0), axis=0, keepdims=True)
                column = column + weights[p:p + 1] * value
            out_ref[:, pl.ds(off, CHUNK)] = column

        chunks(total, body)

    return pl.pallas_call(
        kernel,
        out_shape=jax.ShapeDtypeStruct((1, total), jnp.float32),
        scratch_shapes=[pltpu.VMEM((2 * rows, HI), jnp.bfloat16)],
    )(table, ids, held)


def source_scatter(values, scales, ids, width, with_norm=False):
    n, total = values.shape
    cols = width // HI
    rows = n * cols
    count = len(scales)

    def kernel(val_ref, *refs):
        scale_refs = refs[:count]
        ids_ref, out_ref = refs[count:count + 2]
        norm_ref = refs[count + 2:]
        out_ref[...] = jnp.zeros(out_ref.shape, jnp.float32)

        def body(off):
            idc = ids_ref[:, pl.ds(off, CHUNK)]
            scale = scale_refs[0][:, pl.ds(off, CHUNK)]
            for other in scale_refs[1:]:
                scale = scale * other[:, pl.ds(off, CHUNK)]
            v = val_ref[:, pl.ds(off, CHUNK)] * scale
            sel = group_mask(idc, cols, CHUNK, cols)
            parts = []
            for piece in pieces(v):
                for p in range(n):
                    parts.append(jnp.where(sel, piece[p:p + 1, :], jnp.zeros((), jnp.bfloat16)))
            spread = jnp.concatenate(parts, axis=0)
            res = lax.dot_general(
                spread, hot_rows(idc, CHUNK), (((1,), (1,)), ((), ())),
                preferred_element_type=jnp.float32,
            )
            out_ref[...] += res[:rows] + res[rows:]

        chunks(total, body)
        if with_norm:
            grad = out_ref[...]
            norm_ref[0][...] = jnp.sum(jnp.sum(grad * grad, axis=0, keepdims=True), axis=1, keepdims=True)

    shape = jax.ShapeDtypeStruct((rows, HI), jnp.float32)
    if not with_norm:
        return pl.pallas_call(kernel, out_shape=shape)(values, *scales, ids)
    grad, norm = pl.pallas_call(
        kernel, out_shape=(shape, jax.ShapeDtypeStruct((1, 1), jnp.float32))
    )(values, *scales, ids)
    return grad, norm.reshape(())


def knot_gather(extended, first_ids, basis, zsrc, weight, extra, knots, parts, width):
    total = first_ids.shape[1]
    cols = knots // HI
    shifted = jnp.stack([extended[q:q + knots] for q in range(4)], axis=0)
    rows = 4 * cols
    per_chunk = CHUNK // width
    line = 128 + -(-width // 128) * 128

    def kernel(tab_ref, ids_ref, basis_ref, zsrc_ref, weight_ref, extra_ref, out_ref, pay_ref, big_ref, norm_ref):
        split_into(tab_ref, big_ref)
        norm_ref[...] = jnp.zeros(norm_ref.shape, jnp.float32)

        for i in range(total // CHUNK):
            off = i * CHUNK
            idc = ids_ref[:, pl.ds(off, CHUNK)]
            picked = jnp.dot(big_ref[...], hot_rows(idc, CHUNK), preferred_element_type=jnp.float32)
            acc = picked[:rows] + picked[rows:]
            sel = group_mask(idc, cols, CHUNK, cols)
            b = basis_ref[:, pl.ds(off, CHUNK)]
            z = jnp.zeros((1, CHUNK), jnp.float32)
            for q in range(4):
                value = jnp.sum(jnp.where(sel, acc[q * cols:(q + 1) * cols], 0.0), axis=0, keepdims=True)
                z = z + b[q:q + 1] * value
            shift = zsrc_ref[:, pl.ds(off, CHUNK)] + z
            out_ref[:, pl.ds(off, CHUNK)] = shift
            for r in range(per_chunk):
                start = (i * per_chunk + r) * line + 128
                pay_ref[:, start:start + width] = shift[:, r * width:(r + 1) * width]
            norm_ref[...] += jnp.sum(weight_ref[:, pl.ds(off, CHUNK)] * shift * shift, axis=1, keepdims=True)

        lane = lax.broadcasted_iota(jnp.int32, (1, 128), 1)
        sums = jnp.where(lane == 0, norm_ref[...], jnp.where(lane == 1, extra_ref[...], 0.0))
        for r in range(parts):
            pay_ref[:, r * line:r * line + 128] = sums
            if line > 128 + width:
                pay_ref[:, r * line + 128 + width:(r + 1) * line] = jnp.zeros((1, line - 128 - width), jnp.float32)

    return pl.pallas_call(
        kernel,
        out_shape=(
            jax.ShapeDtypeStruct((1, total), jnp.float32),
            jax.ShapeDtypeStruct((1, parts * line), jnp.float32),
        ),
        scratch_shapes=[pltpu.VMEM((2 * rows, HI), jnp.bfloat16), pltpu.VMEM((1, 1), jnp.float32)],
    )(shifted.reshape(rows, HI), first_ids, basis, zsrc, weight, extra.reshape(1, 1))


def knot_scatter(values, first_ids, basis16, s_norm, knots, parts):
    total = first_ids.shape[1]
    cols = knots // HI
    rows = 4 * cols
    line = 128 + (cols + 1) * HI

    def kernel(val_ref, ids_ref, basis_ref, norm_ref, pay_ref, acc_ref):
        acc_ref[...] = jnp.zeros(acc_ref.shape, jnp.float32)

        def body(off):
            idc = ids_ref[:, pl.ds(off, CHUNK)]
            sel = group_mask(idc, rows, CHUNK, cols)
            v = jnp.where(sel, basis_ref[:, pl.ds(off, CHUNK)] * val_ref[:, pl.ds(off, CHUNK)], 0.0)
            spread = jnp.concatenate(pieces(v), axis=0)
            res = lax.dot_general(
                spread, hot_rows(idc, CHUNK), (((1,), (1,)), ((), ())),
                preferred_element_type=jnp.float32,
            )
            acc_ref[...] += res[:rows] + res[rows:]

        chunks(total, body)
        lane = lax.broadcasted_iota(jnp.int32, (cols, HI), 1)
        same = acc_ref[0:cols, :]
        carried = jnp.zeros((cols, HI), jnp.float32)
        for q in range(1, 4):
            moved = pltpu.roll(acc_ref[q * cols:(q + 1) * cols, :], q, 1)
            same = same + jnp.where(lane >= q, moved, 0.0)
            carried = carried + jnp.where(lane < q, moved, 0.0)
        blank = jnp.zeros((1, HI), jnp.float32)
        grid = jnp.concatenate([same, blank], axis=0) + jnp.concatenate([blank, carried], axis=0)
        head = jnp.where(lax.broadcasted_iota(jnp.int32, (1, 128), 1) == 0, norm_ref[...], 0.0)
        row = jnp.concatenate([head] + [grid[c:c + 1, :] for c in range(cols + 1)], axis=1)
        for r in range(parts):
            pay_ref[:, r * line:(r + 1) * line] = row

    return pl.pallas_call(
        kernel,
        out_shape=jax.ShapeDtypeStruct((1, parts * line), jnp.float32),
        scratch_shapes=[pltpu.VMEM((rows, HI), jnp.float32)],
    )(values, first_ids, basis16, s_norm.reshape(1, 1)).reshape(parts, line)


def per_device(
    observed_residual,
    source_partials,
    spread_derivative_table,
    detector_index,
    first_knot_interval,
    interval_fraction,
    live_slot_count,
    slot_owned_source,
):
    rows = observed_residual.shape[1]
    n_time = lax.axis_size("tm")
    n_share = lax.axis_size("src")
    n_ranks = n_time * n_share
    capacity = rows // n_ranks
    n_params = source_partials.shape[0]
    detector_count = spread_derivative_table.shape[1]
    knots = KN
    n_knots = n_time * knots
    owned = SRC_DEV
    everyone = ("tm", "src")
    place = jnp.arange(capacity, dtype=jnp.int32)[None, :]
    live = (place < live_slot_count[0][:, None]).astype(jnp.float32).reshape(1, rows)
    indicator = (
        detector_index[None, :] == jnp.arange(detector_count, dtype=jnp.int32)[:, None]
    ).astype(jnp.float32)
    weight_factor = jnp.dot(
        spread_derivative_table,
        indicator,
        precision=lax.Precision.HIGHEST,
        preferred_element_type=jnp.float32,
    )
    weight_sq = live * jnp.sum(weight_factor * weight_factor, axis=0, keepdims=True)
    basis16 = jnp.repeat(jnp.stack(spline_basis(interval_fraction), axis=0), knots // HI, axis=0)
    first_ids = first_knot_interval.reshape(1, rows)
    ids = slot_owned_source[0].reshape(1, rows)
    zbar0 = live * jnp.sum(weight_factor * observed_residual, axis=0, keepdims=True)

    packed = jnp.concatenate(
        [
            source_partials,
            zbar0,
            weight_sq,
            interval_fraction[None],
            first_knot_interval.astype(jnp.float32)[None],
        ],
        axis=0,
    )
    n_rows = packed.shape[0]
    blocks = packed.reshape(n_rows, n_ranks, capacity).transpose(1, 0, 2).reshape(n_ranks, n_rows * capacity)
    got = lax.all_to_all(blocks, everyone, 0, 0, tiled=True)
    got = got.reshape(n_ranks, n_rows, capacity).transpose(1, 0, 2).reshape(n_rows, rows)
    held = got[:n_params]
    zbar0_own = got[n_params:n_params + 1]
    weight_sq_own = got[n_params + 1:n_params + 2]
    basis_own = jnp.concatenate(spline_basis(got[n_params + 2:n_params + 3]), axis=0)
    slot_device = jnp.arange(rows, dtype=jnp.int32)[None, :] // capacity
    base_own = (slot_device // n_share) * knots + got[n_params + 3:n_params + 4].astype(jnp.int32)
    table_rows = n_params * (owned // HI)

    def combine(sent):
        every = lax.all_to_all(sent, everyone, 0, 0, tiled=True)
        block = jnp.sum(every[:, 128:128 + knots + 3].reshape(n_time, n_share, knots + 3), axis=1)
        main = block[:, :knots].at[1:, :3].add(block[:-1, knots:])
        grad_a = main.reshape(n_knots)
        norm = jnp.sum(every[:, 0]) + jnp.sum(grad_a * grad_a)
        return grad_a, norm

    def forward(zsrc, dir_a, extra):
        extended = jnp.concatenate([dir_a, jnp.zeros((3,), jnp.float32)])
        shift_own, payload = knot_gather(
            extended, base_own, basis_own, zsrc, weight_sq_own, extra, n_knots, n_ranks, capacity
        )
        back = lax.all_to_all(payload.reshape(n_ranks, -1), everyone, 0, 0, tiled=True)
        totals = jnp.sum(back[:, :2], axis=0)
        return shift_own, back[:, 128:128 + capacity].reshape(1, rows) * live, totals[0], totals[1]

    sol_s = jnp.zeros((n_params, owned), jnp.float32)
    sol_a = jnp.zeros((n_knots,), jnp.float32)
    resid = observed_residual
    zbar_slot = zbar0
    sent = knot_scatter(zbar_slot, first_ids, basis16, jnp.zeros((), jnp.float32), knots, n_ranks)
    sent, held, zbar0_own = lax.optimization_barrier((sent, held, zbar0_own))
    grad_a, gamma_a = combine(sent)
    grad_s, extra = source_scatter(held, [zbar0_own], ids, owned, with_norm=True)
    dir_s, dir_a = (grad_s, grad_a)
    pulled = source_gather(dir_s, ids, held)
    for step in range(ITERS):
        shift_own, shift_slot, image_sq, extra_sum = forward(pulled, dir_a, extra)
        if step == 0:
            gamma = extra_sum + gamma_a
        alpha = gamma / image_sq
        sol_s = sol_s + alpha * dir_s.reshape(n_params, owned)
        sol_a = sol_a + alpha * dir_a
        resid = resid - alpha * (weight_factor * shift_slot)
        if step + 1 < ITERS:
            pushed = source_scatter(held, [weight_sq_own, shift_own], ids, owned)
            zbar_slot = zbar_slot - alpha * (weight_sq * shift_slot)
            grad_s = grad_s - alpha * pushed
            grad_a, fresh = combine(
                knot_scatter(zbar_slot, first_ids, basis16, jnp.sum(grad_s * grad_s), knots, n_ranks)
            )
            raw = source_gather(grad_s, ids, held)
            beta = fresh / gamma
            dir_s = grad_s + beta * dir_s
            dir_a = grad_a + beta * dir_a
            pulled = raw + beta * pulled
            gamma = fresh
            extra = jnp.zeros((), jnp.float32)
    mine_a = lax.dynamic_slice(sol_a, (lax.axis_index("tm") * knots,), (knots,))
    return (sol_s, mine_a, resid)


def solution(mesh):
    placed = (
        P(None, ("tm", "src")),
        P(None, ("tm", "src")),
        P(),
        P(("tm", "src")),
        P(("tm", "src")),
        P(("tm", "src")),
        P(("tm", "src"), None),
        P(("tm", "src"), None),
    )
    return jax.shard_map(
        per_device,
        mesh=mesh,
        in_specs=placed,
        out_specs=(P(None, ("tm", "src")), P("tm"), P(None, ("tm", "src"))),
        check_vma=False,
    )
```

```python
import jax
import jax.numpy as jnp
from jax import lax
from jax.experimental import pallas as pl
from jax.experimental.pallas import tpu as pltpu
from jax.sharding import PartitionSpec as P

SRC_DEV = 32768
KN = 1024
ITERS = 2
HI = 256
CHUNK = 4096


def passed_along(block, axis, distance):
    devices = range(lax.axis_size(axis))
    route = [(i - distance, i) for i in devices if i - distance in devices]
    return lax.ppermute(block, axis, route)


def spline_basis(frac):
    u2 = frac * frac
    u3 = u2 * frac
    one = 1.0 - frac
    return [
        one * one * one / 6.0,
        (3.0 * u3 - 6.0 * u2 + 4.0) / 6.0,
        (-3.0 * u3 + 3.0 * u2 + 3.0 * frac + 1.0) / 6.0,
        u3 / 6.0,
    ]


def pieces(x):
    h = x.astype(jnp.bfloat16)
    m = (x - h.astype(jnp.float32)).astype(jnp.bfloat16)
    return h, m


def hot_rows(ids, width):
    low = jnp.bitwise_and(ids, HI - 1)
    return (lax.broadcasted_iota(jnp.int32, (HI, width), 0) == low).astype(jnp.bfloat16)


def group_mask(ids, rows, width, groups):
    high = lax.shift_right_logical(ids, 8)
    iota = lax.broadcasted_iota(jnp.int32, (rows, width), 0)
    return (iota % groups) == high


def chunks(total, body):
    def step(i, carry):
        body(pl.multiple_of(i * CHUNK, CHUNK))
        return carry

    lax.fori_loop(0, total // CHUNK, step, 0)


def split_into(src_ref, big_ref):
    rows = src_ref.shape[0]
    for k, part in enumerate(pieces(src_ref[...])):
        big_ref[k * rows:(k + 1) * rows, :] = part


def source_gather(table, ids, held):
    n, total = held.shape
    rows = table.shape[0]
    cols = rows // n

    def kernel(tab_ref, ids_ref, held_ref, out_ref, big_ref):
        split_into(tab_ref, big_ref)

        def body(off):
            idc = ids_ref[:, pl.ds(off, CHUNK)]
            picked = jnp.dot(big_ref[...], hot_rows(idc, CHUNK), preferred_element_type=jnp.float32)
            sel = group_mask(idc, cols, CHUNK, cols)
            weights = held_ref[:, pl.ds(off, CHUNK)]
            column = jnp.zeros((1, CHUNK), jnp.float32)
            for p in range(n):
                acc = (
                    picked[p * cols:(p + 1) * cols]
                    + picked[rows + p * cols:rows + (p + 1) * cols]
                )
                value = jnp.sum(jnp.where(sel, acc, 0.0), axis=0, keepdims=True)
                column = column + weights[p:p + 1] * value
            out_ref[:, pl.ds(off, CHUNK)] = column

        chunks(total, body)

    return pl.pallas_call(
        kernel,
        out_shape=jax.ShapeDtypeStruct((1, total), jnp.float32),
        scratch_shapes=[pltpu.VMEM((2 * rows, HI), jnp.bfloat16)],
    )(table, ids, held)


def source_scatter(values, scales, ids, width, with_norm=False):
    n, total = values.shape
    cols = width // HI
    rows = n * cols
    count = len(scales)

    def kernel(val_ref, *refs):
        scale_refs = refs[:count]
        ids_ref, out_ref = refs[count:count + 2]
        norm_ref = refs[count + 2:]
        out_ref[...] = jnp.zeros(out_ref.shape, jnp.float32)

        def body(off):
            idc = ids_ref[:, pl.ds(off, CHUNK)]
            scale = scale_refs[0][:, pl.ds(off, CHUNK)]
            for other in scale_refs[1:]:
                scale = scale * other[:, pl.ds(off, CHUNK)]
            v = val_ref[:, pl.ds(off, CHUNK)] * scale
            sel = group_mask(idc, cols, CHUNK, cols)
            parts = []
            for piece in pieces(v):
                for p in range(n):
                    parts.append(jnp.where(sel, piece[p:p + 1, :], jnp.zeros((), jnp.bfloat16)))
            spread = jnp.concatenate(parts, axis=0)
            res = lax.dot_general(
                spread, hot_rows(idc, CHUNK), (((1,), (1,)), ((), ())),
                preferred_element_type=jnp.float32,
            )
            out_ref[...] += res[:rows] + res[rows:]

        chunks(total, body)
        if with_norm:
            grad = out_ref[...]
            norm_ref[0][...] = jnp.sum(jnp.sum(grad * grad, axis=0, keepdims=True), axis=1, keepdims=True)

    shape = jax.ShapeDtypeStruct((rows, HI), jnp.float32)
    if not with_norm:
        return pl.pallas_call(kernel, out_shape=shape)(values, *scales, ids)
    grad, norm = pl.pallas_call(
        kernel, out_shape=(shape, jax.ShapeDtypeStruct((1, 1), jnp.float32))
    )(values, *scales, ids)
    return grad, norm.reshape(())


def knot_gather(extended, first_ids, basis, zsrc, weight, extra, knots, parts, width):
    total = first_ids.shape[1]
    cols = knots // HI
    shifted = jnp.stack([extended[q:q + knots] for q in range(4)], axis=0)
    rows = 4 * cols
    per_chunk = CHUNK // width
    line = 128 + -(-width // 128) * 128

    def kernel(tab_ref, ids_ref, basis_ref, zsrc_ref, weight_ref, extra_ref, out_ref, pay_ref, big_ref, norm_ref):
        split_into(tab_ref, big_ref)
        norm_ref[...] = jnp.zeros(norm_ref.shape, jnp.float32)

        for i in range(total // CHUNK):
            off = i * CHUNK
            idc = ids_ref[:, pl.ds(off, CHUNK)]
            picked = jnp.dot(big_ref[...], hot_rows(idc, CHUNK), preferred_element_type=jnp.float32)
            acc = picked[:rows] + picked[rows:]
            sel = group_mask(idc, cols, CHUNK, cols)
            b = basis_ref[:, pl.ds(off, CHUNK)]
            z = jnp.zeros((1, CHUNK), jnp.float32)
            for q in range(4):
                value = jnp.sum(jnp.where(sel, acc[q * cols:(q + 1) * cols], 0.0), axis=0, keepdims=True)
                z = z + b[q:q + 1] * value
            shift = zsrc_ref[:, pl.ds(off, CHUNK)] + z
            out_ref[:, pl.ds(off, CHUNK)] = shift
            for r in range(per_chunk):
                start = (i * per_chunk + r) * line + 128
                pay_ref[:, start:start + width] = shift[:, r * width:(r + 1) * width]
            norm_ref[...] += jnp.sum(weight_ref[:, pl.ds(off, CHUNK)] * shift * shift, axis=1, keepdims=True)

        lane = lax.broadcasted_iota(jnp.int32, (1, 128), 1)
        sums = jnp.where(lane == 0, norm_ref[...], jnp.where(lane == 1, extra_ref[...], 0.0))
        for r in range(parts):
            pay_ref[:, r * line:r * line + 128] = sums
            if line > 128 + width:
                pay_ref[:, r * line + 128 + width:(r + 1) * line] = jnp.zeros((1, line - 128 - width), jnp.float32)

    return pl.pallas_call(
        kernel,
        out_shape=(
            jax.ShapeDtypeStruct((1, total), jnp.float32),
            jax.ShapeDtypeStruct((1, parts * line), jnp.float32),
        ),
        scratch_shapes=[pltpu.VMEM((2 * rows, HI), jnp.bfloat16), pltpu.VMEM((1, 1), jnp.float32)],
    )(shifted.reshape(rows, HI), first_ids, basis, zsrc, weight, extra.reshape(1, 1))


def knot_scatter(values, first_ids, basis16, s_norm, knots, parts):
    total = first_ids.shape[1]
    cols = knots // HI
    rows = 4 * cols
    line = 128 + (cols + 1) * HI

    def kernel(val_ref, ids_ref, basis_ref, norm_ref, pay_ref, acc_ref):
        acc_ref[...] = jnp.zeros(acc_ref.shape, jnp.float32)

        def body(off):
            idc = ids_ref[:, pl.ds(off, CHUNK)]
            sel = group_mask(idc, rows, CHUNK, cols)
            v = jnp.where(sel, basis_ref[:, pl.ds(off, CHUNK)] * val_ref[:, pl.ds(off, CHUNK)], 0.0)
            spread = jnp.concatenate(pieces(v), axis=0)
            res = lax.dot_general(
                spread, hot_rows(idc, CHUNK), (((1,), (1,)), ((), ())),
                preferred_element_type=jnp.float32,
            )
            acc_ref[...] += res[:rows] + res[rows:]

        chunks(total, body)
        lane = lax.broadcasted_iota(jnp.int32, (cols, HI), 1)
        same = acc_ref[0:cols, :]
        carried = jnp.zeros((cols, HI), jnp.float32)
        for q in range(1, 4):
            moved = pltpu.roll(acc_ref[q * cols:(q + 1) * cols, :], q, 1)
            same = same + jnp.where(lane >= q, moved, 0.0)
            carried = carried + jnp.where(lane < q, moved, 0.0)
        blank = jnp.zeros((1, HI), jnp.float32)
        grid = jnp.concatenate([same, blank], axis=0) + jnp.concatenate([blank, carried], axis=0)
        head = jnp.where(lax.broadcasted_iota(jnp.int32, (1, 128), 1) == 0, norm_ref[...], 0.0)
        row = jnp.concatenate([head] + [grid[c:c + 1, :] for c in range(cols + 1)], axis=1)
        for r in range(parts):
            pay_ref[:, r * line:(r + 1) * line] = row

    return pl.pallas_call(
        kernel,
        out_shape=jax.ShapeDtypeStruct((1, parts * line), jnp.float32),
        scratch_shapes=[pltpu.VMEM((rows, HI), jnp.float32)],
    )(values, first_ids, basis16, s_norm.reshape(1, 1)).reshape(parts, line)


def per_device(
    observed_residual,
    source_partials,
    spread_derivative_table,
    detector_index,
    first_knot_interval,
    interval_fraction,
    live_slot_count,
    slot_owned_source,
):
    rows = observed_residual.shape[1]
    n_time = lax.axis_size("tm")
    n_share = lax.axis_size("src")
    n_ranks = n_time * n_share
    capacity = rows // n_ranks
    n_params = source_partials.shape[0]
    detector_count = spread_derivative_table.shape[1]
    knots = KN
    n_knots = n_time * knots
    owned = SRC_DEV
    everyone = ("tm", "src")
    place = jnp.arange(capacity, dtype=jnp.int32)[None, :]
    live = (place < live_slot_count[0][:, None]).astype(jnp.float32).reshape(1, rows)
    indicator = (
        detector_index[None, :] == jnp.arange(detector_count, dtype=jnp.int32)[:, None]
    ).astype(jnp.float32)
    weight_factor = jnp.dot(
        spread_derivative_table,
        indicator,
        precision=lax.Precision.HIGH,
        preferred_element_type=jnp.float32,
    )
    weight_sq = live * jnp.sum(weight_factor * weight_factor, axis=0, keepdims=True)
    basis16 = jnp.repeat(jnp.stack(spline_basis(interval_fraction), axis=0), knots // HI, axis=0)
    first_ids = first_knot_interval.reshape(1, rows)
    ids = slot_owned_source[0].reshape(1, rows)
    zbar0 = live * jnp.sum(weight_factor * observed_residual, axis=0, keepdims=True)

    packed = jnp.concatenate(
        [
            source_partials,
            zbar0,
            weight_sq,
            interval_fraction[None],
            first_knot_interval.astype(jnp.float32)[None],
        ],
        axis=0,
    )
    n_rows = packed.shape[0]
    blocks = packed.reshape(n_rows, n_ranks, capacity).transpose(1, 0, 2).reshape(n_ranks, n_rows * capacity)
    got = lax.all_to_all(blocks, everyone, 0, 0, tiled=True)
    got = got.reshape(n_ranks, n_rows, capacity).transpose(1, 0, 2).reshape(n_rows, rows)
    held = got[:n_params]
    zbar0_own = got[n_params:n_params + 1]
    weight_sq_own = got[n_params + 1:n_params + 2]
    basis_own = jnp.concatenate(spline_basis(got[n_params + 2:n_params + 3]), axis=0)
    slot_device = jnp.arange(rows, dtype=jnp.int32)[None, :] // capacity
    base_own = (slot_device // n_share) * knots + got[n_params + 3:n_params + 4].astype(jnp.int32)
    table_rows = n_params * (owned // HI)

    def combine(sent):
        every = lax.all_to_all(sent, everyone, 0, 0, tiled=True)
        block = jnp.sum(every[:, 128:128 + knots + 3].reshape(n_time, n_share, knots + 3), axis=1)
        main = block[:, :knots].at[1:, :3].add(block[:-1, knots:])
        grad_a = main.reshape(n_knots)
        norm = jnp.sum(every[:, 0]) + jnp.sum(grad_a * grad_a)
        return grad_a, norm

    def forward(zsrc, dir_a, extra):
        extended = jnp.concatenate([dir_a, jnp.zeros((3,), jnp.float32)])
        shift_own, payload = knot_gather(
            extended, base_own, basis_own, zsrc, weight_sq_own, extra, n_knots, n_ranks, capacity
        )
        back = lax.all_to_all(payload.reshape(n_ranks, -1), everyone, 0, 0, tiled=True)
        totals = jnp.sum(back[:, :2], axis=0)
        return shift_own, back[:, 128:128 + capacity].reshape(1, rows) * live, totals[0], totals[1]

    sol_s = jnp.zeros((n_params, owned), jnp.float32)
    sol_a = jnp.zeros((n_knots,), jnp.float32)
    resid = observed_residual
    zbar_slot = zbar0
    sent = knot_scatter(zbar_slot, first_ids, basis16, jnp.zeros((), jnp.float32), knots, n_ranks)
    sent, held, zbar0_own = lax.optimization_barrier((sent, held, zbar0_own))
    grad_a, gamma_a = combine(sent)
    grad_s, extra = source_scatter(held, [zbar0_own], ids, owned, with_norm=True)
    dir_s, dir_a = (grad_s, grad_a)
    pulled = source_gather(dir_s, ids, held)
    for step in range(ITERS):
        shift_own, shift_slot, image_sq, extra_sum = forward(pulled, dir_a, extra)
        if step == 0:
            gamma = extra_sum + gamma_a
        alpha = gamma / image_sq
        sol_s = sol_s + alpha * dir_s.reshape(n_params, owned)
        sol_a = sol_a + alpha * dir_a
        resid = resid - alpha * (weight_factor * shift_slot)
        if step + 1 < ITERS:
            pushed = source_scatter(held, [weight_sq_own, shift_own], ids, owned)
            zbar_slot = zbar_slot - alpha * (weight_sq * shift_slot)
            grad_s = grad_s - alpha * pushed
            grad_a, fresh = combine(
                knot_scatter(zbar_slot, first_ids, basis16, jnp.sum(grad_s * grad_s), knots, n_ranks)
            )
            raw = source_gather(grad_s, ids, held)
            beta = fresh / gamma
            dir_s = grad_s + beta * dir_s
            dir_a = grad_a + beta * dir_a
            pulled = raw + beta * pulled
            gamma = fresh
            extra = jnp.zeros((), jnp.float32)
    mine_a = lax.dynamic_slice(sol_a, (lax.axis_index("tm") * knots,), (knots,))
    return (sol_s, mine_a, resid)


def solution(mesh):
    placed = (
        P(None, ("tm", "src")),
        P(None, ("tm", "src")),
        P(),
        P(("tm", "src")),
        P(("tm", "src")),
        P(("tm", "src")),
        P(("tm", "src"), None),
        P(("tm", "src"), None),
    )
    return jax.shard_map(
        per_device,
        mesh=mesh,
        in_specs=placed,
        out_specs=(P(None, ("tm", "src")), P("tm"), P(None, ("tm", "src"))),
        check_vma=False,
    )
```

```python
import jax
import jax.numpy as jnp
from jax import lax
from jax.experimental import pallas as pl
from jax.experimental.pallas import tpu as pltpu
from jax.sharding import PartitionSpec as P

SRC_DEV = 32768
KN = 1024
ITERS = 2
HI = 256
CHUNK = 4096


def passed_along(block, axis, distance):
    devices = range(lax.axis_size(axis))
    route = [(i - distance, i) for i in devices if i - distance in devices]
    return lax.ppermute(block, axis, route)


def spline_basis(frac):
    u2 = frac * frac
    u3 = u2 * frac
    one = 1.0 - frac
    return [
        one * one * one / 6.0,
        (3.0 * u3 - 6.0 * u2 + 4.0) / 6.0,
        (-3.0 * u3 + 3.0 * u2 + 3.0 * frac + 1.0) / 6.0,
        u3 / 6.0,
    ]


def pieces(x):
    h = x.astype(jnp.bfloat16)
    m = (x - h.astype(jnp.float32)).astype(jnp.bfloat16)
    return h, m


def hot_rows(ids, width):
    low = jnp.bitwise_and(ids, HI - 1)
    return (lax.broadcasted_iota(jnp.int32, (HI, width), 0) == low).astype(jnp.bfloat16)


def group_mask(ids, rows, width, groups):
    high = lax.shift_right_logical(ids, 8)
    iota = lax.broadcasted_iota(jnp.int32, (rows, width), 0)
    return (iota % groups) == high


def chunks(total, body):
    def step(i, carry):
        body(pl.multiple_of(i * CHUNK, CHUNK))
        return carry

    lax.fori_loop(0, total // CHUNK, step, 0)


def split_into(src_ref, big_ref):
    rows = src_ref.shape[0]
    for k, part in enumerate(pieces(src_ref[...])):
        big_ref[k * rows:(k + 1) * rows, :] = part


def source_gather(table, ids, held):
    n, total = held.shape
    rows = table.shape[0]
    cols = rows // n

    def kernel(tab_ref, ids_ref, held_ref, out_ref, big_ref):
        split_into(tab_ref, big_ref)

        def body(off):
            idc = ids_ref[:, pl.ds(off, CHUNK)]
            picked = jnp.dot(big_ref[...], hot_rows(idc, CHUNK), preferred_element_type=jnp.float32)
            sel = group_mask(idc, cols, CHUNK, cols)
            weights = held_ref[:, pl.ds(off, CHUNK)]
            column = jnp.zeros((1, CHUNK), jnp.float32)
            for p in range(n):
                acc = (
                    picked[p * cols:(p + 1) * cols]
                    + picked[rows + p * cols:rows + (p + 1) * cols]
                )
                value = jnp.sum(jnp.where(sel, acc, 0.0), axis=0, keepdims=True)
                column = column + weights[p:p + 1] * value
            out_ref[:, pl.ds(off, CHUNK)] = column

        chunks(total, body)

    return pl.pallas_call(
        kernel,
        out_shape=jax.ShapeDtypeStruct((1, total), jnp.float32),
        scratch_shapes=[pltpu.VMEM((2 * rows, HI), jnp.bfloat16)],
    )(table, ids, held)


def source_scatter(values, scales, ids, width, with_norm=False):
    n, total = values.shape
    cols = width // HI
    rows = n * cols
    count = len(scales)

    def kernel(val_ref, *refs):
        scale_refs = refs[:count]
        ids_ref, out_ref = refs[count:count + 2]
        norm_ref = refs[count + 2:]
        out_ref[...] = jnp.zeros(out_ref.shape, jnp.float32)

        def body(off):
            idc = ids_ref[:, pl.ds(off, CHUNK)]
            scale = scale_refs[0][:, pl.ds(off, CHUNK)]
            for other in scale_refs[1:]:
                scale = scale * other[:, pl.ds(off, CHUNK)]
            v = val_ref[:, pl.ds(off, CHUNK)] * scale
            sel = group_mask(idc, cols, CHUNK, cols)
            parts = []
            for piece in pieces(v):
                for p in range(n):
                    parts.append(jnp.where(sel, piece[p:p + 1, :], jnp.zeros((), jnp.bfloat16)))
            spread = jnp.concatenate(parts, axis=0)
            res = lax.dot_general(
                spread, hot_rows(idc, CHUNK), (((1,), (1,)), ((), ())),
                preferred_element_type=jnp.float32,
            )
            out_ref[...] += res[:rows] + res[rows:]

        chunks(total, body)
        if with_norm:
            grad = out_ref[...]
            norm_ref[0][...] = jnp.sum(jnp.sum(grad * grad, axis=0, keepdims=True), axis=1, keepdims=True)

    shape = jax.ShapeDtypeStruct((rows, HI), jnp.float32)
    if not with_norm:
        return pl.pallas_call(kernel, out_shape=shape)(values, *scales, ids)
    grad, norm = pl.pallas_call(
        kernel, out_shape=(shape, jax.ShapeDtypeStruct((1, 1), jnp.float32))
    )(values, *scales, ids)
    return grad, norm.reshape(())


def knot_gather(extended, first_ids, basis, zsrc, weight, extra, knots, parts, width, carry=None):
    total = first_ids.shape[1]
    cols = knots // HI
    shifted = jnp.stack([extended[q:q + knots] for q in range(4)], axis=0)
    rows = 4 * cols
    per_chunk = CHUNK // width
    line = 128 + -(-width // 128) * 128

    extras = [] if carry is None else [carry[0].reshape(1, 1), carry[1]]

    def kernel(tab_ref, ids_ref, basis_ref, zsrc_ref, weight_ref, extra_ref, *refs):
        out_ref, pay_ref, big_ref, norm_ref = refs[-4:]
        split_into(tab_ref, big_ref)
        norm_ref[...] = jnp.zeros(norm_ref.shape, jnp.float32)

        for i in range(total // CHUNK):
            off = i * CHUNK
            idc = ids_ref[:, pl.ds(off, CHUNK)]
            picked = jnp.dot(big_ref[...], hot_rows(idc, CHUNK), preferred_element_type=jnp.float32)
            acc = picked[:rows] + picked[rows:]
            sel = group_mask(idc, cols, CHUNK, cols)
            b = basis_ref[:, pl.ds(off, CHUNK)]
            z = jnp.zeros((1, CHUNK), jnp.float32)
            for q in range(4):
                value = jnp.sum(jnp.where(sel, acc[q * cols:(q + 1) * cols], 0.0), axis=0, keepdims=True)
                z = z + b[q:q + 1] * value
            shift = zsrc_ref[:, pl.ds(off, CHUNK)] + z
            if carry is not None:
                shift = shift + refs[0][...] * refs[1][:, pl.ds(off, CHUNK)]
            out_ref[:, pl.ds(off, CHUNK)] = shift
            for r in range(per_chunk):
                start = (i * per_chunk + r) * line + 128
                pay_ref[:, start:start + width] = shift[:, r * width:(r + 1) * width]
            norm_ref[...] += jnp.sum(weight_ref[:, pl.ds(off, CHUNK)] * shift * shift, axis=1, keepdims=True)

        lane = lax.broadcasted_iota(jnp.int32, (1, 128), 1)
        sums = jnp.where(lane == 0, norm_ref[...], jnp.where(lane == 1, extra_ref[...], 0.0))
        for r in range(parts):
            pay_ref[:, r * line:r * line + 128] = sums
            if line > 128 + width:
                pay_ref[:, r * line + 128 + width:(r + 1) * line] = jnp.zeros((1, line - 128 - width), jnp.float32)

    return pl.pallas_call(
        kernel,
        out_shape=(
            jax.ShapeDtypeStruct((1, total), jnp.float32),
            jax.ShapeDtypeStruct((1, parts * line), jnp.float32),
        ),
        scratch_shapes=[pltpu.VMEM((2 * rows, HI), jnp.bfloat16), pltpu.VMEM((1, 1), jnp.float32)],
    )(shifted.reshape(rows, HI), first_ids, basis, zsrc, weight, extra.reshape(1, 1), *extras)


def knot_scatter(values, first_ids, basis16, s_norm, knots, parts):
    total = first_ids.shape[1]
    cols = knots // HI
    rows = 4 * cols
    line = 128 + (cols + 1) * HI

    def kernel(val_ref, ids_ref, basis_ref, norm_ref, pay_ref, acc_ref):
        acc_ref[...] = jnp.zeros(acc_ref.shape, jnp.float32)

        def body(off):
            idc = ids_ref[:, pl.ds(off, CHUNK)]
            sel = group_mask(idc, rows, CHUNK, cols)
            v = jnp.where(sel, basis_ref[:, pl.ds(off, CHUNK)] * val_ref[:, pl.ds(off, CHUNK)], 0.0)
            spread = jnp.concatenate(pieces(v), axis=0)
            res = lax.dot_general(
                spread, hot_rows(idc, CHUNK), (((1,), (1,)), ((), ())),
                preferred_element_type=jnp.float32,
            )
            acc_ref[...] += res[:rows] + res[rows:]

        chunks(total, body)
        lane = lax.broadcasted_iota(jnp.int32, (cols, HI), 1)
        same = acc_ref[0:cols, :]
        carried = jnp.zeros((cols, HI), jnp.float32)
        for q in range(1, 4):
            moved = pltpu.roll(acc_ref[q * cols:(q + 1) * cols, :], q, 1)
            same = same + jnp.where(lane >= q, moved, 0.0)
            carried = carried + jnp.where(lane < q, moved, 0.0)
        blank = jnp.zeros((1, HI), jnp.float32)
        grid = jnp.concatenate([same, blank], axis=0) + jnp.concatenate([blank, carried], axis=0)
        head = jnp.where(lax.broadcasted_iota(jnp.int32, (1, 128), 1) == 0, norm_ref[...], 0.0)
        row = jnp.concatenate([head] + [grid[c:c + 1, :] for c in range(cols + 1)], axis=1)
        for r in range(parts):
            pay_ref[:, r * line:(r + 1) * line] = row

    return pl.pallas_call(
        kernel,
        out_shape=jax.ShapeDtypeStruct((1, parts * line), jnp.float32),
        scratch_shapes=[pltpu.VMEM((rows, HI), jnp.float32)],
    )(values, first_ids, basis16, s_norm.reshape(1, 1)).reshape(parts, line)


def per_device(
    observed_residual,
    source_partials,
    spread_derivative_table,
    detector_index,
    first_knot_interval,
    interval_fraction,
    live_slot_count,
    slot_owned_source,
):
    rows = observed_residual.shape[1]
    n_time = lax.axis_size("tm")
    n_share = lax.axis_size("src")
    n_ranks = n_time * n_share
    capacity = rows // n_ranks
    n_params = source_partials.shape[0]
    detector_count = spread_derivative_table.shape[1]
    knots = KN
    n_knots = n_time * knots
    owned = SRC_DEV
    everyone = ("tm", "src")
    place = jnp.arange(capacity, dtype=jnp.int32)[None, :]
    live = (place < live_slot_count[0][:, None]).astype(jnp.float32).reshape(1, rows)
    indicator = (
        detector_index[None, :] == jnp.arange(detector_count, dtype=jnp.int32)[:, None]
    ).astype(jnp.float32)
    weight_factor = jnp.dot(
        spread_derivative_table,
        indicator,
        precision=lax.Precision.HIGHEST,
        preferred_element_type=jnp.float32,
    )
    weight_sq = live * jnp.sum(weight_factor * weight_factor, axis=0, keepdims=True)
    basis16 = jnp.repeat(jnp.stack(spline_basis(interval_fraction), axis=0), knots // HI, axis=0)
    first_ids = first_knot_interval.reshape(1, rows)
    ids = slot_owned_source[0].reshape(1, rows)
    zbar0 = live * jnp.sum(weight_factor * observed_residual, axis=0, keepdims=True)

    packed = jnp.concatenate(
        [
            source_partials,
            zbar0,
            weight_sq,
            interval_fraction[None],
            first_knot_interval.astype(jnp.float32)[None],
        ],
        axis=0,
    )
    n_rows = packed.shape[0]
    blocks = packed.reshape(n_rows, n_ranks, capacity).transpose(1, 0, 2).reshape(n_ranks, n_rows * capacity)
    got = lax.all_to_all(blocks, everyone, 0, 0, tiled=True)
    got = got.reshape(n_ranks, n_rows, capacity).transpose(1, 0, 2).reshape(n_rows, rows)
    held = got[:n_params]
    zbar0_own = got[n_params:n_params + 1]
    weight_sq_own = got[n_params + 1:n_params + 2]
    basis_own = jnp.concatenate(spline_basis(got[n_params + 2:n_params + 3]), axis=0)
    slot_device = jnp.arange(rows, dtype=jnp.int32)[None, :] // capacity
    base_own = (slot_device // n_share) * knots + got[n_params + 3:n_params + 4].astype(jnp.int32)
    table_rows = n_params * (owned // HI)

    def combine(sent):
        every = lax.all_to_all(sent, everyone, 0, 0, tiled=True)
        block = jnp.sum(every[:, 128:128 + knots + 3].reshape(n_time, n_share, knots + 3), axis=1)
        main = block[:, :knots].at[1:, :3].add(block[:-1, knots:])
        grad_a = main.reshape(n_knots)
        norm = jnp.sum(every[:, 0]) + jnp.sum(grad_a * grad_a)
        return grad_a, norm

    def forward(zsrc, dir_a, extra, carry=None):
        extended = jnp.concatenate([dir_a, jnp.zeros((3,), jnp.float32)])
        shift_own, payload = knot_gather(
            extended, base_own, basis_own, zsrc, weight_sq_own, extra, n_knots, n_ranks, capacity, carry
        )
        back = lax.all_to_all(payload.reshape(n_ranks, -1), everyone, 0, 0, tiled=True)
        totals = jnp.sum(back[:, :2], axis=0)
        return shift_own, back[:, 128:128 + capacity].reshape(1, rows) * live, totals[0], totals[1]

    sol_s = jnp.zeros((n_params, owned), jnp.float32)
    sol_a = jnp.zeros((n_knots,), jnp.float32)
    resid = observed_residual
    zbar_slot = zbar0
    sent = knot_scatter(zbar_slot, first_ids, basis16, jnp.zeros((), jnp.float32), knots, n_ranks)
    sent, held, zbar0_own = lax.optimization_barrier((sent, held, zbar0_own))
    grad_a, gamma_a = combine(sent)
    grad_s, extra = source_scatter(held, [zbar0_own], ids, owned, with_norm=True)
    dir_s, dir_a = (grad_s, grad_a)
    zsrc, att, carry = source_gather(dir_s, ids, held), dir_a, None
    for step in range(ITERS):
        shift_own, shift_slot, image_sq, extra_sum = forward(zsrc, att, extra, carry)
        if step == 0:
            gamma = extra_sum + gamma_a
        alpha = gamma / image_sq
        sol_s = sol_s + alpha * dir_s.reshape(n_params, owned)
        sol_a = sol_a + alpha * dir_a
        resid = resid - alpha * (weight_factor * shift_slot)
        if step + 1 < ITERS:
            pushed = source_scatter(held, [weight_sq_own, shift_own], ids, owned)
            zbar_slot = zbar_slot - alpha * (weight_sq * shift_slot)
            grad_s = grad_s - alpha * pushed
            grad_a, fresh = combine(
                knot_scatter(zbar_slot, first_ids, basis16, jnp.sum(grad_s * grad_s), knots, n_ranks)
            )
            zsrc, att = source_gather(grad_s, ids, held), grad_a
            beta = fresh / gamma
            carry = (beta, shift_own)
            dir_s = grad_s + beta * dir_s
            dir_a = grad_a + beta * dir_a
            gamma = fresh
            extra = jnp.zeros((), jnp.float32)
    mine_a = lax.dynamic_slice(sol_a, (lax.axis_index("tm") * knots,), (knots,))
    return (sol_s, mine_a, resid)


def solution(mesh):
    placed = (
        P(None, ("tm", "src")),
        P(None, ("tm", "src")),
        P(),
        P(("tm", "src")),
        P(("tm", "src")),
        P(("tm", "src")),
        P(("tm", "src"), None),
        P(("tm", "src"), None),
    )
    return jax.shard_map(
        per_device,
        mesh=mesh,
        in_specs=placed,
        out_specs=(P(None, ("tm", "src")), P("tm"), P(None, ("tm", "src"))),
        check_vma=False,
    )
```

```python
import jax
import jax.numpy as jnp
from jax import lax
from jax.experimental import pallas as pl
from jax.experimental.pallas import tpu as pltpu
from jax.sharding import PartitionSpec as P

SRC_DEV = 32768
KN = 1024
ITERS = 2
HI = 256
CHUNK = 4096


def passed_along(block, axis, distance):
    devices = range(lax.axis_size(axis))
    route = [(i - distance, i) for i in devices if i - distance in devices]
    return lax.ppermute(block, axis, route)


def spline_basis(frac):
    u2 = frac * frac
    u3 = u2 * frac
    one = 1.0 - frac
    return [
        one * one * one / 6.0,
        (3.0 * u3 - 6.0 * u2 + 4.0) / 6.0,
        (-3.0 * u3 + 3.0 * u2 + 3.0 * frac + 1.0) / 6.0,
        u3 / 6.0,
    ]


def pieces(x):
    h = x.astype(jnp.bfloat16)
    m = (x - h.astype(jnp.float32)).astype(jnp.bfloat16)
    return h, m


def hot_rows(ids, width):
    low = jnp.bitwise_and(ids, HI - 1)
    return (lax.broadcasted_iota(jnp.int32, (HI, width), 0) == low).astype(jnp.bfloat16)


def group_mask(ids, rows, width, groups):
    high = lax.shift_right_logical(ids, 8)
    iota = lax.broadcasted_iota(jnp.int32, (rows, width), 0)
    return (iota % groups) == high


def chunks(total, body):
    def step(i, carry):
        body(pl.multiple_of(i * CHUNK, CHUNK))
        return carry

    lax.fori_loop(0, total // CHUNK, step, 0)


def split_into(src_ref, big_ref):
    rows = src_ref.shape[0]
    for k, part in enumerate(pieces(src_ref[...])):
        big_ref[k * rows:(k + 1) * rows, :] = part


def source_gather(table, ids, held):
    n, total = held.shape
    rows = table.shape[0]
    cols = rows // n

    def kernel(tab_ref, ids_ref, held_ref, out_ref, big_ref):
        split_into(tab_ref, big_ref)

        def body(off):
            idc = ids_ref[:, pl.ds(off, CHUNK)]
            picked = jnp.dot(big_ref[...], hot_rows(idc, CHUNK), preferred_element_type=jnp.float32)
            sel = group_mask(idc, cols, CHUNK, cols)
            weights = held_ref[:, pl.ds(off, CHUNK)]
            column = jnp.zeros((1, CHUNK), jnp.float32)
            for p in range(n):
                acc = (
                    picked[p * cols:(p + 1) * cols]
                    + picked[rows + p * cols:rows + (p + 1) * cols]
                )
                value = jnp.sum(jnp.where(sel, acc, 0.0), axis=0, keepdims=True)
                column = column + weights[p:p + 1] * value
            out_ref[:, pl.ds(off, CHUNK)] = column

        chunks(total, body)

    return pl.pallas_call(
        kernel,
        out_shape=jax.ShapeDtypeStruct((1, total), jnp.float32),
        scratch_shapes=[pltpu.VMEM((2 * rows, HI), jnp.bfloat16)],
    )(table, ids, held)


def source_scatter(values, scales, ids, width, with_norm=False):
    n, total = values.shape
    cols = width // HI
    rows = n * cols
    count = len(scales)

    def kernel(val_ref, *refs):
        scale_refs = refs[:count]
        ids_ref, out_ref = refs[count:count + 2]
        norm_ref = refs[count + 2:]
        out_ref[...] = jnp.zeros(out_ref.shape, jnp.float32)

        def body(off):
            idc = ids_ref[:, pl.ds(off, CHUNK)]
            scale = scale_refs[0][:, pl.ds(off, CHUNK)]
            for other in scale_refs[1:]:
                scale = scale * other[:, pl.ds(off, CHUNK)]
            v = val_ref[:, pl.ds(off, CHUNK)] * scale
            sel = group_mask(idc, cols, CHUNK, cols)
            parts = []
            for piece in pieces(v):
                for p in range(n):
                    parts.append(jnp.where(sel, piece[p:p + 1, :], jnp.zeros((), jnp.bfloat16)))
            spread = jnp.concatenate(parts, axis=0)
            res = lax.dot_general(
                spread, hot_rows(idc, CHUNK), (((1,), (1,)), ((), ())),
                preferred_element_type=jnp.float32,
            )
            out_ref[...] += res[:rows] + res[rows:]

        chunks(total, body)
        if with_norm:
            grad = out_ref[...]
            norm_ref[0][...] = jnp.sum(jnp.sum(grad * grad, axis=0, keepdims=True), axis=1, keepdims=True)

    shape = jax.ShapeDtypeStruct((rows, HI), jnp.float32)
    if not with_norm:
        return pl.pallas_call(kernel, out_shape=shape)(values, *scales, ids)
    grad, norm = pl.pallas_call(
        kernel, out_shape=(shape, jax.ShapeDtypeStruct((1, 1), jnp.float32))
    )(values, *scales, ids)
    return grad, norm.reshape(())


def knot_gather(extended, frac, first, block_knots, share, zsrc, weight, extra, knots, parts, width, carry=None):
    total = frac.shape[1]
    cols = knots // HI
    shifted = jnp.stack([extended[q:q + knots] for q in range(4)], axis=0)
    rows = 4 * cols
    per_chunk = CHUNK // width
    line = 128 + -(-width // 128) * 128

    extras = [] if carry is None else [carry[0].reshape(1, 1), carry[1]]

    def kernel(tab_ref, frac_ref, first_ref, zsrc_ref, weight_ref, extra_ref, *refs):
        out_ref, pay_ref, big_ref, norm_ref = refs[-4:]
        split_into(tab_ref, big_ref)
        norm_ref[...] = jnp.zeros(norm_ref.shape, jnp.float32)

        for i in range(total // CHUNK):
            off = i * CHUNK
            slot = lax.broadcasted_iota(jnp.int32, (1, CHUNK), 1) + off
            idc = (slot // width // share) * block_knots + first_ref[:, pl.ds(off, CHUNK)].astype(jnp.int32)
            picked = jnp.dot(big_ref[...], hot_rows(idc, CHUNK), preferred_element_type=jnp.float32)
            acc = picked[:rows] + picked[rows:]
            sel = group_mask(idc, cols, CHUNK, cols)
            b = spline_basis(frac_ref[:, pl.ds(off, CHUNK)])
            z = jnp.zeros((1, CHUNK), jnp.float32)
            for q in range(4):
                value = jnp.sum(jnp.where(sel, acc[q * cols:(q + 1) * cols], 0.0), axis=0, keepdims=True)
                z = z + b[q] * value
            shift = zsrc_ref[:, pl.ds(off, CHUNK)] + z
            if carry is not None:
                shift = shift + refs[0][...] * refs[1][:, pl.ds(off, CHUNK)]
            out_ref[:, pl.ds(off, CHUNK)] = shift
            for r in range(per_chunk):
                start = (i * per_chunk + r) * line + 128
                pay_ref[:, start:start + width] = shift[:, r * width:(r + 1) * width]
            norm_ref[...] += jnp.sum(weight_ref[:, pl.ds(off, CHUNK)] * shift * shift, axis=1, keepdims=True)

        lane = lax.broadcasted_iota(jnp.int32, (1, 128), 1)
        sums = jnp.where(lane == 0, norm_ref[...], jnp.where(lane == 1, extra_ref[...], 0.0))
        for r in range(parts):
            pay_ref[:, r * line:r * line + 128] = sums
            if line > 128 + width:
                pay_ref[:, r * line + 128 + width:(r + 1) * line] = jnp.zeros((1, line - 128 - width), jnp.float32)

    return pl.pallas_call(
        kernel,
        out_shape=(
            jax.ShapeDtypeStruct((1, total), jnp.float32),
            jax.ShapeDtypeStruct((1, parts * line), jnp.float32),
        ),
        scratch_shapes=[pltpu.VMEM((2 * rows, HI), jnp.bfloat16), pltpu.VMEM((1, 1), jnp.float32)],
    )(shifted.reshape(rows, HI), frac, first, zsrc, weight, extra.reshape(1, 1), *extras)


def knot_scatter(values, first_ids, basis16, s_norm, knots, parts):
    total = first_ids.shape[1]
    cols = knots // HI
    rows = 4 * cols
    line = 128 + (cols + 1) * HI

    def kernel(val_ref, ids_ref, basis_ref, norm_ref, pay_ref, acc_ref):
        acc_ref[...] = jnp.zeros(acc_ref.shape, jnp.float32)

        def body(off):
            idc = ids_ref[:, pl.ds(off, CHUNK)]
            sel = group_mask(idc, rows, CHUNK, cols)
            v = jnp.where(sel, basis_ref[:, pl.ds(off, CHUNK)] * val_ref[:, pl.ds(off, CHUNK)], 0.0)
            spread = jnp.concatenate(pieces(v), axis=0)
            res = lax.dot_general(
                spread, hot_rows(idc, CHUNK), (((1,), (1,)), ((), ())),
                preferred_element_type=jnp.float32,
            )
            acc_ref[...] += res[:rows] + res[rows:]

        chunks(total, body)
        lane = lax.broadcasted_iota(jnp.int32, (cols, HI), 1)
        same = acc_ref[0:cols, :]
        carried = jnp.zeros((cols, HI), jnp.float32)
        for q in range(1, 4):
            moved = pltpu.roll(acc_ref[q * cols:(q + 1) * cols, :], q, 1)
            same = same + jnp.where(lane >= q, moved, 0.0)
            carried = carried + jnp.where(lane < q, moved, 0.0)
        blank = jnp.zeros((1, HI), jnp.float32)
        grid = jnp.concatenate([same, blank], axis=0) + jnp.concatenate([blank, carried], axis=0)
        head = jnp.where(lax.broadcasted_iota(jnp.int32, (1, 128), 1) == 0, norm_ref[...], 0.0)
        row = jnp.concatenate([head] + [grid[c:c + 1, :] for c in range(cols + 1)], axis=1)
        for r in range(parts):
            pay_ref[:, r * line:(r + 1) * line] = row

    return pl.pallas_call(
        kernel,
        out_shape=jax.ShapeDtypeStruct((1, parts * line), jnp.float32),
        scratch_shapes=[pltpu.VMEM((rows, HI), jnp.float32)],
    )(values, first_ids, basis16, s_norm.reshape(1, 1)).reshape(parts, line)


def per_device(
    observed_residual,
    source_partials,
    spread_derivative_table,
    detector_index,
    first_knot_interval,
    interval_fraction,
    live_slot_count,
    slot_owned_source,
):
    rows = observed_residual.shape[1]
    n_time = lax.axis_size("tm")
    n_share = lax.axis_size("src")
    n_ranks = n_time * n_share
    capacity = rows // n_ranks
    n_params = source_partials.shape[0]
    detector_count = spread_derivative_table.shape[1]
    knots = KN
    n_knots = n_time * knots
    owned = SRC_DEV
    everyone = ("tm", "src")
    place = jnp.arange(capacity, dtype=jnp.int32)[None, :]
    live = (place < live_slot_count[0][:, None]).astype(jnp.float32).reshape(1, rows)
    indicator = (
        detector_index[None, :] == jnp.arange(detector_count, dtype=jnp.int32)[:, None]
    ).astype(jnp.float32)
    weight_factor = jnp.dot(
        spread_derivative_table,
        indicator,
        precision=lax.Precision.HIGHEST,
        preferred_element_type=jnp.float32,
    )
    weight_sq = live * jnp.sum(weight_factor * weight_factor, axis=0, keepdims=True)
    basis16 = jnp.repeat(jnp.stack(spline_basis(interval_fraction), axis=0), knots // HI, axis=0)
    first_ids = first_knot_interval.reshape(1, rows)
    ids = slot_owned_source[0].reshape(1, rows)
    zbar0 = live * jnp.sum(weight_factor * observed_residual, axis=0, keepdims=True)

    packed = jnp.concatenate(
        [
            source_partials,
            zbar0,
            weight_sq,
            interval_fraction[None],
            first_knot_interval.astype(jnp.float32)[None],
        ],
        axis=0,
    )
    n_rows = packed.shape[0]
    blocks = packed.reshape(n_rows, n_ranks, capacity).transpose(1, 0, 2).reshape(n_ranks, n_rows * capacity)
    got = lax.all_to_all(blocks, everyone, 0, 0, tiled=True)
    got = got.reshape(n_ranks, n_rows, capacity).transpose(1, 0, 2).reshape(n_rows, rows)
    held = got[:n_params]
    zbar0_own = got[n_params:n_params + 1]
    weight_sq_own = got[n_params + 1:n_params + 2]
    frac_own = got[n_params + 2:n_params + 3]
    first_own = got[n_params + 3:n_params + 4]
    table_rows = n_params * (owned // HI)

    def combine(sent):
        every = lax.all_to_all(sent, everyone, 0, 0, tiled=True)
        block = jnp.sum(every[:, 128:128 + knots + 3].reshape(n_time, n_share, knots + 3), axis=1)
        main = block[:, :knots].at[1:, :3].add(block[:-1, knots:])
        grad_a = main.reshape(n_knots)
        norm = jnp.sum(every[:, 0]) + jnp.sum(grad_a * grad_a)
        return grad_a, norm

    def forward(zsrc, dir_a, extra, carry=None):
        extended = jnp.concatenate([dir_a, jnp.zeros((3,), jnp.float32)])
        shift_own, payload = knot_gather(
            extended, frac_own, first_own, knots, n_share, zsrc, weight_sq_own, extra, n_knots, n_ranks,
            capacity, carry,
        )
        back = lax.all_to_all(payload.reshape(n_ranks, -1), everyone, 0, 0, tiled=True)
        totals = jnp.sum(back[:, :2], axis=0)
        return shift_own, back[:, 128:128 + capacity].reshape(1, rows) * live, totals[0], totals[1]

    sol_s = jnp.zeros((n_params, owned), jnp.float32)
    sol_a = jnp.zeros((n_knots,), jnp.float32)
    resid = observed_residual
    zbar_slot = zbar0
    sent = knot_scatter(zbar_slot, first_ids, basis16, jnp.zeros((), jnp.float32), knots, n_ranks)
    sent, held, zbar0_own = lax.optimization_barrier((sent, held, zbar0_own))
    grad_a, gamma_a = combine(sent)
    grad_s, extra = source_scatter(held, [zbar0_own], ids, owned, with_norm=True)
    dir_s, dir_a = (grad_s, grad_a)
    zsrc, att, carry = source_gather(dir_s, ids, held), dir_a, None
    for step in range(ITERS):
        shift_own, shift_slot, image_sq, extra_sum = forward(zsrc, att, extra, carry)
        if step == 0:
            gamma = extra_sum + gamma_a
        alpha = gamma / image_sq
        sol_s = sol_s + alpha * dir_s.reshape(n_params, owned)
        sol_a = sol_a + alpha * dir_a
        resid = resid - alpha * (weight_factor * shift_slot)
        if step + 1 < ITERS:
            pushed = source_scatter(held, [weight_sq_own, shift_own], ids, owned)
            zbar_slot = zbar_slot - alpha * (weight_sq * shift_slot)
            grad_s = grad_s - alpha * pushed
            grad_a, fresh = combine(
                knot_scatter(zbar_slot, first_ids, basis16, jnp.sum(grad_s * grad_s), knots, n_ranks)
            )
            zsrc, att = source_gather(grad_s, ids, held), grad_a
            beta = fresh / gamma
            carry = (beta, shift_own)
            dir_s = grad_s + beta * dir_s
            dir_a = grad_a + beta * dir_a
            gamma = fresh
            extra = jnp.zeros((), jnp.float32)
    mine_a = lax.dynamic_slice(sol_a, (lax.axis_index("tm") * knots,), (knots,))
    return (sol_s, mine_a, resid)


def solution(mesh):
    placed = (
        P(None, ("tm", "src")),
        P(None, ("tm", "src")),
        P(),
        P(("tm", "src")),
        P(("tm", "src")),
        P(("tm", "src")),
        P(("tm", "src"), None),
        P(("tm", "src"), None),
    )
    return jax.shard_map(
        per_device,
        mesh=mesh,
        in_specs=placed,
        out_specs=(P(None, ("tm", "src")), P("tm"), P(None, ("tm", "src"))),
        check_vma=False,
    )
```

```python
import jax
import jax.numpy as jnp
from jax import lax
from jax.experimental import pallas as pl
from jax.experimental.pallas import tpu as pltpu
from jax.sharding import PartitionSpec as P

SRC_DEV = 32768
KN = 1024
ITERS = 2
HI = 256
CHUNK = 4096


def passed_along(block, axis, distance):
    devices = range(lax.axis_size(axis))
    route = [(i - distance, i) for i in devices if i - distance in devices]
    return lax.ppermute(block, axis, route)


def spline_basis(frac):
    u2 = frac * frac
    u3 = u2 * frac
    one = 1.0 - frac
    return [
        one * one * one / 6.0,
        (3.0 * u3 - 6.0 * u2 + 4.0) / 6.0,
        (-3.0 * u3 + 3.0 * u2 + 3.0 * frac + 1.0) / 6.0,
        u3 / 6.0,
    ]


def pieces(x):
    h = x.astype(jnp.bfloat16)
    m = (x - h.astype(jnp.float32)).astype(jnp.bfloat16)
    return h, m


def hot_rows(ids, width):
    low = jnp.bitwise_and(ids, HI - 1)
    return (lax.broadcasted_iota(jnp.int32, (HI, width), 0) == low).astype(jnp.bfloat16)


def group_mask(ids, rows, width, groups):
    high = lax.shift_right_logical(ids, 8)
    iota = lax.broadcasted_iota(jnp.int32, (rows, width), 0)
    return (iota % groups) == high


def chunks(total, body):
    def step(i, carry):
        body(pl.multiple_of(i * CHUNK, CHUNK))
        return carry

    lax.fori_loop(0, total // CHUNK, step, 0)


def split_into(src_ref, big_ref):
    rows = src_ref.shape[0]
    for k, part in enumerate(pieces(src_ref[...])):
        big_ref[k * rows:(k + 1) * rows, :] = part


def source_gather(table, ids, held):
    n, total = held.shape
    rows = table.shape[0]
    cols = rows // n

    def kernel(tab_ref, ids_ref, held_ref, out_ref, big_ref):
        split_into(tab_ref, big_ref)

        def body(off):
            idc = ids_ref[:, pl.ds(off, CHUNK)]
            picked = jnp.dot(big_ref[...], hot_rows(idc, CHUNK), preferred_element_type=jnp.float32)
            sel = group_mask(idc, cols, CHUNK, cols)
            weights = held_ref[:, pl.ds(off, CHUNK)]
            column = jnp.zeros((1, CHUNK), jnp.float32)
            for p in range(n):
                acc = (
                    picked[p * cols:(p + 1) * cols]
                    + picked[rows + p * cols:rows + (p + 1) * cols]
                )
                value = jnp.sum(jnp.where(sel, acc, 0.0), axis=0, keepdims=True)
                column = column + weights[p:p + 1] * value
            out_ref[:, pl.ds(off, CHUNK)] = column

        chunks(total, body)

    return pl.pallas_call(
        kernel,
        out_shape=jax.ShapeDtypeStruct((1, total), jnp.float32),
        scratch_shapes=[pltpu.VMEM((2 * rows, HI), jnp.bfloat16)],
    )(table, ids, held)


def source_scatter(values, scales, ids, width, with_norm=False):
    n, total = values.shape
    cols = width // HI
    rows = n * cols
    count = len(scales)

    def kernel(val_ref, *refs):
        scale_refs = refs[:count]
        ids_ref, out_ref = refs[count:count + 2]
        norm_ref = refs[count + 2:]
        out_ref[...] = jnp.zeros(out_ref.shape, jnp.float32)

        def body(off):
            idc = ids_ref[:, pl.ds(off, CHUNK)]
            scale = scale_refs[0][:, pl.ds(off, CHUNK)]
            for other in scale_refs[1:]:
                scale = scale * other[:, pl.ds(off, CHUNK)]
            v = val_ref[:, pl.ds(off, CHUNK)] * scale
            sel = group_mask(idc, cols, CHUNK, cols)
            parts = []
            for piece in pieces(v):
                for p in range(n):
                    parts.append(jnp.where(sel, piece[p:p + 1, :], jnp.zeros((), jnp.bfloat16)))
            spread = jnp.concatenate(parts, axis=0)
            res = lax.dot_general(
                spread, hot_rows(idc, CHUNK), (((1,), (1,)), ((), ())),
                preferred_element_type=jnp.float32,
            )
            out_ref[...] += res[:rows] + res[rows:]

        chunks(total, body)
        if with_norm:
            grad = out_ref[...]
            norm_ref[0][...] = jnp.sum(jnp.sum(grad * grad, axis=0, keepdims=True), axis=1, keepdims=True)

    shape = jax.ShapeDtypeStruct((rows, HI), jnp.float32)
    if not with_norm:
        return pl.pallas_call(kernel, out_shape=shape)(values, *scales, ids)
    grad, norm = pl.pallas_call(
        kernel, out_shape=(shape, jax.ShapeDtypeStruct((1, 1), jnp.float32))
    )(values, *scales, ids)
    return grad, norm.reshape(())


def knot_gather(extended, frac, first, block_knots, share, zsrc, weight, extra, knots, parts, width, carry=None):
    total = frac.shape[1]
    cols = knots // HI
    shifted = jnp.stack([extended[q:q + knots] for q in range(4)], axis=0)
    rows = 4 * cols
    per_chunk = CHUNK // width
    line = 128 + -(-width // 128) * 128

    extras = [] if carry is None else [carry[0].reshape(1, 1), carry[1]]

    def kernel(tab_ref, frac_ref, first_ref, zsrc_ref, weight_ref, extra_ref, *refs):
        out_ref, pay_ref, big_ref, norm_ref = refs[-4:]
        split_into(tab_ref, big_ref)
        norm_ref[...] = jnp.zeros(norm_ref.shape, jnp.float32)

        for i in range(total // CHUNK):
            off = i * CHUNK
            slot = lax.broadcasted_iota(jnp.int32, (1, CHUNK), 1) + off
            idc = (slot // width // share) * block_knots + first_ref[:, pl.ds(off, CHUNK)].astype(jnp.int32)
            picked = jnp.dot(big_ref[...], hot_rows(idc, CHUNK), preferred_element_type=jnp.float32)
            acc = picked[:rows] + picked[rows:]
            sel = group_mask(idc, cols, CHUNK, cols)
            b = spline_basis(frac_ref[:, pl.ds(off, CHUNK)])
            z = jnp.zeros((1, CHUNK), jnp.float32)
            for q in range(4):
                value = jnp.sum(jnp.where(sel, acc[q * cols:(q + 1) * cols], 0.0), axis=0, keepdims=True)
                z = z + b[q] * value
            shift = zsrc_ref[:, pl.ds(off, CHUNK)] + z
            if carry is not None:
                shift = shift + refs[0][...] * refs[1][:, pl.ds(off, CHUNK)]
            out_ref[:, pl.ds(off, CHUNK)] = shift
            for r in range(per_chunk):
                start = (i * per_chunk + r) * line + 128
                pay_ref[:, start:start + width] = shift[:, r * width:(r + 1) * width]
            norm_ref[...] += jnp.sum(weight_ref[:, pl.ds(off, CHUNK)] * shift * shift, axis=1, keepdims=True)

        lane = lax.broadcasted_iota(jnp.int32, (1, 128), 1)
        sums = jnp.where(lane == 0, norm_ref[...], jnp.where(lane == 1, extra_ref[...], 0.0))
        for r in range(parts):
            pay_ref[:, r * line:r * line + 128] = sums
            if line > 128 + width:
                pay_ref[:, r * line + 128 + width:(r + 1) * line] = jnp.zeros((1, line - 128 - width), jnp.float32)

    return pl.pallas_call(
        kernel,
        out_shape=(
            jax.ShapeDtypeStruct((1, total), jnp.float32),
            jax.ShapeDtypeStruct((1, parts * line), jnp.float32),
        ),
        scratch_shapes=[pltpu.VMEM((2 * rows, HI), jnp.bfloat16), pltpu.VMEM((1, 1), jnp.float32)],
    )(shifted.reshape(rows, HI), frac, first, zsrc, weight, extra.reshape(1, 1), *extras)


def knot_scatter(values, first_ids, basis16, s_norm, knots, parts, norm_of=None):
    total = first_ids.shape[1]
    cols = knots // HI
    rows = 4 * cols
    line = 128 + (cols + 1) * HI

    def kernel(val_ref, ids_ref, basis_ref, norm_ref, *refs):
        pay_ref, acc_ref = refs[-2:]
        acc_ref[...] = jnp.zeros(acc_ref.shape, jnp.float32)

        def body(off):
            idc = ids_ref[:, pl.ds(off, CHUNK)]
            sel = group_mask(idc, rows, CHUNK, cols)
            v = jnp.where(sel, basis_ref[:, pl.ds(off, CHUNK)] * val_ref[:, pl.ds(off, CHUNK)], 0.0)
            spread = jnp.concatenate(pieces(v), axis=0)
            res = lax.dot_general(
                spread, hot_rows(idc, CHUNK), (((1,), (1,)), ((), ())),
                preferred_element_type=jnp.float32,
            )
            acc_ref[...] += res[:rows] + res[rows:]

        chunks(total, body)
        lane = lax.broadcasted_iota(jnp.int32, (cols, HI), 1)
        same = acc_ref[0:cols, :]
        carried = jnp.zeros((cols, HI), jnp.float32)
        for q in range(1, 4):
            moved = pltpu.roll(acc_ref[q * cols:(q + 1) * cols, :], q, 1)
            same = same + jnp.where(lane >= q, moved, 0.0)
            carried = carried + jnp.where(lane < q, moved, 0.0)
        blank = jnp.zeros((1, HI), jnp.float32)
        grid = jnp.concatenate([same, blank], axis=0) + jnp.concatenate([blank, carried], axis=0)
        norm = norm_ref[...]
        if norm_of is not None:
            grad = refs[0][...] - refs[2][...] * refs[1][...]
            norm = jnp.sum(jnp.sum(grad * grad, axis=0, keepdims=True), axis=1, keepdims=True)
        head = jnp.where(lax.broadcasted_iota(jnp.int32, (1, 128), 1) == 0, norm, 0.0)
        row = jnp.concatenate([head] + [grid[c:c + 1, :] for c in range(cols + 1)], axis=1)
        for r in range(parts):
            pay_ref[:, r * line:(r + 1) * line] = row

    extras = [] if norm_of is None else [norm_of[0], norm_of[1], norm_of[2].reshape(1, 1)]
    return pl.pallas_call(
        kernel,
        out_shape=jax.ShapeDtypeStruct((1, parts * line), jnp.float32),
        scratch_shapes=[pltpu.VMEM((rows, HI), jnp.float32)],
    )(values, first_ids, basis16, s_norm.reshape(1, 1), *extras).reshape(parts, line)


def per_device(
    observed_residual,
    source_partials,
    spread_derivative_table,
    detector_index,
    first_knot_interval,
    interval_fraction,
    live_slot_count,
    slot_owned_source,
):
    rows = observed_residual.shape[1]
    n_time = lax.axis_size("tm")
    n_share = lax.axis_size("src")
    n_ranks = n_time * n_share
    capacity = rows // n_ranks
    n_params = source_partials.shape[0]
    detector_count = spread_derivative_table.shape[1]
    knots = KN
    n_knots = n_time * knots
    owned = SRC_DEV
    everyone = ("tm", "src")
    place = jnp.arange(capacity, dtype=jnp.int32)[None, :]
    live = (place < live_slot_count[0][:, None]).astype(jnp.float32).reshape(1, rows)
    indicator = (
        detector_index[None, :] == jnp.arange(detector_count, dtype=jnp.int32)[:, None]
    ).astype(jnp.float32)
    weight_factor = jnp.dot(
        spread_derivative_table,
        indicator,
        precision=lax.Precision.HIGHEST,
        preferred_element_type=jnp.float32,
    )
    weight_sq = live * jnp.sum(weight_factor * weight_factor, axis=0, keepdims=True)
    basis16 = jnp.repeat(jnp.stack(spline_basis(interval_fraction), axis=0), knots // HI, axis=0)
    first_ids = first_knot_interval.reshape(1, rows)
    ids = slot_owned_source[0].reshape(1, rows)
    zbar0 = live * jnp.sum(weight_factor * observed_residual, axis=0, keepdims=True)

    packed = jnp.concatenate(
        [
            source_partials,
            zbar0,
            weight_sq,
            interval_fraction[None],
            first_knot_interval.astype(jnp.float32)[None],
        ],
        axis=0,
    )
    n_rows = packed.shape[0]
    blocks = packed.reshape(n_rows, n_ranks, capacity).transpose(1, 0, 2).reshape(n_ranks, n_rows * capacity)
    got = lax.all_to_all(blocks, everyone, 0, 0, tiled=True)
    got = got.reshape(n_ranks, n_rows, capacity).transpose(1, 0, 2).reshape(n_rows, rows)
    held = got[:n_params]
    zbar0_own = got[n_params:n_params + 1]
    weight_sq_own = got[n_params + 1:n_params + 2]
    frac_own = got[n_params + 2:n_params + 3]
    first_own = got[n_params + 3:n_params + 4]
    table_rows = n_params * (owned // HI)

    def combine(sent):
        every = lax.all_to_all(sent, everyone, 0, 0, tiled=True)
        block = jnp.sum(every[:, 128:128 + knots + 3].reshape(n_time, n_share, knots + 3), axis=1)
        main = block[:, :knots].at[1:, :3].add(block[:-1, knots:])
        grad_a = main.reshape(n_knots)
        norm = jnp.sum(every[:, 0]) + jnp.sum(grad_a * grad_a)
        return grad_a, norm

    def forward(zsrc, dir_a, extra, carry=None):
        extended = jnp.concatenate([dir_a, jnp.zeros((3,), jnp.float32)])
        shift_own, payload = knot_gather(
            extended, frac_own, first_own, knots, n_share, zsrc, weight_sq_own, extra, n_knots, n_ranks,
            capacity, carry,
        )
        back = lax.all_to_all(payload.reshape(n_ranks, -1), everyone, 0, 0, tiled=True)
        totals = jnp.sum(back[:, :2], axis=0)
        return shift_own, back[:, 128:128 + capacity].reshape(1, rows) * live, totals[0], totals[1]

    sol_s = jnp.zeros((n_params, owned), jnp.float32)
    sol_a = jnp.zeros((n_knots,), jnp.float32)
    resid = observed_residual
    zbar_slot = zbar0
    sent = knot_scatter(zbar_slot, first_ids, basis16, jnp.zeros((), jnp.float32), knots, n_ranks)
    sent, held, zbar0_own = lax.optimization_barrier((sent, held, zbar0_own))
    grad_a, gamma_a = combine(sent)
    grad_s, extra = source_scatter(held, [zbar0_own], ids, owned, with_norm=True)
    dir_s, dir_a = (grad_s, grad_a)
    zsrc, att, carry = source_gather(dir_s, ids, held), dir_a, None
    for step in range(ITERS):
        shift_own, shift_slot, image_sq, extra_sum = forward(zsrc, att, extra, carry)
        if step == 0:
            gamma = extra_sum + gamma_a
        alpha = gamma / image_sq
        sol_s = sol_s + alpha * dir_s.reshape(n_params, owned)
        sol_a = sol_a + alpha * dir_a
        resid = resid - alpha * (weight_factor * shift_slot)
        if step + 1 < ITERS:
            pushed = source_scatter(held, [weight_sq_own, shift_own], ids, owned)
            zbar_slot = zbar_slot - alpha * (weight_sq * shift_slot)
            grad_before = grad_s
            grad_s = grad_s - alpha * pushed
            grad_a, fresh = combine(
                knot_scatter(
                    zbar_slot, first_ids, basis16, jnp.zeros((), jnp.float32), knots, n_ranks,
                    (grad_before, pushed, alpha),
                )
            )
            zsrc, att = source_gather(grad_s, ids, held), grad_a
            beta = fresh / gamma
            carry = (beta, shift_own)
            dir_s = grad_s + beta * dir_s
            dir_a = grad_a + beta * dir_a
            gamma = fresh
            extra = jnp.zeros((), jnp.float32)
    mine_a = lax.dynamic_slice(sol_a, (lax.axis_index("tm") * knots,), (knots,))
    return (sol_s, mine_a, resid)


def solution(mesh):
    placed = (
        P(None, ("tm", "src")),
        P(None, ("tm", "src")),
        P(),
        P(("tm", "src")),
        P(("tm", "src")),
        P(("tm", "src")),
        P(("tm", "src"), None),
        P(("tm", "src"), None),
    )
    return jax.shard_map(
        per_device,
        mesh=mesh,
        in_specs=placed,
        out_specs=(P(None, ("tm", "src")), P("tm"), P(None, ("tm", "src"))),
        check_vma=False,
    )
```

```python
import jax
import jax.numpy as jnp
from jax import lax
from jax.experimental import pallas as pl
from jax.experimental.pallas import tpu as pltpu
from jax.sharding import PartitionSpec as P

SRC_DEV = 32768
KN = 1024
ITERS = 2
HI = 256
CHUNK = 4096


def passed_along(block, axis, distance):
    devices = range(lax.axis_size(axis))
    route = [(i - distance, i) for i in devices if i - distance in devices]
    return lax.ppermute(block, axis, route)


def spline_basis(frac):
    u2 = frac * frac
    u3 = u2 * frac
    one = 1.0 - frac
    return [
        one * one * one / 6.0,
        (3.0 * u3 - 6.0 * u2 + 4.0) / 6.0,
        (-3.0 * u3 + 3.0 * u2 + 3.0 * frac + 1.0) / 6.0,
        u3 / 6.0,
    ]


def pieces(x):
    h = x.astype(jnp.bfloat16)
    m = (x - h.astype(jnp.float32)).astype(jnp.bfloat16)
    return h, m


def hot_rows(ids, width):
    low = jnp.bitwise_and(ids, HI - 1)
    return (lax.broadcasted_iota(jnp.int32, (HI, width), 0) == low).astype(jnp.bfloat16)


def group_mask(ids, rows, width, groups):
    high = lax.shift_right_logical(ids, 8)
    iota = lax.broadcasted_iota(jnp.int32, (rows, width), 0)
    return (iota % groups) == high


def chunks(total, body):
    def step(i, carry):
        body(pl.multiple_of(i * CHUNK, CHUNK))
        return carry

    lax.fori_loop(0, total // CHUNK, step, 0)


def split_into(src_ref, big_ref):
    rows = src_ref.shape[0]
    for k, part in enumerate(pieces(src_ref[...])):
        big_ref[k * rows:(k + 1) * rows, :] = part


def source_gather(table, ids, held):
    n, total = held.shape
    rows = table.shape[0]
    cols = rows // n

    def kernel(tab_ref, ids_ref, held_ref, out_ref, big_ref):
        split_into(tab_ref, big_ref)

        def body(off):
            idc = ids_ref[:, pl.ds(off, CHUNK)]
            picked = jnp.dot(big_ref[...], hot_rows(idc, CHUNK), preferred_element_type=jnp.float32)
            sel = group_mask(idc, cols, CHUNK, cols)
            weights = held_ref[:, pl.ds(off, CHUNK)]
            column = jnp.zeros((1, CHUNK), jnp.float32)
            for p in range(n):
                acc = (
                    picked[p * cols:(p + 1) * cols]
                    + picked[rows + p * cols:rows + (p + 1) * cols]
                )
                value = jnp.sum(jnp.where(sel, acc, 0.0), axis=0, keepdims=True)
                column = column + weights[p:p + 1] * value
            out_ref[:, pl.ds(off, CHUNK)] = column

        chunks(total, body)

    return pl.pallas_call(
        kernel,
        out_shape=jax.ShapeDtypeStruct((1, total), jnp.float32),
        scratch_shapes=[pltpu.VMEM((2 * rows, HI), jnp.bfloat16)],
    )(table, ids, held)


def source_scatter(values, scales, ids, width, with_norm=False):
    n, total = values.shape
    cols = width // HI
    rows = n * cols
    count = len(scales)

    def kernel(val_ref, *refs):
        scale_refs = refs[:count]
        ids_ref, out_ref = refs[count:count + 2]
        norm_ref = refs[count + 2:]
        out_ref[...] = jnp.zeros(out_ref.shape, jnp.float32)

        def body(off):
            idc = ids_ref[:, pl.ds(off, CHUNK)]
            scale = scale_refs[0][:, pl.ds(off, CHUNK)]
            for other in scale_refs[1:]:
                scale = scale * other[:, pl.ds(off, CHUNK)]
            v = val_ref[:, pl.ds(off, CHUNK)] * scale
            sel = group_mask(idc, cols, CHUNK, cols)
            parts = []
            for piece in pieces(v):
                for p in range(n):
                    parts.append(jnp.where(sel, piece[p:p + 1, :], jnp.zeros((), jnp.bfloat16)))
            spread = jnp.concatenate(parts, axis=0)
            res = lax.dot_general(
                spread, hot_rows(idc, CHUNK), (((1,), (1,)), ((), ())),
                preferred_element_type=jnp.float32,
            )
            out_ref[...] += res[:rows] + res[rows:]

        chunks(total, body)
        if with_norm:
            grad = out_ref[...]
            norm_ref[0][...] = jnp.sum(jnp.sum(grad * grad, axis=0, keepdims=True), axis=1, keepdims=True)

    shape = jax.ShapeDtypeStruct((rows, HI), jnp.float32)
    if not with_norm:
        return pl.pallas_call(kernel, out_shape=shape)(values, *scales, ids)
    grad, norm = pl.pallas_call(
        kernel, out_shape=(shape, jax.ShapeDtypeStruct((1, 1), jnp.float32))
    )(values, *scales, ids)
    return grad, norm.reshape(())


def knot_gather(extended, frac, first, block_knots, share, zsrc, weight, extra, knots, parts, width, carry=None):
    total = frac.shape[1]
    cols = knots // HI
    shifted = jnp.stack([extended[q:q + knots] for q in range(4)], axis=0)
    rows = 4 * cols
    per_chunk = CHUNK // width
    line = 128 + -(-width // 128) * 128

    extras = [] if carry is None else [carry[0].reshape(1, 1), carry[1].reshape(1, 1), carry[2]]

    def kernel(tab_ref, frac_ref, first_ref, zsrc_ref, weight_ref, extra_ref, *refs):
        out_ref, pay_ref, big_ref, norm_ref = refs[-4:]
        split_into(tab_ref, big_ref)
        norm_ref[...] = jnp.zeros(norm_ref.shape, jnp.float32)
        if carry is not None:
            first_shift = tab_ref[0:cols, :]
            a_norm = jnp.sum(jnp.sum(first_shift * first_shift, axis=0, keepdims=True), axis=1, keepdims=True)
            beta = (refs[0][...] + a_norm) / refs[1][...]

        for i in range(total // CHUNK):
            off = i * CHUNK
            slot = lax.broadcasted_iota(jnp.int32, (1, CHUNK), 1) + off
            idc = (slot // width // share) * block_knots + first_ref[:, pl.ds(off, CHUNK)].astype(jnp.int32)
            picked = jnp.dot(big_ref[...], hot_rows(idc, CHUNK), preferred_element_type=jnp.float32)
            acc = picked[:rows] + picked[rows:]
            sel = group_mask(idc, cols, CHUNK, cols)
            b = spline_basis(frac_ref[:, pl.ds(off, CHUNK)])
            z = jnp.zeros((1, CHUNK), jnp.float32)
            for q in range(4):
                value = jnp.sum(jnp.where(sel, acc[q * cols:(q + 1) * cols], 0.0), axis=0, keepdims=True)
                z = z + b[q] * value
            shift = zsrc_ref[:, pl.ds(off, CHUNK)] + z
            if carry is not None:
                shift = shift + beta * refs[2][:, pl.ds(off, CHUNK)]
            out_ref[:, pl.ds(off, CHUNK)] = shift
            for r in range(per_chunk):
                start = (i * per_chunk + r) * line + 128
                pay_ref[:, start:start + width] = shift[:, r * width:(r + 1) * width]
            norm_ref[...] += jnp.sum(weight_ref[:, pl.ds(off, CHUNK)] * shift * shift, axis=1, keepdims=True)

        lane = lax.broadcasted_iota(jnp.int32, (1, 128), 1)
        sums = jnp.where(lane == 0, norm_ref[...], jnp.where(lane == 1, extra_ref[...], 0.0))
        for r in range(parts):
            pay_ref[:, r * line:r * line + 128] = sums
            if line > 128 + width:
                pay_ref[:, r * line + 128 + width:(r + 1) * line] = jnp.zeros((1, line - 128 - width), jnp.float32)

    return pl.pallas_call(
        kernel,
        out_shape=(
            jax.ShapeDtypeStruct((1, total), jnp.float32),
            jax.ShapeDtypeStruct((1, parts * line), jnp.float32),
        ),
        scratch_shapes=[pltpu.VMEM((2 * rows, HI), jnp.bfloat16), pltpu.VMEM((1, 1), jnp.float32)],
    )(shifted.reshape(rows, HI), frac, first, zsrc, weight, extra.reshape(1, 1), *extras)


def knot_scatter(values, first_ids, basis16, s_norm, knots, parts, norm_of=None):
    total = first_ids.shape[1]
    cols = knots // HI
    rows = 4 * cols
    line = 128 + (cols + 1) * HI

    def kernel(val_ref, ids_ref, basis_ref, norm_ref, *refs):
        pay_ref, acc_ref = refs[-2:]
        acc_ref[...] = jnp.zeros(acc_ref.shape, jnp.float32)

        def body(off):
            idc = ids_ref[:, pl.ds(off, CHUNK)]
            sel = group_mask(idc, rows, CHUNK, cols)
            v = jnp.where(sel, basis_ref[:, pl.ds(off, CHUNK)] * val_ref[:, pl.ds(off, CHUNK)], 0.0)
            spread = jnp.concatenate(pieces(v), axis=0)
            res = lax.dot_general(
                spread, hot_rows(idc, CHUNK), (((1,), (1,)), ((), ())),
                preferred_element_type=jnp.float32,
            )
            acc_ref[...] += res[:rows] + res[rows:]

        chunks(total, body)
        lane = lax.broadcasted_iota(jnp.int32, (cols, HI), 1)
        same = acc_ref[0:cols, :]
        carried = jnp.zeros((cols, HI), jnp.float32)
        for q in range(1, 4):
            moved = pltpu.roll(acc_ref[q * cols:(q + 1) * cols, :], q, 1)
            same = same + jnp.where(lane >= q, moved, 0.0)
            carried = carried + jnp.where(lane < q, moved, 0.0)
        blank = jnp.zeros((1, HI), jnp.float32)
        grid = jnp.concatenate([same, blank], axis=0) + jnp.concatenate([blank, carried], axis=0)
        norm = norm_ref[...]
        if norm_of is not None:
            grad = refs[0][...] - refs[2][...] * refs[1][...]
            norm = jnp.sum(jnp.sum(grad * grad, axis=0, keepdims=True), axis=1, keepdims=True)
        head = jnp.where(lax.broadcasted_iota(jnp.int32, (1, 128), 1) == 0, norm, 0.0)
        row = jnp.concatenate([head] + [grid[c:c + 1, :] for c in range(cols + 1)], axis=1)
        for r in range(parts):
            pay_ref[:, r * line:(r + 1) * line] = row

    extras = [] if norm_of is None else [norm_of[0], norm_of[1], norm_of[2].reshape(1, 1)]
    return pl.pallas_call(
        kernel,
        out_shape=jax.ShapeDtypeStruct((1, parts * line), jnp.float32),
        scratch_shapes=[pltpu.VMEM((rows, HI), jnp.float32)],
    )(values, first_ids, basis16, s_norm.reshape(1, 1), *extras).reshape(parts, line)


def per_device(
    observed_residual,
    source_partials,
    spread_derivative_table,
    detector_index,
    first_knot_interval,
    interval_fraction,
    live_slot_count,
    slot_owned_source,
):
    rows = observed_residual.shape[1]
    n_time = lax.axis_size("tm")
    n_share = lax.axis_size("src")
    n_ranks = n_time * n_share
    capacity = rows // n_ranks
    n_params = source_partials.shape[0]
    detector_count = spread_derivative_table.shape[1]
    knots = KN
    n_knots = n_time * knots
    owned = SRC_DEV
    everyone = ("tm", "src")
    place = jnp.arange(capacity, dtype=jnp.int32)[None, :]
    live = (place < live_slot_count[0][:, None]).astype(jnp.float32).reshape(1, rows)
    indicator = (
        detector_index[None, :] == jnp.arange(detector_count, dtype=jnp.int32)[:, None]
    ).astype(jnp.float32)
    weight_factor = jnp.dot(
        spread_derivative_table,
        indicator,
        precision=lax.Precision.HIGHEST,
        preferred_element_type=jnp.float32,
    )
    weight_sq = live * jnp.sum(weight_factor * weight_factor, axis=0, keepdims=True)
    basis16 = jnp.repeat(jnp.stack(spline_basis(interval_fraction), axis=0), knots // HI, axis=0)
    first_ids = first_knot_interval.reshape(1, rows)
    ids = slot_owned_source[0].reshape(1, rows)
    zbar0 = live * jnp.sum(weight_factor * observed_residual, axis=0, keepdims=True)

    packed = jnp.concatenate(
        [
            source_partials,
            zbar0,
            weight_sq,
            interval_fraction[None],
            first_knot_interval.astype(jnp.float32)[None],
        ],
        axis=0,
    )
    n_rows = packed.shape[0]
    blocks = packed.reshape(n_rows, n_ranks, capacity).transpose(1, 0, 2).reshape(n_ranks, n_rows * capacity)
    got = lax.all_to_all(blocks, everyone, 0, 0, tiled=True)
    got = got.reshape(n_ranks, n_rows, capacity).transpose(1, 0, 2).reshape(n_rows, rows)
    held = got[:n_params]
    zbar0_own = got[n_params:n_params + 1]
    weight_sq_own = got[n_params + 1:n_params + 2]
    frac_own = got[n_params + 2:n_params + 3]
    first_own = got[n_params + 3:n_params + 4]
    table_rows = n_params * (owned // HI)

    def combine(sent):
        every = lax.all_to_all(sent, everyone, 0, 0, tiled=True)
        block = jnp.sum(every[:, 128:128 + knots + 3].reshape(n_time, n_share, knots + 3), axis=1)
        main = block[:, :knots].at[1:, :3].add(block[:-1, knots:])
        grad_a = main.reshape(n_knots)
        s_sum = jnp.sum(every[:, 0])
        return grad_a, s_sum + jnp.sum(grad_a * grad_a), s_sum

    def forward(zsrc, dir_a, extra, carry=None):
        extended = jnp.concatenate([dir_a, jnp.zeros((3,), jnp.float32)])
        shift_own, payload = knot_gather(
            extended, frac_own, first_own, knots, n_share, zsrc, weight_sq_own, extra, n_knots, n_ranks,
            capacity, carry,
        )
        back = lax.all_to_all(payload.reshape(n_ranks, -1), everyone, 0, 0, tiled=True)
        totals = jnp.sum(back[:, :2], axis=0)
        return shift_own, back[:, 128:128 + capacity].reshape(1, rows) * live, totals[0], totals[1]

    sol_s = jnp.zeros((n_params, owned), jnp.float32)
    sol_a = jnp.zeros((n_knots,), jnp.float32)
    resid = observed_residual
    zbar_slot = zbar0
    sent = knot_scatter(zbar_slot, first_ids, basis16, jnp.zeros((), jnp.float32), knots, n_ranks)
    sent, held, zbar0_own = lax.optimization_barrier((sent, held, zbar0_own))
    grad_a, gamma_a, unused = combine(sent)
    grad_s, extra = source_scatter(held, [zbar0_own], ids, owned, with_norm=True)
    dir_s, dir_a = (grad_s, grad_a)
    zsrc, att, carry = source_gather(dir_s, ids, held), dir_a, None
    for step in range(ITERS):
        shift_own, shift_slot, image_sq, extra_sum = forward(zsrc, att, extra, carry)
        if step == 0:
            gamma = extra_sum + gamma_a
        alpha = gamma / image_sq
        sol_s = sol_s + alpha * dir_s.reshape(n_params, owned)
        sol_a = sol_a + alpha * dir_a
        resid = resid - alpha * (weight_factor * shift_slot)
        if step + 1 < ITERS:
            pushed = source_scatter(held, [weight_sq_own, shift_own], ids, owned)
            zbar_slot = zbar_slot - alpha * (weight_sq * shift_slot)
            grad_before = grad_s
            grad_s = grad_s - alpha * pushed
            grad_a, fresh, s_sum = combine(
                knot_scatter(
                    zbar_slot, first_ids, basis16, jnp.zeros((), jnp.float32), knots, n_ranks,
                    (grad_before, pushed, alpha),
                )
            )
            zsrc, att = source_gather(grad_s, ids, held), grad_a
            beta = fresh / gamma
            carry = (s_sum, gamma, shift_own)
            dir_s = grad_s + beta * dir_s
            dir_a = grad_a + beta * dir_a
            gamma = fresh
            extra = jnp.zeros((), jnp.float32)
    mine_a = lax.dynamic_slice(sol_a, (lax.axis_index("tm") * knots,), (knots,))
    return (sol_s, mine_a, resid)


def solution(mesh):
    placed = (
        P(None, ("tm", "src")),
        P(None, ("tm", "src")),
        P(),
        P(("tm", "src")),
        P(("tm", "src")),
        P(("tm", "src")),
        P(("tm", "src"), None),
        P(("tm", "src"), None),
    )
    return jax.shard_map(
        per_device,
        mesh=mesh,
        in_specs=placed,
        out_specs=(P(None, ("tm", "src")), P("tm"), P(None, ("tm", "src"))),
        check_vma=False,
    )
```
